32 devices in a mesh: gx: 4 (over y, x), gy: 4 (over z), gz: 2 (over core).
Axes of the slice: x: 2, y: 2, z: 4, core: 2. Of those that a mesh axis runs over, the one named last changes fastest.
Arguments:
- heart_state: float32 [19, 32, 128, 256], P(None, 'gx', 'gy', 'gz'), may hold values from -4 to 4, as said below
- cell_type: int32 [32, 128, 256], P('gx', 'gy', 'gz'), may hold values from 0 to 2
- gate_half: float32 [18], replicated, may hold values from -1 to 1
- gate_slope: float32 [18], replicated, may hold values from 0.15 to 0.6
- gate_tau: float32 [18], replicated, may hold values from 0.03 to 1.5
- conduct: float32 [3, 9], replicated, may hold values from 0.1 to 1.5
- reversal: float32 [9], replicated, may hold values from -2 to 2
- block_device: int32 [32, 128, 2], P('gx', 'gy', 'gz'), may hold values from 0 to 31, as said below
- block_row: int32 [32, 128, 2], P('gx', 'gy', 'gz'), may hold values from 0 to 2047, as said below
- tissue: int32 [128, 256, 256], P('gx', 'gy', 'gz'), may hold values from 0 to 3
- tissue_sigma: float32 [4, 3], replicated, may hold values from 0.2 to 2
Outputs:
- heart_next: float32 [19, 32, 128, 256], P(None, 'gx', 'gy', 'gz')
- potential: float32 [128, 256, 4, 256], P('gx', 'gy', None, 'gz')
The draws below stay inside these ranges and needn't reach their ends.
Inputs may be any that keep to these rules, and one draw needn't show every extreme that they name: `heart_state`: row 0 (the voltage) lies within -4 to 4, rows 1 to 18 (gates) within 0 to 1. `block_device`: in every aligned group of four devices, one device is named exactly 24 times by the blocks of every device, one exactly 24 // 3 times by the blocks of every device, and the other two by none; which ones, and the order of the blocks, vary. `block_row`: blocks sent to the same device cover different rows; a device receives at most 768 blocks, and a quarter of the devices receive exactly that many.
All inputs are finite; a program needn't handle non-finite values.
Results may differ from the reference program's by a relative error of at most 0.0001.
Values sent between devices are 32-bit elements; how exact they have to be, the bound alone decides.
No kernel may reach another device: no remote copies, remote signals or barrier semaphores. Data moves between devices by JAX's collectives and lax.ppermute only.
A program may use at most 256 MiB of HBM per device.

```python
import math
import jax
import jax.numpy as jnp

NSTATE = 19
CHANNELS = 9
CELLTYPES = 3
TISSUES = 4
STEPS = 4
SWEEPS = 4
HX = 8
HY = 32
ROW = 128
TX = 32
TY = 64
HNX = 32
HNY = 128
HNZ = 256
TNX = 128
TNY = 256
TNZ = 256
N_GX = 4
N_GY = 4
N_GZ = 2


def draw_heart_state(key, part):
    key_volt, key_gate = jax.random.split(key)
    volt_shape = (1, HX * N_GX, HY * N_GY, ROW * N_GZ)
    gate_shape = (NSTATE - 1, HX * N_GX, HY * N_GY, ROW * N_GZ)
    voltage = jnp.clip(jax.random.normal(key_volt, volt_shape, jnp.float32), -4.0, 4.0)
    gate_state = jax.random.uniform(key_gate, gate_shape, jnp.float32, 0.0, 1.0)
    return jnp.concatenate([voltage, gate_state], axis=0)


def one_permutation(key, length):
    return jax.random.permutation(key, length)


def block_plan(key):
    devices = N_GX * N_GY * N_GZ
    blocks = HX * HY
    quarter = devices // 4
    capacity = 3 * blocks // devices
    low_count = blocks // devices
    base = jax.random.fold_in(key, 7)
    key_role, key_send, key_row = jax.random.split(base, 3)
    role_perm = jax.vmap(lambda item: one_permutation(item, 4))(jax.random.split(key_role, quarter))
    group_base = jnp.arange(quarter, dtype=jnp.int32) * 4
    busy_ids = group_base + jnp.argmax(role_perm == 0, axis=1).astype(jnp.int32)
    middle_ids = group_base + jnp.argmax(role_perm == 1, axis=1).astype(jnp.int32)
    dest_list = jnp.concatenate([jnp.repeat(busy_ids, capacity), jnp.repeat(middle_ids, low_count)])
    occurrence = jnp.concatenate([jnp.arange(quarter * capacity, dtype=jnp.int32) % capacity, jnp.arange(quarter * low_count, dtype=jnp.int32) % low_count])
    per_count = jnp.concatenate([jnp.full((quarter * capacity,), capacity, jnp.int32), jnp.full((quarter * low_count,), low_count, jnp.int32)])
    send_perm = jax.vmap(lambda item: one_permutation(item, blocks))(jax.random.split(key_send, devices))
    dest_dev = dest_list[send_perm]
    sender_ids = jnp.arange(devices, dtype=jnp.int32)[:, None]
    position = sender_ids * per_count[send_perm] + occurrence[send_perm]
    row_perm = jax.vmap(lambda item: one_permutation(item, TX * TY))(jax.random.split(key_row, devices))
    dest_row = row_perm[dest_dev, position].astype(jnp.int32)

    def to_global(table):
        shaped = table.reshape(N_GX, N_GY, N_GZ, HX, HY)
        return jnp.transpose(shaped, (0, 3, 1, 4, 2)).reshape(HX * N_GX, HY * N_GY, N_GZ).astype(jnp.int32)
    return (to_global(dest_dev), to_global(dest_row))


def draw_block_device(key, part):
    return block_plan(key)[0]


def draw_block_row(key, part):
    return block_plan(key)[1]


def set_ends(entries, stream_key, low, top_value):
    longest = entries.shape.index(max(entries.shape))
    spots = []
    for shift in (0, 1):
        where = [jax.random.randint(jax.random.fold_in(stream_key, axis), (), 0, length) for axis, length in enumerate(entries.shape)]
        where[longest] = (where[longest] + shift) % entries.shape[longest]
        spots.append(tuple(where))
    return entries.at[spots[0]].set(low).at[spots[1]].set(top_value)


def setup_inputs(seed: int = 0) -> dict:
    arg_keys = jax.random.split(jax.random.key(seed), 12)
    heart_state = draw_heart_state(jax.random.fold_in(arg_keys[11], 71), 0)
    cell_type = set_ends(jax.random.randint(arg_keys[1], (HNX, HNY, HNZ), 0, CELLTYPES), jax.random.fold_in(arg_keys[1], 1), 0, CELLTYPES - 1).astype(jnp.int32)
    gate_half = jnp.clip(jax.random.uniform(arg_keys[2], (2 * CHANNELS,), jnp.float32, -1.0, 1.0), -1.0, 1.0)
    gate_slope = jnp.clip(jnp.exp(jax.random.uniform(arg_keys[3], (2 * CHANNELS,), jnp.float32, math.log(0.15), math.log(0.6))), 0.15, 0.6)
    gate_tau = jnp.clip(jnp.exp(jax.random.uniform(arg_keys[4], (2 * CHANNELS,), jnp.float32, math.log(0.03), math.log(1.5))), 0.03, 1.5)
    conduct = jnp.clip(jnp.exp(jax.random.uniform(arg_keys[5], (CELLTYPES, CHANNELS), jnp.float32, math.log(0.1), math.log(1.5))), 0.1, 1.5)
    reversal = jnp.clip(jax.random.uniform(arg_keys[6], (CHANNELS,), jnp.float32, -2.0, 2.0), -2.0, 2.0)
    block_device = draw_block_device(jax.random.fold_in(arg_keys[11], 71), 0)
    block_row = draw_block_row(jax.random.fold_in(arg_keys[11], 71), 0)
    tissue = set_ends(jax.random.randint(arg_keys[9], (TNX, TNY, TNZ), 0, TISSUES), jax.random.fold_in(arg_keys[9], 1), 0, TISSUES - 1).astype(jnp.int32)
    tissue_sigma = jnp.clip(jnp.exp(jax.random.uniform(arg_keys[10], (TISSUES, 3), jnp.float32, math.log(0.2), math.log(2.0))), 0.2, 2.0)
    return dict(heart_state=heart_state, cell_type=cell_type, gate_half=gate_half, gate_slope=gate_slope, gate_tau=gate_tau, conduct=conduct, reversal=reversal, block_device=block_device, block_row=block_row, tissue=tissue, tissue_sigma=tissue_sigma)


DT_HEART = 0.05
SIGMA_HEART = 1.0
SCREEN = 0.05
LOW_EDGE = 0.1
HIGH_EDGE = 1.9


def chebyshev_weights(sweep_count):
    spectrum_mid = 0.5 * (HIGH_EDGE + LOW_EDGE)
    half_width = 0.5 * (HIGH_EDGE - LOW_EDGE)
    half_ratio = spectrum_mid / half_width
    rho_old = 1.0 / half_ratio
    first_coef = []
    second_coef = []
    for sweep in range(1, sweep_count):
        rho_new = 1.0 / (2.0 * half_ratio - rho_old)
        first_coef.append(rho_new * rho_old)
        second_coef.append(2.0 * rho_new / half_width)
        rho_old = rho_new
    return spectrum_mid, first_coef, second_coef


def membrane(voltage, gate_state, cell_type, gate_half, gate_slope, gate_tau, conduct, reversal):
    gate_count = gate_half.shape[0]
    lead_shape = (-1,) + (1,) * voltage.ndim
    gate_sign = jnp.where(jnp.arange(gate_count) % 2 == 0, 1.0, -1.0).astype(jnp.float32)
    exponent = (gate_sign / gate_slope).reshape(lead_shape) * (voltage[None] - gate_half.reshape(lead_shape))
    steady = jax.nn.sigmoid(exponent)
    time_const = gate_tau.reshape(lead_shape) * (0.5 + steady)
    gate_state = steady + (gate_state - steady) * jnp.exp(-DT_HEART / time_const)
    weight = jnp.zeros(gate_state[0::2].shape, jnp.float32)
    for cell_kind in range(conduct.shape[0]):
        weight = weight + jnp.where(cell_type[None] == cell_kind, conduct[cell_kind].reshape(lead_shape), 0.0)
    ion_current = jnp.sum(weight * gate_state[0::2] * gate_state[1::2] * (voltage[None] - reversal.reshape(lead_shape)), axis=0)
    return gate_state, ion_current


def heart_laplace(padded):
    centre = padded[1:-1, 1:-1, 1:-1]
    total = padded[2:, 1:-1, 1:-1] + padded[:-2, 1:-1, 1:-1]
    total = total + padded[1:-1, 2:, 1:-1] + padded[1:-1, :-2, 1:-1]
    total = total + padded[1:-1, 1:-1, 2:] + padded[1:-1, 1:-1, :-2]
    return total - 6.0 * centre


def face_terms(sig_pad):
    centre = sig_pad[1:-1, 1:-1, :, 1:-1]
    plus_x = 0.5 * (centre[:, :, 0:1] + sig_pad[2:, 1:-1, 0:1, 1:-1])
    minus_x = 0.5 * (centre[:, :, 0:1] + sig_pad[:-2, 1:-1, 0:1, 1:-1])
    plus_y = 0.5 * (centre[:, :, 1:2] + sig_pad[1:-1, 2:, 1:2, 1:-1])
    minus_y = 0.5 * (centre[:, :, 1:2] + sig_pad[1:-1, :-2, 1:2, 1:-1])
    plus_z = 0.5 * (centre[:, :, 2:3] + sig_pad[1:-1, 1:-1, 2:3, 2:])
    minus_z = 0.5 * (centre[:, :, 2:3] + sig_pad[1:-1, 1:-1, 2:3, :-2])
    diagonal = SCREEN + plus_x + minus_x + plus_y + minus_y + plus_z + minus_z
    return (plus_x, minus_x, plus_y, minus_y, plus_z, minus_z), diagonal


def apply_operator(dir_pad, face_list, diagonal):
    centre = dir_pad[1:-1, 1:-1, :, 1:-1]
    beside = face_list[0] * dir_pad[2:, 1:-1, :, 1:-1] + face_list[1] * dir_pad[:-2, 1:-1, :, 1:-1]
    beside = beside + face_list[2] * dir_pad[1:-1, 2:, :, 1:-1] + face_list[3] * dir_pad[1:-1, :-2, :, 1:-1]
    beside = beside + face_list[4] * dir_pad[1:-1, 1:-1, :, 2:] + face_list[5] * dir_pad[1:-1, 1:-1, :, :-2]
    return diagonal * centre - beside


def reference(heart_state, cell_type, gate_half, gate_slope, gate_tau, conduct, reversal, block_device, block_row, tissue, tissue_sigma):
    voltage = heart_state[0]
    gate_state = heart_state[1:]
    currents = []
    for time_step in range(STEPS):
        gate_state, ion_current = membrane(voltage, gate_state, cell_type, gate_half, gate_slope, gate_tau, conduct, reversal)
        current = SIGMA_HEART * heart_laplace(jnp.pad(voltage, 1))
        currents.append(current)
        voltage = voltage + DT_HEART * (current - ion_current)
    heart_next = jnp.concatenate([voltage[None], gate_state], axis=0)
    stacked = jnp.stack(currents, 0).reshape(STEPS, HNX, HNY, N_GZ, ROW)
    block_values = jnp.transpose(stacked, (1, 2, 3, 0, 4)).reshape(-1, STEPS, ROW)
    dest_dev = block_device.reshape(-1)
    dest_row = block_row.reshape(-1)
    dev_x = dest_dev // (N_GY * N_GZ)
    dev_y = (dest_dev // N_GZ) % N_GY
    dev_z = dest_dev % N_GZ
    cell_x = dev_x * TX + dest_row // TY
    cell_y = dev_y * TY + dest_row % TY
    source = jnp.zeros((TNX, TNY, STEPS, N_GZ, ROW), jnp.float32)
    source = source.at[cell_x, cell_y, :, dev_z, :].add(block_values)
    source = source.reshape(TNX, TNY, STEPS, TNZ)
    conductivity = jnp.zeros((TNX, TNY, 3, TNZ), jnp.float32)
    for tissue_kind in range(tissue_sigma.shape[0]):
        conductivity = conductivity + jnp.where(tissue[:, :, None, :] == tissue_kind, tissue_sigma[tissue_kind][None, :, None], 0.0)
    pad_spec = ((1, 1), (1, 1), (0, 0), (1, 1))
    face_list, diagonal = face_terms(jnp.pad(conductivity, pad_spec))
    spectrum_mid, first_coef, second_coef = chebyshev_weights(SWEEPS)
    residual = source
    step_dir = (residual / diagonal) / spectrum_mid
    potential = step_dir
    for sweep in range(1, SWEEPS):
        residual = residual - apply_operator(jnp.pad(step_dir, pad_spec), face_list, diagonal)
        step_dir = first_coef[sweep - 1] * step_dir + second_coef[sweep - 1] * (residual / diagonal)
        potential = potential + step_dir
    return heart_next, potential
```

```python
import jax
import jax.numpy as jnp
from jax import lax
from jax.sharding import PartitionSpec as P

STEPS = 4
SWEEPS = 4


DT_HEART = 0.05
SIGMA_HEART = 1.0
SCREEN = 0.05
LOW_EDGE = 0.1
HIGH_EDGE = 1.9


def chebyshev_weights(sweep_count):
    spectrum_mid = 0.5 * (HIGH_EDGE + LOW_EDGE)
    half_width = 0.5 * (HIGH_EDGE - LOW_EDGE)
    half_ratio = spectrum_mid / half_width
    rho_old = 1.0 / half_ratio
    first_coef = []
    second_coef = []
    for sweep in range(1, sweep_count):
        rho_new = 1.0 / (2.0 * half_ratio - rho_old)
        first_coef.append(rho_new * rho_old)
        second_coef.append(2.0 * rho_new / half_width)
        rho_old = rho_new
    return (spectrum_mid, first_coef, second_coef)


def face_halos(block, axis, dim):
    count = lax.axis_size(axis)
    forward = [(i, i + 1) for i in range(count - 1)]
    backward = [(i + 1, i) for i in range(count - 1)]
    top = lax.index_in_dim(block, block.shape[dim] - 1, axis=dim, keepdims=False)
    bottom = lax.index_in_dim(block, 0, axis=dim, keepdims=False)
    low = lax.ppermute(top, axis, forward)
    high = lax.ppermute(bottom, axis, backward)
    return low, high


def shifted(block, low, high, dim):
    n = block.shape[dim]
    low = jnp.expand_dims(low, dim)
    high = jnp.expand_dims(high, dim)
    minus = jnp.concatenate([low, lax.slice_in_dim(block, 0, n - 1, axis=dim)], axis=dim)
    plus = jnp.concatenate([lax.slice_in_dim(block, 1, n, axis=dim), high], axis=dim)
    return minus, plus


def membrane(voltage, gate_state, cell_type, gate_half, gate_slope, gate_tau, conduct, reversal):
    gate_count = gate_half.shape[0]
    lead_shape = (-1,) + (1,) * voltage.ndim
    gate_sign = jnp.where(jnp.arange(gate_count) % 2 == 0, 1.0, -1.0).astype(jnp.float32)
    exponent = (gate_sign / gate_slope).reshape(lead_shape) * (
        voltage[None] - gate_half.reshape(lead_shape)
    )
    steady = jax.nn.sigmoid(exponent)
    time_const = gate_tau.reshape(lead_shape) * (0.5 + steady)
    gate_state = steady + (gate_state - steady) * jnp.exp(-DT_HEART / time_const)
    weight = jnp.zeros(gate_state[0::2].shape, jnp.float32)
    for cell_kind in range(conduct.shape[0]):
        weight = weight + jnp.where(
            cell_type[None] == cell_kind, conduct[cell_kind].reshape(lead_shape), 0.0
        )
    ion_current = jnp.sum(
        weight
        * gate_state[0::2]
        * gate_state[1::2]
        * (voltage[None] - reversal.reshape(lead_shape)),
        axis=0,
    )
    return (gate_state, ion_current)


def heart_laplace(voltage):
    parts = []
    for axis, dim in (("gx", 0), ("gy", 1), ("gz", 2)):
        low, high = face_halos(voltage, axis, dim)
        minus, plus = shifted(voltage, low, high, dim)
        parts.append((plus, minus))
    total = parts[0][0] + parts[0][1]
    total = total + parts[1][0] + parts[1][1]
    total = total + parts[2][0] + parts[2][1]
    return total - 6.0 * voltage


def local(
    heart_state,
    cell_type,
    gate_half,
    gate_slope,
    gate_tau,
    conduct,
    reversal,
    block_device,
    block_row,
    tissue,
    tissue_sigma,
):
    voltage = heart_state[0]
    gate_state = heart_state[1:]
    heart_x, heart_y, row_len = voltage.shape
    blocks = heart_x * heart_y
    devices = lax.axis_size("gx") * lax.axis_size("gy") * lax.axis_size("gz")
    capacity = 3 * blocks // devices
    slots = devices * capacity
    torso_x, torso_y, torso_z = tissue.shape
    torso_rows = torso_x * torso_y

    dest_dev = block_device.reshape(blocks)
    dest_row = block_row.reshape(blocks)
    one_hot = (dest_dev[:, None] == jnp.arange(devices, dtype=jnp.int32)[None, :]).astype(jnp.int32)
    running = jnp.cumsum(one_hot, axis=0) - 1
    slot_rank = jnp.sum(running * one_hot, axis=1)
    slot_index = dest_dev * capacity + slot_rank
    slot_match = slot_index[None, :] == jnp.arange(slots, dtype=jnp.int32)[:, None]
    slot_used = jnp.any(slot_match, axis=1)
    slot_block = jnp.argmax(slot_match, axis=1).astype(jnp.int32)
    send_rows = jnp.where(slot_used, dest_row[slot_block], torso_rows)
    recv_rows = lax.all_to_all(
        send_rows.reshape(devices, capacity), ("gx", "gy", "gz"), 0, 0, tiled=True
    ).reshape(slots)
    row_match = recv_rows[None, :] == jnp.arange(torso_rows, dtype=jnp.int32)[:, None]
    row_used = jnp.any(row_match, axis=1)
    row_slot = jnp.argmax(row_match, axis=1).astype(jnp.int32)

    currents = []
    for time_step in range(STEPS):
        gate_state, ion_current = membrane(
            voltage, gate_state, cell_type, gate_half, gate_slope, gate_tau, conduct, reversal
        )
        current = SIGMA_HEART * heart_laplace(voltage)
        currents.append(current)
        voltage = voltage + DT_HEART * (current - ion_current)
    heart_next = jnp.concatenate([voltage[None], gate_state], axis=0)

    payload = jnp.stack([item.reshape(blocks, row_len) for item in currents], axis=0)
    send_values = jnp.where(slot_used[None, :, None], jnp.take(payload, slot_block, axis=1), 0.0)
    received = lax.all_to_all(
        send_values.reshape(STEPS, devices, capacity, row_len),
        ("gx", "gy", "gz"),
        1,
        1,
        tiled=True,
    ).reshape(STEPS, slots, row_len)
    source = jnp.where(row_used[None, :, None], jnp.take(received, row_slot, axis=1), 0.0)
    source = source.reshape(STEPS, torso_x, torso_y, torso_z)

    sigma = []
    for dim_index in range(3):
        value = jnp.zeros(tissue.shape, jnp.float32)
        for tissue_kind in range(tissue_sigma.shape[0]):
            value = value + jnp.where(tissue == tissue_kind, tissue_sigma[tissue_kind, dim_index], 0.0)
        sigma.append(value)
    faces = []
    for dim_index, axis in enumerate(("gx", "gy", "gz")):
        low, high = face_halos(sigma[dim_index], axis, dim_index)
        minus, plus = shifted(sigma[dim_index], low, high, dim_index)
        faces.append(0.5 * (sigma[dim_index] + plus))
        faces.append(0.5 * (sigma[dim_index] + minus))
    diagonal = SCREEN + faces[0] + faces[1] + faces[2] + faces[3] + faces[4] + faces[5]

    spectrum_mid, first_coef, second_coef = chebyshev_weights(SWEEPS)
    residual = source
    step_dir = residual / diagonal / spectrum_mid
    potential = step_dir
    for sweep in range(1, SWEEPS):
        near = []
        for dim_index, axis in enumerate(("gx", "gy", "gz")):
            low, high = face_halos(step_dir, axis, dim_index + 1)
            minus, plus = shifted(step_dir, low, high, dim_index + 1)
            near.append((plus, minus))
        beside = faces[0] * near[0][0] + faces[1] * near[0][1]
        beside = beside + faces[2] * near[1][0] + faces[3] * near[1][1]
        beside = beside + faces[4] * near[2][0] + faces[5] * near[2][1]
        residual = residual - (diagonal * step_dir - beside)
        step_dir = first_coef[sweep - 1] * step_dir + second_coef[sweep - 1] * (residual / diagonal)
        potential = potential + step_dir
    return (heart_next, jnp.transpose(potential, (1, 2, 0, 3)))


def solution(mesh):
    in_specs = (
        P(None, "gx", "gy", "gz"),
        P("gx", "gy", "gz"),
        P(),
        P(),
        P(),
        P(),
        P(),
        P("gx", "gy", "gz"),
        P("gx", "gy", "gz"),
        P("gx", "gy", "gz"),
        P(),
    )
    out_specs = (P(None, "gx", "gy", "gz"), P("gx", "gy", None, "gz"))
    return jax.shard_map(local, mesh=mesh, in_specs=in_specs, out_specs=out_specs, check_vma=False)
```

```python
import jax
import jax.numpy as jnp
from jax import lax
from jax.sharding import PartitionSpec as P
from jax.experimental import pallas as pl
from jax.experimental.pallas import tpu as pltpu
import functools

STEPS = 4
SWEEPS = 4


DT_HEART = 0.05
SIGMA_HEART = 1.0
SCREEN = 0.05
LOW_EDGE = 0.1
HIGH_EDGE = 1.9


def chebyshev_weights(sweep_count):
    spectrum_mid = 0.5 * (HIGH_EDGE + LOW_EDGE)
    half_width = 0.5 * (HIGH_EDGE - LOW_EDGE)
    half_ratio = spectrum_mid / half_width
    rho_old = 1.0 / half_ratio
    first_coef = []
    second_coef = []
    for sweep in range(1, sweep_count):
        rho_new = 1.0 / (2.0 * half_ratio - rho_old)
        first_coef.append(rho_new * rho_old)
        second_coef.append(2.0 * rho_new / half_width)
        rho_old = rho_new
    return (spectrum_mid, first_coef, second_coef)


def face_halos(block, axis, dim):
    count = lax.axis_size(axis)
    forward = [(i, i + 1) for i in range(count - 1)]
    backward = [(i + 1, i) for i in range(count - 1)]
    top = lax.index_in_dim(block, block.shape[dim] - 1, axis=dim, keepdims=False)
    bottom = lax.index_in_dim(block, 0, axis=dim, keepdims=False)
    low = lax.ppermute(top, axis, forward)
    high = lax.ppermute(bottom, axis, backward)
    return low, high


def shifted(block, low, high, dim):
    n = block.shape[dim]
    low = jnp.expand_dims(low, dim)
    high = jnp.expand_dims(high, dim)
    minus = jnp.concatenate([low, lax.slice_in_dim(block, 0, n - 1, axis=dim)], axis=dim)
    plus = jnp.concatenate([lax.slice_in_dim(block, 1, n, axis=dim), high], axis=dim)
    return minus, plus


def membrane(voltage, gate_state, cell_type, gate_half, gate_slope, gate_tau, conduct, reversal):
    gate_count = gate_half.shape[0]
    lead_shape = (-1,) + (1,) * voltage.ndim
    gate_sign = jnp.where(jnp.arange(gate_count) % 2 == 0, 1.0, -1.0).astype(jnp.float32)
    exponent = (gate_sign / gate_slope).reshape(lead_shape) * (
        voltage[None] - gate_half.reshape(lead_shape)
    )
    steady = jax.nn.sigmoid(exponent)
    time_const = gate_tau.reshape(lead_shape) * (0.5 + steady)
    gate_state = steady + (gate_state - steady) * jnp.exp(-DT_HEART / time_const)
    weight = jnp.zeros(gate_state[0::2].shape, jnp.float32)
    for cell_kind in range(conduct.shape[0]):
        weight = weight + jnp.where(
            cell_type[None] == cell_kind, conduct[cell_kind].reshape(lead_shape), 0.0
        )
    ion_current = jnp.sum(
        weight
        * gate_state[0::2]
        * gate_state[1::2]
        * (voltage[None] - reversal.reshape(lead_shape)),
        axis=0,
    )
    return (gate_state, ion_current)


def heart_laplace(voltage):
    parts = []
    for axis, dim in (("gx", 0), ("gy", 1), ("gz", 2)):
        low, high = face_halos(voltage, axis, dim)
        minus, plus = shifted(voltage, low, high, dim)
        parts.append((plus, minus))
    total = parts[0][0] + parts[0][1]
    total = total + parts[1][0] + parts[1][1]
    total = total + parts[2][0] + parts[2][1]
    return total - 6.0 * voltage


def sweep_kernel(first, second, d_ref, r_ref, p_ref, fxp, fxm, fyp, fym, fzp, fzm, dg_ref,
                 xlo, xhi, ylo, yhi, zedge, r_out, d_out, p_out):
    nx, ny, nz = d_ref.shape[1], d_ref.shape[2], d_ref.shape[3]
    row = lax.broadcasted_iota(jnp.int32, (ny, nz), 0)
    lane = lax.broadcasted_iota(jnp.int32, (ny, nz), 1)

    def body(x, carry):
        centre = d_ref[0, x]
        below = d_ref[0, jnp.maximum(x - 1, 0)]
        above = d_ref[0, jnp.minimum(x + 1, nx - 1)]
        x_minus = jnp.where(x == 0, xlo[0], below)
        x_plus = jnp.where(x == nx - 1, xhi[0], above)
        y_minus = jnp.where(row == 0, ylo[0, x], pltpu.roll(centre, 1, 0))
        y_plus = jnp.where(row == ny - 1, yhi[0, x], pltpu.roll(centre, ny - 1, 0))
        edge = zedge[0, x]
        z_minus = jnp.where(lane == 0, edge, pltpu.roll(centre, 1, 1))
        z_plus = jnp.where(lane == nz - 1, edge, pltpu.roll(centre, nz - 1, 1))
        beside = fxp[x] * x_plus + fxm[x] * x_minus
        beside = beside + fyp[x] * y_plus + fym[x] * y_minus
        beside = beside + fzp[x] * z_plus + fzm[x] * z_minus
        diag = dg_ref[x]
        residual = r_ref[0, x] - (diag * centre - beside)
        step_dir = first * centre + second * (residual / diag)
        r_out[0, x] = residual
        d_out[0, x] = step_dir
        p_out[0, x] = p_ref[0, x] + step_dir
        return carry

    lax.fori_loop(0, nx, body, 0)


def run_sweep(first, second, step_dir, residual, potential, faces, diagonal, halos):
    steps, nx, ny, nz = step_dir.shape
    full = pl.BlockSpec((1, nx, ny, nz), lambda s: (s, 0, 0, 0))
    fixed = pl.BlockSpec((nx, ny, nz), lambda s: (0, 0, 0))
    x_face = pl.BlockSpec((1, ny, nz), lambda s: (s, 0, 0))
    y_face = pl.BlockSpec((1, nx, 1, nz), lambda s: (s, 0, 0, 0))
    shape = jax.ShapeDtypeStruct(step_dir.shape, jnp.float32)
    size = step_dir.size
    return pl.pallas_call(
        functools.partial(sweep_kernel, first, second),
        grid=(steps,),
        in_specs=[full, full, full] + [fixed] * 7 + [x_face, x_face, y_face, y_face, full],
        out_specs=[full, full, full],
        out_shape=[shape, shape, shape],
        cost_estimate=pl.CostEstimate(flops=30 * size, transcendentals=0, bytes_accessed=4 * 7 * size + 4 * 7 * size // steps),
        name="chebyshev_sweep",
    )(step_dir, residual, potential, *faces, diagonal, *halos)


def local(
    heart_state,
    cell_type,
    gate_half,
    gate_slope,
    gate_tau,
    conduct,
    reversal,
    block_device,
    block_row,
    tissue,
    tissue_sigma,
):
    voltage = heart_state[0]
    gate_state = heart_state[1:]
    heart_x, heart_y, row_len = voltage.shape
    blocks = heart_x * heart_y
    devices = lax.axis_size("gx") * lax.axis_size("gy") * lax.axis_size("gz")
    capacity = 3 * blocks // devices
    slots = devices * capacity
    torso_x, torso_y, torso_z = tissue.shape
    torso_rows = torso_x * torso_y

    dest_dev = block_device.reshape(blocks)
    dest_row = block_row.reshape(blocks)
    one_hot = (dest_dev[:, None] == jnp.arange(devices, dtype=jnp.int32)[None, :]).astype(jnp.int32)
    running = jnp.cumsum(one_hot, axis=0) - 1
    slot_rank = jnp.sum(running * one_hot, axis=1)
    slot_index = dest_dev * capacity + slot_rank
    slot_match = slot_index[None, :] == jnp.arange(slots, dtype=jnp.int32)[:, None]
    slot_used = jnp.any(slot_match, axis=1)
    slot_block = jnp.argmax(slot_match, axis=1).astype(jnp.int32)
    send_rows = jnp.where(slot_used, dest_row[slot_block], torso_rows)
    recv_rows = lax.all_to_all(
        send_rows.reshape(devices, capacity), ("gx", "gy", "gz"), 0, 0, tiled=True
    ).reshape(slots)
    row_match = recv_rows[None, :] == jnp.arange(torso_rows, dtype=jnp.int32)[:, None]
    row_used = jnp.any(row_match, axis=1)
    row_slot = jnp.argmax(row_match, axis=1).astype(jnp.int32)

    currents = []
    for time_step in range(STEPS):
        gate_state, ion_current = membrane(
            voltage, gate_state, cell_type, gate_half, gate_slope, gate_tau, conduct, reversal
        )
        current = SIGMA_HEART * heart_laplace(voltage)
        currents.append(current)
        voltage = voltage + DT_HEART * (current - ion_current)
    heart_next = jnp.concatenate([voltage[None], gate_state], axis=0)

    payload = jnp.stack([item.reshape(blocks, row_len) for item in currents], axis=0)
    send_values = jnp.where(slot_used[None, :, None], jnp.take(payload, slot_block, axis=1), 0.0)
    received = lax.all_to_all(
        send_values.reshape(STEPS, devices, capacity, row_len),
        ("gx", "gy", "gz"),
        1,
        1,
        tiled=True,
    ).reshape(STEPS, slots, row_len)
    source = jnp.where(row_used[None, :, None], jnp.take(received, row_slot, axis=1), 0.0)
    source = source.reshape(STEPS, torso_x, torso_y, torso_z)

    sigma = []
    for dim_index in range(3):
        value = jnp.zeros(tissue.shape, jnp.float32)
        for tissue_kind in range(tissue_sigma.shape[0]):
            value = value + jnp.where(tissue == tissue_kind, tissue_sigma[tissue_kind, dim_index], 0.0)
        sigma.append(value)
    faces = []
    for dim_index, axis in enumerate(("gx", "gy", "gz")):
        low, high = face_halos(sigma[dim_index], axis, dim_index)
        minus, plus = shifted(sigma[dim_index], low, high, dim_index)
        faces.append(0.5 * (sigma[dim_index] + plus))
        faces.append(0.5 * (sigma[dim_index] + minus))
    diagonal = SCREEN + faces[0] + faces[1] + faces[2] + faces[3] + faces[4] + faces[5]

    spectrum_mid, first_coef, second_coef = chebyshev_weights(SWEEPS)
    residual = source
    step_dir = residual / diagonal / spectrum_mid
    potential = step_dir
    lane = lax.broadcasted_iota(jnp.int32, step_dir.shape, 3)
    for sweep in range(1, SWEEPS):
        x_low, x_high = face_halos(step_dir, "gx", 1)
        y_low, y_high = face_halos(step_dir, "gy", 2)
        z_low, z_high = face_halos(step_dir, "gz", 3)
        zedge = jnp.where(lane == 0, z_low[..., None], jnp.where(lane == torso_z - 1, z_high[..., None], 0.0))
        halos = (x_low, x_high, y_low[:, :, None, :], y_high[:, :, None, :], zedge)
        residual, step_dir, potential = run_sweep(
            first_coef[sweep - 1], second_coef[sweep - 1], step_dir, residual, potential, faces, diagonal, halos
        )
    return (heart_next, jnp.transpose(potential, (1, 2, 0, 3)))


def solution(mesh):
    in_specs = (
        P(None, "gx", "gy", "gz"),
        P("gx", "gy", "gz"),
        P(),
        P(),
        P(),
        P(),
        P(),
        P("gx", "gy", "gz"),
        P("gx", "gy", "gz"),
        P("gx", "gy", "gz"),
        P(),
    )
    out_specs = (P(None, "gx", "gy", "gz"), P("gx", "gy", None, "gz"))
    return jax.shard_map(local, mesh=mesh, in_specs=in_specs, out_specs=out_specs, check_vma=False)
```

```python
import jax
import jax.numpy as jnp
from jax import lax
from jax.sharding import PartitionSpec as P
from jax.experimental import pallas as pl
from jax.experimental.pallas import tpu as pltpu
import functools

STEPS = 4
SWEEPS = 4


DT_HEART = 0.05
SIGMA_HEART = 1.0
SCREEN = 0.05
LOW_EDGE = 0.1
HIGH_EDGE = 1.9


def chebyshev_weights(sweep_count):
    spectrum_mid = 0.5 * (HIGH_EDGE + LOW_EDGE)
    half_width = 0.5 * (HIGH_EDGE - LOW_EDGE)
    half_ratio = spectrum_mid / half_width
    rho_old = 1.0 / half_ratio
    first_coef = []
    second_coef = []
    for sweep in range(1, sweep_count):
        rho_new = 1.0 / (2.0 * half_ratio - rho_old)
        first_coef.append(rho_new * rho_old)
        second_coef.append(2.0 * rho_new / half_width)
        rho_old = rho_new
    return (spectrum_mid, first_coef, second_coef)


def face_halos(block, axis, dim):
    top = lax.index_in_dim(block, block.shape[dim] - 1, axis=dim, keepdims=False)
    bottom = lax.index_in_dim(block, 0, axis=dim, keepdims=False)
    return exchange(top, bottom, axis)


def shifted(block, low, high, dim):
    n = block.shape[dim]
    low = jnp.expand_dims(low, dim)
    high = jnp.expand_dims(high, dim)
    minus = jnp.concatenate([low, lax.slice_in_dim(block, 0, n - 1, axis=dim)], axis=dim)
    plus = jnp.concatenate([lax.slice_in_dim(block, 1, n, axis=dim), high], axis=dim)
    return minus, plus


def membrane(voltage, gate_state, cell_type, gate_half, gate_slope, gate_tau, conduct, reversal):
    gate_count = gate_half.shape[0]
    lead_shape = (-1,) + (1,) * voltage.ndim
    gate_sign = jnp.where(jnp.arange(gate_count) % 2 == 0, 1.0, -1.0).astype(jnp.float32)
    exponent = (gate_sign / gate_slope).reshape(lead_shape) * (
        voltage[None] - gate_half.reshape(lead_shape)
    )
    steady = jax.nn.sigmoid(exponent)
    time_const = gate_tau.reshape(lead_shape) * (0.5 + steady)
    gate_state = steady + (gate_state - steady) * jnp.exp(-DT_HEART / time_const)
    weight = jnp.zeros(gate_state[0::2].shape, jnp.float32)
    for cell_kind in range(conduct.shape[0]):
        weight = weight + jnp.where(
            cell_type[None] == cell_kind, conduct[cell_kind].reshape(lead_shape), 0.0
        )
    ion_current = jnp.sum(
        weight
        * gate_state[0::2]
        * gate_state[1::2]
        * (voltage[None] - reversal.reshape(lead_shape)),
        axis=0,
    )
    return (gate_state, ion_current)


def heart_laplace(voltage):
    parts = []
    for axis, dim in (("gx", 0), ("gy", 1), ("gz", 2)):
        low, high = face_halos(voltage, axis, dim)
        minus, plus = shifted(voltage, low, high, dim)
        parts.append((plus, minus))
    total = parts[0][0] + parts[0][1]
    total = total + parts[1][0] + parts[1][1]
    total = total + parts[2][0] + parts[2][1]
    return total - 6.0 * voltage


def exchange(top, bottom, axis):
    count = lax.axis_size(axis)
    if count == 2:
        index = lax.axis_index(axis)
        got = lax.ppermute(jnp.where(index == 0, top, bottom), axis, [(0, 1), (1, 0)])
        zero = jnp.zeros_like(got)
        return jnp.where(index == 1, got, zero), jnp.where(index == 0, got, zero)
    forward = [(i, i + 1) for i in range(count - 1)]
    backward = [(i + 1, i) for i in range(count - 1)]
    return lax.ppermute(top, axis, forward), lax.ppermute(bottom, axis, backward)


def write_faces(x, value, xf_lo, xf_hi, yf_lo, yf_hi, zf_lo, zf_hi):
    nx = yf_lo.shape[1]
    ny, nz = value.shape

    @pl.when(x == 0)
    def _():
        xf_lo[0] = value

    @pl.when(x == nx - 1)
    def _():
        xf_hi[0] = value

    yf_lo[0, x] = value[0:1, :]
    yf_hi[0, x] = value[ny - 1:ny, :]
    flipped = value.T
    zf_lo[0, pl.ds(x, 1), :] = flipped[0:1, :]
    zf_hi[0, pl.ds(x, 1), :] = flipped[nz - 1:nz, :]


def sweep_kernel(first, second, d_ref, r_ref, p_ref, fxp, fxm, fyp, fym, fzp, fzm, dg_ref,
                 xlo, xhi, ylo, yhi, zedge, r_out, d_out, p_out, *face_out):
    nx, ny, nz = d_ref.shape[1], d_ref.shape[2], d_ref.shape[3]
    row = lax.broadcasted_iota(jnp.int32, (ny, nz), 0)
    lane = lax.broadcasted_iota(jnp.int32, (ny, nz), 1)

    def body(x, carry):
        centre = d_ref[0, x]
        below = d_ref[0, jnp.maximum(x - 1, 0)]
        above = d_ref[0, jnp.minimum(x + 1, nx - 1)]
        x_minus = jnp.where(x == 0, xlo[0], below)
        x_plus = jnp.where(x == nx - 1, xhi[0], above)
        y_minus = jnp.where(row == 0, ylo[0, x], pltpu.roll(centre, 1, 0))
        y_plus = jnp.where(row == ny - 1, yhi[0, x], pltpu.roll(centre, ny - 1, 0))
        edge = zedge[0, x]
        z_minus = jnp.where(lane == 0, edge, pltpu.roll(centre, 1, 1))
        z_plus = jnp.where(lane == nz - 1, edge, pltpu.roll(centre, nz - 1, 1))
        beside = fxp[x] * x_plus + fxm[x] * x_minus
        beside = beside + fyp[x] * y_plus + fym[x] * y_minus
        beside = beside + fzp[x] * z_plus + fzm[x] * z_minus
        diag = dg_ref[x]
        residual = r_ref[0, x] - (diag * centre - beside)
        step_dir = first * centre + second * (residual / diag)
        r_out[0, x] = residual
        d_out[0, x] = step_dir
        p_out[0, x] = p_ref[0, x] + step_dir
        write_faces(x, step_dir, *face_out)
        return carry

    lax.fori_loop(0, nx, body, 0)


def initial_kernel(mid, r_ref, dg_ref, d_out, *face_out):
    nx = r_ref.shape[1]

    def body(x, carry):
        step_dir = r_ref[0, x] / dg_ref[x] / mid
        d_out[0, x] = step_dir
        write_faces(x, step_dir, *face_out)
        return carry

    lax.fori_loop(0, nx, body, 0)


def specs(shape):
    steps, nx, ny, nz = shape
    full = pl.BlockSpec((1, nx, ny, nz), lambda s: (s, 0, 0, 0))
    fixed = pl.BlockSpec((nx, ny, nz), lambda s: (0, 0, 0))
    x_face = pl.BlockSpec((1, ny, nz), lambda s: (s, 0, 0))
    y_face = pl.BlockSpec((1, nx, 1, nz), lambda s: (s, 0, 0, 0))
    z_face = pl.BlockSpec((1, nx, ny), lambda s: (s, 0, 0))
    face_specs = [x_face, x_face, y_face, y_face, z_face, z_face]
    face_shapes = [
        jax.ShapeDtypeStruct((steps, ny, nz), jnp.float32),
        jax.ShapeDtypeStruct((steps, ny, nz), jnp.float32),
        jax.ShapeDtypeStruct((steps, nx, 1, nz), jnp.float32),
        jax.ShapeDtypeStruct((steps, nx, 1, nz), jnp.float32),
        jax.ShapeDtypeStruct((steps, nx, ny), jnp.float32),
        jax.ShapeDtypeStruct((steps, nx, ny), jnp.float32),
    ]
    return full, fixed, face_specs, face_shapes


def run_initial(mid, source, diagonal):
    full, fixed, face_specs, face_shapes = specs(source.shape)
    shape = jax.ShapeDtypeStruct(source.shape, jnp.float32)
    size = source.size
    outs = pl.pallas_call(
        functools.partial(initial_kernel, mid),
        grid=(source.shape[0],),
        in_specs=[full, fixed],
        out_specs=[full] + face_specs,
        out_shape=[shape] + face_shapes,
        cost_estimate=pl.CostEstimate(flops=2 * size, transcendentals=0, bytes_accessed=8 * size + 4 * size // source.shape[0]),
        name="chebyshev_start",
    )(source, diagonal)
    return outs[0], outs[1:]


def run_sweep(first, second, step_dir, residual, potential, faces, diagonal, halos):
    full, fixed, face_specs, face_shapes = specs(step_dir.shape)
    steps, nx, ny, nz = step_dir.shape
    x_face, y_face = face_specs[0], face_specs[2]
    shape = jax.ShapeDtypeStruct(step_dir.shape, jnp.float32)
    size = step_dir.size
    outs = pl.pallas_call(
        functools.partial(sweep_kernel, first, second),
        grid=(steps,),
        in_specs=[full, full, full] + [fixed] * 7 + [x_face, x_face, y_face, y_face, full],
        out_specs=[full, full, full] + face_specs,
        out_shape=[shape, shape, shape] + face_shapes,
        cost_estimate=pl.CostEstimate(flops=30 * size, transcendentals=0, bytes_accessed=4 * 7 * size + 4 * 7 * size // steps),
        name="chebyshev_sweep",
    )(step_dir, residual, potential, *faces, diagonal, *halos)
    return outs[0], outs[1], outs[2], outs[3:]


def local(
    heart_state,
    cell_type,
    gate_half,
    gate_slope,
    gate_tau,
    conduct,
    reversal,
    block_device,
    block_row,
    tissue,
    tissue_sigma,
):
    voltage = heart_state[0]
    gate_state = heart_state[1:]
    heart_x, heart_y, row_len = voltage.shape
    blocks = heart_x * heart_y
    devices = lax.axis_size("gx") * lax.axis_size("gy") * lax.axis_size("gz")
    capacity = 3 * blocks // devices
    slots = devices * capacity
    torso_x, torso_y, torso_z = tissue.shape
    torso_rows = torso_x * torso_y

    dest_dev = block_device.reshape(blocks)
    dest_row = block_row.reshape(blocks)
    one_hot = (dest_dev[:, None] == jnp.arange(devices, dtype=jnp.int32)[None, :]).astype(jnp.int32)
    running = jnp.cumsum(one_hot, axis=0) - 1
    slot_rank = jnp.sum(running * one_hot, axis=1)
    slot_index = dest_dev * capacity + slot_rank
    slot_match = slot_index[None, :] == jnp.arange(slots, dtype=jnp.int32)[:, None]
    slot_used = jnp.any(slot_match, axis=1)
    slot_block = jnp.argmax(slot_match, axis=1).astype(jnp.int32)
    send_rows = jnp.where(slot_used, dest_row[slot_block], torso_rows)
    recv_rows = lax.all_to_all(
        send_rows.reshape(devices, capacity), ("gx", "gy", "gz"), 0, 0, tiled=True
    ).reshape(slots)
    row_match = recv_rows[None, :] == jnp.arange(torso_rows, dtype=jnp.int32)[:, None]
    row_used = jnp.any(row_match, axis=1)
    row_slot = jnp.argmax(row_match, axis=1).astype(jnp.int32)

    currents = []
    for time_step in range(STEPS):
        gate_state, ion_current = membrane(
            voltage, gate_state, cell_type, gate_half, gate_slope, gate_tau, conduct, reversal
        )
        current = SIGMA_HEART * heart_laplace(voltage)
        currents.append(current)
        voltage = voltage + DT_HEART * (current - ion_current)
    heart_next = jnp.concatenate([voltage[None], gate_state], axis=0)

    payload = jnp.stack([item.reshape(blocks, row_len) for item in currents], axis=0)
    send_values = jnp.where(slot_used[None, :, None], jnp.take(payload, slot_block, axis=1), 0.0)
    received = lax.all_to_all(
        send_values.reshape(STEPS, devices, capacity, row_len),
        ("gx", "gy", "gz"),
        1,
        1,
        tiled=True,
    ).reshape(STEPS, slots, row_len)
    source = jnp.where(row_used[None, :, None], jnp.take(received, row_slot, axis=1), 0.0)
    source = source.reshape(STEPS, torso_x, torso_y, torso_z)

    sigma = []
    for dim_index in range(3):
        value = jnp.zeros(tissue.shape, jnp.float32)
        for tissue_kind in range(tissue_sigma.shape[0]):
            value = value + jnp.where(tissue == tissue_kind, tissue_sigma[tissue_kind, dim_index], 0.0)
        sigma.append(value)
    faces = []
    for dim_index, axis in enumerate(("gx", "gy", "gz")):
        low, high = face_halos(sigma[dim_index], axis, dim_index)
        minus, plus = shifted(sigma[dim_index], low, high, dim_index)
        faces.append(0.5 * (sigma[dim_index] + plus))
        faces.append(0.5 * (sigma[dim_index] + minus))
    diagonal = SCREEN + faces[0] + faces[1] + faces[2] + faces[3] + faces[4] + faces[5]

    spectrum_mid, first_coef, second_coef = chebyshev_weights(SWEEPS)
    residual = source
    step_dir, dir_faces = run_initial(spectrum_mid, residual, diagonal)
    potential = step_dir
    lane = lax.broadcasted_iota(jnp.int32, step_dir.shape, 3)
    for sweep in range(1, SWEEPS):
        x_low, x_high = exchange(dir_faces[1], dir_faces[0], "gx")
        y_low, y_high = exchange(dir_faces[3], dir_faces[2], "gy")
        z_low, z_high = exchange(dir_faces[5], dir_faces[4], "gz")
        zedge = jnp.where(lane == 0, z_low[..., None], jnp.where(lane == torso_z - 1, z_high[..., None], 0.0))
        halos = (x_low, x_high, y_low, y_high, zedge)
        residual, step_dir, potential, dir_faces = run_sweep(
            first_coef[sweep - 1], second_coef[sweep - 1], step_dir, residual, potential, faces, diagonal, halos
        )
    return (heart_next, jnp.transpose(potential, (1, 2, 0, 3)))


def solution(mesh):
    in_specs = (
        P(None, "gx", "gy", "gz"),
        P("gx", "gy", "gz"),
        P(),
        P(),
        P(),
        P(),
        P(),
        P("gx", "gy", "gz"),
        P("gx", "gy", "gz"),
        P("gx", "gy", "gz"),
        P(),
    )
    out_specs = (P(None, "gx", "gy", "gz"), P("gx", "gy", None, "gz"))
    return jax.shard_map(local, mesh=mesh, in_specs=in_specs, out_specs=out_specs, check_vma=False)
```

```python
import jax
import jax.numpy as jnp
from jax import lax
from jax.sharding import PartitionSpec as P
from jax.experimental import pallas as pl
from jax.experimental.pallas import tpu as pltpu
import functools

STEPS = 4
SWEEPS = 4


DT_HEART = 0.05
SIGMA_HEART = 1.0
SCREEN = 0.05
LOW_EDGE = 0.1
HIGH_EDGE = 1.9


def chebyshev_weights(sweep_count):
    spectrum_mid = 0.5 * (HIGH_EDGE + LOW_EDGE)
    half_width = 0.5 * (HIGH_EDGE - LOW_EDGE)
    half_ratio = spectrum_mid / half_width
    rho_old = 1.0 / half_ratio
    first_coef = []
    second_coef = []
    for sweep in range(1, sweep_count):
        rho_new = 1.0 / (2.0 * half_ratio - rho_old)
        first_coef.append(rho_new * rho_old)
        second_coef.append(2.0 * rho_new / half_width)
        rho_old = rho_new
    return (spectrum_mid, first_coef, second_coef)


def face_halos(block, axis, dim):
    top = lax.index_in_dim(block, block.shape[dim] - 1, axis=dim, keepdims=False)
    bottom = lax.index_in_dim(block, 0, axis=dim, keepdims=False)
    return exchange(top, bottom, axis)


def shifted(block, low, high, dim):
    n = block.shape[dim]
    low = jnp.expand_dims(low, dim)
    high = jnp.expand_dims(high, dim)
    minus = jnp.concatenate([low, lax.slice_in_dim(block, 0, n - 1, axis=dim)], axis=dim)
    plus = jnp.concatenate([lax.slice_in_dim(block, 1, n, axis=dim), high], axis=dim)
    return minus, plus


def membrane(voltage, gate_state, cell_type, gate_half, gate_slope, gate_tau, conduct, reversal):
    gate_count = gate_half.shape[0]
    lead_shape = (-1,) + (1,) * voltage.ndim
    gate_sign = jnp.where(jnp.arange(gate_count) % 2 == 0, 1.0, -1.0).astype(jnp.float32)
    exponent = (gate_sign / gate_slope).reshape(lead_shape) * (
        voltage[None] - gate_half.reshape(lead_shape)
    )
    steady = jax.nn.sigmoid(exponent)
    time_const = gate_tau.reshape(lead_shape) * (0.5 + steady)
    gate_state = steady + (gate_state - steady) * jnp.exp(-DT_HEART / time_const)
    weight = jnp.zeros(gate_state[0::2].shape, jnp.float32)
    for cell_kind in range(conduct.shape[0]):
        weight = weight + jnp.where(
            cell_type[None] == cell_kind, conduct[cell_kind].reshape(lead_shape), 0.0
        )
    ion_current = jnp.sum(
        weight
        * gate_state[0::2]
        * gate_state[1::2]
        * (voltage[None] - reversal.reshape(lead_shape)),
        axis=0,
    )
    return (gate_state, ion_current)


def heart_laplace(voltage):
    parts = []
    for axis, dim in (("gx", 0), ("gy", 1), ("gz", 2)):
        low, high = face_halos(voltage, axis, dim)
        minus, plus = shifted(voltage, low, high, dim)
        parts.append((plus, minus))
    total = parts[0][0] + parts[0][1]
    total = total + parts[1][0] + parts[1][1]
    total = total + parts[2][0] + parts[2][1]
    return total - 6.0 * voltage


def exchange(top, bottom, axis):
    count = lax.axis_size(axis)
    if count == 2:
        index = lax.axis_index(axis)
        got = lax.ppermute(jnp.where(index == 0, top, bottom), axis, [(0, 1), (1, 0)])
        zero = jnp.zeros_like(got)
        return jnp.where(index == 1, got, zero), jnp.where(index == 0, got, zero)
    forward = [(i, i + 1) for i in range(count - 1)]
    backward = [(i + 1, i) for i in range(count - 1)]
    return lax.ppermute(top, axis, forward), lax.ppermute(bottom, axis, backward)


def write_faces(x, value, columns, xf_lo, xf_hi, yf_lo, yf_hi, zf_lo, zf_hi):
    nx = yf_lo.shape[1]
    ny, nz = value.shape
    half = nz // 2
    lane = lax.broadcasted_iota(jnp.int32, (ny, nz), 1)

    @pl.when(x == 0)
    def _():
        xf_lo[0] = value

    @pl.when(x == nx - 1)
    def _():
        xf_hi[0] = value

    yf_lo[0, x] = value[0:1, :]
    yf_hi[0, x] = value[ny - 1:ny, :]
    columns = jnp.where(lane == x, jnp.broadcast_to(value[:, 0:1], (ny, nz)), columns)
    columns = jnp.where(lane == half + x, jnp.broadcast_to(value[:, nz - 1:nz], (ny, nz)), columns)
    return columns


def finish_faces(columns, xf_lo, xf_hi, yf_lo, yf_hi, zf_lo, zf_hi):
    nx = yf_lo.shape[1]
    half = columns.shape[1] // 2
    flipped = columns.T
    zf_lo[0] = flipped[0:nx, :]
    zf_hi[0] = flipped[half:half + nx, :]


def sweep_kernel(first, second, d_ref, r_ref, p_ref, fxp, fxm, fyp, fym, fzp, fzm, dg_ref,
                 xlo, xhi, ylo, yhi, zlo, zhi, r_out, d_out, p_out, *face_out):
    nx, ny, nz = d_ref.shape[1], d_ref.shape[2], d_ref.shape[3]
    row = lax.broadcasted_iota(jnp.int32, (ny, nz), 0)
    lane = lax.broadcasted_iota(jnp.int32, (ny, nz), 1)
    blank = jnp.zeros((nz - nx, ny), jnp.float32)
    low_cols = jnp.concatenate([zlo[0], blank], axis=0).T
    high_rows = zhi[0]
    high_cols = jnp.concatenate([high_rows[1:nx], blank, high_rows[0:1]], axis=0).T

    def body(x, carry):
        centre = d_ref[0, x]
        below = d_ref[0, jnp.maximum(x - 1, 0)]
        above = d_ref[0, jnp.minimum(x + 1, nx - 1)]
        x_minus = jnp.where(x == 0, xlo[0], below)
        x_plus = jnp.where(x == nx - 1, xhi[0], above)
        y_minus = jnp.where(row == 0, ylo[0, x], pltpu.roll(centre, 1, 0))
        y_plus = jnp.where(row == ny - 1, yhi[0, x], pltpu.roll(centre, ny - 1, 0))
        turn = lax.rem(nz - x, nz)
        z_minus = jnp.where(lane == 0, pltpu.roll(low_cols, turn, 1), pltpu.roll(centre, 1, 1))
        z_plus = jnp.where(lane == nz - 1, pltpu.roll(high_cols, turn, 1), pltpu.roll(centre, nz - 1, 1))
        beside = fxp[x] * x_plus + fxm[x] * x_minus
        beside = beside + fyp[x] * y_plus + fym[x] * y_minus
        beside = beside + fzp[x] * z_plus + fzm[x] * z_minus
        diag = dg_ref[x]
        residual = r_ref[0, x] - (diag * centre - beside)
        step_dir = first * centre + second * (residual / diag)
        r_out[0, x] = residual
        d_out[0, x] = step_dir
        p_out[0, x] = p_ref[0, x] + step_dir
        return write_faces(x, step_dir, carry, *face_out)

    columns = lax.fori_loop(0, nx, body, jnp.zeros((ny, nz), jnp.float32))
    finish_faces(columns, *face_out)


def initial_kernel(mid, r_ref, dg_ref, d_out, *face_out):
    nx, ny, nz = r_ref.shape[1], r_ref.shape[2], r_ref.shape[3]

    def body(x, carry):
        step_dir = r_ref[0, x] / dg_ref[x] / mid
        d_out[0, x] = step_dir
        return write_faces(x, step_dir, carry, *face_out)

    columns = lax.fori_loop(0, nx, body, jnp.zeros((ny, nz), jnp.float32))
    finish_faces(columns, *face_out)


def specs(shape):
    steps, nx, ny, nz = shape
    full = pl.BlockSpec((1, nx, ny, nz), lambda s: (s, 0, 0, 0))
    fixed = pl.BlockSpec((nx, ny, nz), lambda s: (0, 0, 0))
    x_face = pl.BlockSpec((1, ny, nz), lambda s: (s, 0, 0))
    y_face = pl.BlockSpec((1, nx, 1, nz), lambda s: (s, 0, 0, 0))
    z_face = pl.BlockSpec((1, nx, ny), lambda s: (s, 0, 0))
    face_specs = [x_face, x_face, y_face, y_face, z_face, z_face]
    face_shapes = [
        jax.ShapeDtypeStruct((steps, ny, nz), jnp.float32),
        jax.ShapeDtypeStruct((steps, ny, nz), jnp.float32),
        jax.ShapeDtypeStruct((steps, nx, 1, nz), jnp.float32),
        jax.ShapeDtypeStruct((steps, nx, 1, nz), jnp.float32),
        jax.ShapeDtypeStruct((steps, nx, ny), jnp.float32),
        jax.ShapeDtypeStruct((steps, nx, ny), jnp.float32),
    ]
    return full, fixed, face_specs, face_shapes


def run_initial(mid, source, diagonal):
    full, fixed, face_specs, face_shapes = specs(source.shape)
    shape = jax.ShapeDtypeStruct(source.shape, jnp.float32)
    size = source.size
    outs = pl.pallas_call(
        functools.partial(initial_kernel, mid),
        grid=(source.shape[0],),
        in_specs=[full, fixed],
        out_specs=[full] + face_specs,
        out_shape=[shape] + face_shapes,
        cost_estimate=pl.CostEstimate(flops=2 * size, transcendentals=0, bytes_accessed=8 * size + 4 * size // source.shape[0]),
        name="chebyshev_start",
    )(source, diagonal)
    return outs[0], outs[1:]


def run_sweep(first, second, step_dir, residual, potential, faces, diagonal, halos):
    full, fixed, face_specs, face_shapes = specs(step_dir.shape)
    steps, nx, ny, nz = step_dir.shape
    x_face, y_face = face_specs[0], face_specs[2]
    shape = jax.ShapeDtypeStruct(step_dir.shape, jnp.float32)
    size = step_dir.size
    outs = pl.pallas_call(
        functools.partial(sweep_kernel, first, second),
        grid=(steps,),
        in_specs=[full, full, full] + [fixed] * 7 + [x_face, x_face, y_face, y_face, face_specs[4], face_specs[4]],
        out_specs=[full, full, full] + face_specs,
        out_shape=[shape, shape, shape] + face_shapes,
        cost_estimate=pl.CostEstimate(flops=30 * size, transcendentals=0, bytes_accessed=4 * 7 * size + 4 * 7 * size // steps),
        name="chebyshev_sweep",
    )(step_dir, residual, potential, *faces, diagonal, *halos)
    return outs[0], outs[1], outs[2], outs[3:]


def local(
    heart_state,
    cell_type,
    gate_half,
    gate_slope,
    gate_tau,
    conduct,
    reversal,
    block_device,
    block_row,
    tissue,
    tissue_sigma,
):
    voltage = heart_state[0]
    gate_state = heart_state[1:]
    heart_x, heart_y, row_len = voltage.shape
    blocks = heart_x * heart_y
    devices = lax.axis_size("gx") * lax.axis_size("gy") * lax.axis_size("gz")
    capacity = 3 * blocks // devices
    slots = devices * capacity
    torso_x, torso_y, torso_z = tissue.shape
    torso_rows = torso_x * torso_y

    dest_dev = block_device.reshape(blocks)
    dest_row = block_row.reshape(blocks)
    one_hot = (dest_dev[:, None] == jnp.arange(devices, dtype=jnp.int32)[None, :]).astype(jnp.int32)
    running = jnp.cumsum(one_hot, axis=0) - 1
    slot_rank = jnp.sum(running * one_hot, axis=1)
    slot_index = dest_dev * capacity + slot_rank
    slot_match = slot_index[None, :] == jnp.arange(slots, dtype=jnp.int32)[:, None]
    slot_used = jnp.any(slot_match, axis=1)
    slot_block = jnp.argmax(slot_match, axis=1).astype(jnp.int32)
    send_rows = jnp.where(slot_used, dest_row[slot_block], torso_rows)
    recv_rows = lax.all_to_all(
        send_rows.reshape(devices, capacity), ("gx", "gy", "gz"), 0, 0, tiled=True
    ).reshape(slots)
    row_match = recv_rows[None, :] == jnp.arange(torso_rows, dtype=jnp.int32)[:, None]
    row_used = jnp.any(row_match, axis=1)
    row_slot = jnp.argmax(row_match, axis=1).astype(jnp.int32)

    currents = []
    for time_step in range(STEPS):
        gate_state, ion_current = membrane(
            voltage, gate_state, cell_type, gate_half, gate_slope, gate_tau, conduct, reversal
        )
        current = SIGMA_HEART * heart_laplace(voltage)
        currents.append(current)
        voltage = voltage + DT_HEART * (current - ion_current)
    heart_next = jnp.concatenate([voltage[None], gate_state], axis=0)

    payload = jnp.stack([item.reshape(blocks, row_len) for item in currents], axis=0)
    send_values = jnp.where(slot_used[None, :, None], jnp.take(payload, slot_block, axis=1), 0.0)
    received = lax.all_to_all(
        send_values.reshape(STEPS, devices, capacity, row_len),
        ("gx", "gy", "gz"),
        1,
        1,
        tiled=True,
    ).reshape(STEPS, slots, row_len)
    source = jnp.where(row_used[None, :, None], jnp.take(received, row_slot, axis=1), 0.0)
    source = source.reshape(STEPS, torso_x, torso_y, torso_z)

    sigma = []
    for dim_index in range(3):
        value = jnp.zeros(tissue.shape, jnp.float32)
        for tissue_kind in range(tissue_sigma.shape[0]):
            value = value + jnp.where(tissue == tissue_kind, tissue_sigma[tissue_kind, dim_index], 0.0)
        sigma.append(value)
    faces = []
    for dim_index, axis in enumerate(("gx", "gy", "gz")):
        low, high = face_halos(sigma[dim_index], axis, dim_index)
        minus, plus = shifted(sigma[dim_index], low, high, dim_index)
        faces.append(0.5 * (sigma[dim_index] + plus))
        faces.append(0.5 * (sigma[dim_index] + minus))
    diagonal = SCREEN + faces[0] + faces[1] + faces[2] + faces[3] + faces[4] + faces[5]

    spectrum_mid, first_coef, second_coef = chebyshev_weights(SWEEPS)
    residual = source
    step_dir, dir_faces = run_initial(spectrum_mid, residual, diagonal)
    potential = step_dir
    for sweep in range(1, SWEEPS):
        x_low, x_high = exchange(dir_faces[1], dir_faces[0], "gx")
        y_low, y_high = exchange(dir_faces[3], dir_faces[2], "gy")
        z_low, z_high = exchange(dir_faces[5], dir_faces[4], "gz")
        halos = (x_low, x_high, y_low, y_high, z_low, z_high)
        residual, step_dir, potential, dir_faces = run_sweep(
            first_coef[sweep - 1], second_coef[sweep - 1], step_dir, residual, potential, faces, diagonal, halos
        )
    return (heart_next, jnp.transpose(potential, (1, 2, 0, 3)))


def solution(mesh):
    in_specs = (
        P(None, "gx", "gy", "gz"),
        P("gx", "gy", "gz"),
        P(),
        P(),
        P(),
        P(),
        P(),
        P("gx", "gy", "gz"),
        P("gx", "gy", "gz"),
        P("gx", "gy", "gz"),
        P(),
    )
    out_specs = (P(None, "gx", "gy", "gz"), P("gx", "gy", None, "gz"))
    return jax.shard_map(local, mesh=mesh, in_specs=in_specs, out_specs=out_specs, check_vma=False)
```

```python
import jax
import jax.numpy as jnp
from jax import lax
from jax.sharding import PartitionSpec as P
from jax.experimental import pallas as pl
from jax.experimental.pallas import tpu as pltpu
import functools

STEPS = 4
SWEEPS = 4


DT_HEART = 0.05
SIGMA_HEART = 1.0
SCREEN = 0.05
LOW_EDGE = 0.1
HIGH_EDGE = 1.9


def chebyshev_weights(sweep_count):
    spectrum_mid = 0.5 * (HIGH_EDGE + LOW_EDGE)
    half_width = 0.5 * (HIGH_EDGE - LOW_EDGE)
    half_ratio = spectrum_mid / half_width
    rho_old = 1.0 / half_ratio
    first_coef = []
    second_coef = []
    for sweep in range(1, sweep_count):
        rho_new = 1.0 / (2.0 * half_ratio - rho_old)
        first_coef.append(rho_new * rho_old)
        second_coef.append(2.0 * rho_new / half_width)
        rho_old = rho_new
    return (spectrum_mid, first_coef, second_coef)


def face_halos(block, axis, dim):
    top = lax.index_in_dim(block, block.shape[dim] - 1, axis=dim, keepdims=False)
    bottom = lax.index_in_dim(block, 0, axis=dim, keepdims=False)
    return exchange(top, bottom, axis)


def shifted(block, low, high, dim):
    n = block.shape[dim]
    low = jnp.expand_dims(low, dim)
    high = jnp.expand_dims(high, dim)
    minus = jnp.concatenate([low, lax.slice_in_dim(block, 0, n - 1, axis=dim)], axis=dim)
    plus = jnp.concatenate([lax.slice_in_dim(block, 1, n, axis=dim), high], axis=dim)
    return minus, plus


def membrane(voltage, gate_state, cell_type, gate_half, gate_slope, gate_tau, conduct, reversal):
    gate_count = gate_half.shape[0]
    lead_shape = (-1,) + (1,) * voltage.ndim
    gate_sign = jnp.where(jnp.arange(gate_count) % 2 == 0, 1.0, -1.0).astype(jnp.float32)
    exponent = (gate_sign / gate_slope).reshape(lead_shape) * (
        voltage[None] - gate_half.reshape(lead_shape)
    )
    steady = jax.nn.sigmoid(exponent)
    time_const = gate_tau.reshape(lead_shape) * (0.5 + steady)
    gate_state = steady + (gate_state - steady) * jnp.exp(-DT_HEART / time_const)
    weight = jnp.zeros(gate_state[0::2].shape, jnp.float32)
    for cell_kind in range(conduct.shape[0]):
        weight = weight + jnp.where(
            cell_type[None] == cell_kind, conduct[cell_kind].reshape(lead_shape), 0.0
        )
    ion_current = jnp.sum(
        weight
        * gate_state[0::2]
        * gate_state[1::2]
        * (voltage[None] - reversal.reshape(lead_shape)),
        axis=0,
    )
    return (gate_state, ion_current)


def faces_of(block, dim):
    top = lax.index_in_dim(block, block.shape[dim] - 1, axis=dim, keepdims=False)
    bottom = lax.index_in_dim(block, 0, axis=dim, keepdims=False)
    return top, bottom


def heart_laplace(voltage, riders=None):
    parts = []
    carried = []
    for index, (axis, dim) in enumerate((("gx", 0), ("gy", 1), ("gz", 2))):
        pairs = [faces_of(voltage, dim)]
        if riders is not None:
            pairs.append(riders[index])
        got = exchange_group(pairs, axis)
        minus, plus = shifted(voltage, got[0][0], got[0][1], dim)
        parts.append((plus, minus))
        carried.append(got[1:])
    total = parts[0][0] + parts[0][1]
    total = total + parts[1][0] + parts[1][1]
    total = total + parts[2][0] + parts[2][1]
    return total - 6.0 * voltage, carried


def exchange(top, bottom, axis):
    count = lax.axis_size(axis)
    if count == 2:
        index = lax.axis_index(axis)
        got = lax.ppermute(jnp.where(index == 0, top, bottom), axis, [(0, 1), (1, 0)])
        zero = jnp.zeros_like(got)
        return jnp.where(index == 1, got, zero), jnp.where(index == 0, got, zero)
    forward = [(i, i + 1) for i in range(count - 1)]
    backward = [(i + 1, i) for i in range(count - 1)]
    return lax.ppermute(top, axis, forward), lax.ppermute(bottom, axis, backward)


def exchange_group(pairs, axis):
    if len(pairs) == 1:
        return [exchange(pairs[0][0], pairs[0][1], axis)]
    top = jnp.concatenate([item.reshape(-1) for item, _ in pairs])
    bottom = jnp.concatenate([item.reshape(-1) for _, item in pairs])
    low, high = exchange(top, bottom, axis)
    result = []
    offset = 0
    for item, _ in pairs:
        size = item.size
        result.append((low[offset:offset + size].reshape(item.shape), high[offset:offset + size].reshape(item.shape)))
        offset += size
    return result


def write_faces(x, value, columns, xf_lo, xf_hi, yf_lo, yf_hi, zf_lo, zf_hi):
    nx = yf_lo.shape[1]
    ny, nz = value.shape
    half = nz // 2
    lane = lax.broadcasted_iota(jnp.int32, (ny, nz), 1)

    @pl.when(x == 0)
    def _():
        xf_lo[0] = value

    @pl.when(x == nx - 1)
    def _():
        xf_hi[0] = value

    yf_lo[0, x] = value[0:1, :]
    yf_hi[0, x] = value[ny - 1:ny, :]
    columns = jnp.where(lane == x, jnp.broadcast_to(value[:, 0:1], (ny, nz)), columns)
    columns = jnp.where(lane == half + x, jnp.broadcast_to(value[:, nz - 1:nz], (ny, nz)), columns)
    return columns


def finish_faces(columns, xf_lo, xf_hi, yf_lo, yf_hi, zf_lo, zf_hi):
    nx = yf_lo.shape[1]
    half = columns.shape[1] // 2
    flipped = columns.T
    zf_lo[0] = flipped[0:nx, :]
    zf_hi[0] = flipped[half:half + nx, :]


def sweep_kernel(first, second, d_ref, r_ref, p_ref, fxp, fxm, fyp, fym, fzp, fzm, dg_ref, inv_ref,
                 xlo, xhi, ylo, yhi, zlo, zhi, r_out, d_out, p_out, *face_out):
    nx, ny, nz = d_ref.shape[1], d_ref.shape[2], d_ref.shape[3]
    row = lax.broadcasted_iota(jnp.int32, (ny, nz), 0)
    lane = lax.broadcasted_iota(jnp.int32, (ny, nz), 1)
    blank = jnp.zeros((nz - nx, ny), jnp.float32)
    low_cols = jnp.concatenate([zlo[0], blank], axis=0).T
    high_rows = zhi[0]
    high_cols = jnp.concatenate([high_rows[1:nx], blank, high_rows[0:1]], axis=0).T

    def body(x, carry):
        centre = d_ref[0, x]
        below = d_ref[0, jnp.maximum(x - 1, 0)]
        above = d_ref[0, jnp.minimum(x + 1, nx - 1)]
        x_minus = jnp.where(x == 0, xlo[0], below)
        x_plus = jnp.where(x == nx - 1, xhi[0], above)
        y_minus = jnp.where(row == 0, ylo[0, x], pltpu.roll(centre, 1, 0))
        y_plus = jnp.where(row == ny - 1, yhi[0, x], pltpu.roll(centre, ny - 1, 0))
        turn = lax.rem(nz - x, nz)
        z_minus = jnp.where(lane == 0, pltpu.roll(low_cols, turn, 1), pltpu.roll(centre, 1, 1))
        z_plus = jnp.where(lane == nz - 1, pltpu.roll(high_cols, turn, 1), pltpu.roll(centre, nz - 1, 1))
        beside = fxp[x] * x_plus + fxm[x] * x_minus
        beside = beside + fyp[x] * y_plus + fym[x] * y_minus
        beside = beside + fzp[x] * z_plus + fzm[x] * z_minus
        diag = dg_ref[x]
        residual = r_ref[0, x] - (diag * centre - beside)
        step_dir = first * centre + second * (residual * inv_ref[x])
        r_out[0, x] = residual
        d_out[0, x] = step_dir
        p_out[0, x] = p_ref[0, x] + step_dir
        return write_faces(x, step_dir, carry, *face_out)

    columns = lax.fori_loop(0, nx, body, jnp.zeros((ny, nz), jnp.float32), unroll=2)
    finish_faces(columns, *face_out)


def initial_kernel(mid, r_ref, inv_ref, d_out, *face_out):
    nx, ny, nz = r_ref.shape[1], r_ref.shape[2], r_ref.shape[3]

    def body(x, carry):
        step_dir = r_ref[0, x] * inv_ref[x] * (1.0 / mid)
        d_out[0, x] = step_dir
        return write_faces(x, step_dir, carry, *face_out)

    columns = lax.fori_loop(0, nx, body, jnp.zeros((ny, nz), jnp.float32), unroll=2)
    finish_faces(columns, *face_out)


def specs(shape):
    steps, nx, ny, nz = shape
    full = pl.BlockSpec((1, nx, ny, nz), lambda s: (s, 0, 0, 0))
    fixed = pl.BlockSpec((nx, ny, nz), lambda s: (0, 0, 0))
    x_face = pl.BlockSpec((1, ny, nz), lambda s: (s, 0, 0))
    y_face = pl.BlockSpec((1, nx, 1, nz), lambda s: (s, 0, 0, 0))
    z_face = pl.BlockSpec((1, nx, ny), lambda s: (s, 0, 0))
    face_specs = [x_face, x_face, y_face, y_face, z_face, z_face]
    face_shapes = [
        jax.ShapeDtypeStruct((steps, ny, nz), jnp.float32),
        jax.ShapeDtypeStruct((steps, ny, nz), jnp.float32),
        jax.ShapeDtypeStruct((steps, nx, 1, nz), jnp.float32),
        jax.ShapeDtypeStruct((steps, nx, 1, nz), jnp.float32),
        jax.ShapeDtypeStruct((steps, nx, ny), jnp.float32),
        jax.ShapeDtypeStruct((steps, nx, ny), jnp.float32),
    ]
    return full, fixed, face_specs, face_shapes


def run_initial(mid, source, inverse):
    full, fixed, face_specs, face_shapes = specs(source.shape)
    shape = jax.ShapeDtypeStruct(source.shape, jnp.float32)
    size = source.size
    outs = pl.pallas_call(
        functools.partial(initial_kernel, mid),
        grid=(source.shape[0],),
        in_specs=[full, fixed],
        out_specs=[full] + face_specs,
        out_shape=[shape] + face_shapes,
        cost_estimate=pl.CostEstimate(flops=2 * size, transcendentals=0, bytes_accessed=8 * size + 4 * size // source.shape[0]),
        name="chebyshev_start",
    )(source, inverse)
    return outs[0], outs[1:]


def run_sweep(first, second, step_dir, residual, potential, faces, diagonal, inverse, halos):
    full, fixed, face_specs, face_shapes = specs(step_dir.shape)
    steps, nx, ny, nz = step_dir.shape
    x_face, y_face = face_specs[0], face_specs[2]
    shape = jax.ShapeDtypeStruct(step_dir.shape, jnp.float32)
    size = step_dir.size
    outs = pl.pallas_call(
        functools.partial(sweep_kernel, first, second),
        grid=(steps,),
        in_specs=[full, full, full] + [fixed] * 8 + [x_face, x_face, y_face, y_face, face_specs[4], face_specs[4]],
        out_specs=[full, full, full] + face_specs,
        out_shape=[shape, shape, shape] + face_shapes,
        cost_estimate=pl.CostEstimate(flops=30 * size, transcendentals=0, bytes_accessed=4 * 7 * size + 4 * 7 * size // steps),
        name="chebyshev_sweep",
    )(step_dir, residual, potential, *faces, diagonal, inverse, *halos)
    return outs[0], outs[1], outs[2], outs[3:]


def local(
    heart_state,
    cell_type,
    gate_half,
    gate_slope,
    gate_tau,
    conduct,
    reversal,
    block_device,
    block_row,
    tissue,
    tissue_sigma,
):
    voltage = heart_state[0]
    gate_state = heart_state[1:]
    heart_x, heart_y, row_len = voltage.shape
    blocks = heart_x * heart_y
    devices = lax.axis_size("gx") * lax.axis_size("gy") * lax.axis_size("gz")
    capacity = 3 * blocks // devices
    slots = devices * capacity
    torso_x, torso_y, torso_z = tissue.shape
    torso_rows = torso_x * torso_y

    dest_dev = block_device.reshape(blocks)
    dest_row = block_row.reshape(blocks)
    one_hot = (dest_dev[:, None] == jnp.arange(devices, dtype=jnp.int32)[None, :]).astype(jnp.int32)
    running = jnp.cumsum(one_hot, axis=0) - 1
    slot_rank = jnp.sum(running * one_hot, axis=1)
    slot_index = dest_dev * capacity + slot_rank
    slot_match = slot_index[None, :] == jnp.arange(slots, dtype=jnp.int32)[:, None]
    slot_used = jnp.any(slot_match, axis=1)
    slot_block = jnp.argmax(slot_match, axis=1).astype(jnp.int32)
    send_rows = jnp.where(slot_used, dest_row[slot_block], torso_rows)
    recv_rows = lax.all_to_all(
        send_rows.reshape(devices, capacity), ("gx", "gy", "gz"), 0, 0, tiled=True
    ).reshape(slots)
    row_match = recv_rows[None, :] == jnp.arange(torso_rows, dtype=jnp.int32)[:, None]
    row_used = jnp.any(row_match, axis=1)
    row_slot = jnp.argmax(row_match, axis=1).astype(jnp.int32)

    sigma = []
    for dim_index in range(3):
        value = jnp.zeros(tissue.shape, jnp.float32)
        for tissue_kind in range(tissue_sigma.shape[0]):
            value = value + jnp.where(tissue == tissue_kind, tissue_sigma[tissue_kind, dim_index], 0.0)
        sigma.append(value)
    riders = [faces_of(sigma[dim_index], dim_index) for dim_index in range(3)]

    currents = []
    for time_step in range(STEPS):
        gate_state, ion_current = membrane(
            voltage, gate_state, cell_type, gate_half, gate_slope, gate_tau, conduct, reversal
        )
        laplace, carried = heart_laplace(voltage, riders if time_step == 0 else None)
        if time_step == 0:
            sigma_halos = [item[0] for item in carried]
        current = SIGMA_HEART * laplace
        currents.append(current)
        voltage = voltage + DT_HEART * (current - ion_current)
    heart_next = jnp.concatenate([voltage[None], gate_state], axis=0)

    payload = jnp.stack([item.reshape(blocks, row_len) for item in currents], axis=0)
    send_values = jnp.where(slot_used[None, :, None], jnp.take(payload, slot_block, axis=1), 0.0)
    received = lax.all_to_all(
        send_values.reshape(STEPS, devices, capacity, row_len),
        ("gx", "gy", "gz"),
        1,
        1,
        tiled=True,
    ).reshape(STEPS, slots, row_len)
    source = jnp.where(row_used[None, :, None], jnp.take(received, row_slot, axis=1), 0.0)
    source = source.reshape(STEPS, torso_x, torso_y, torso_z)

    faces = []
    for dim_index in range(3):
        low, high = sigma_halos[dim_index]
        minus, plus = shifted(sigma[dim_index], low, high, dim_index)
        faces.append(0.5 * (sigma[dim_index] + plus))
        faces.append(0.5 * (sigma[dim_index] + minus))
    diagonal = SCREEN + faces[0] + faces[1] + faces[2] + faces[3] + faces[4] + faces[5]

    spectrum_mid, first_coef, second_coef = chebyshev_weights(SWEEPS)
    residual = source
    inverse = 1.0 / diagonal
    step_dir, dir_faces = run_initial(spectrum_mid, residual, inverse)
    potential = step_dir
    for sweep in range(1, SWEEPS):
        x_low, x_high = exchange(dir_faces[1], dir_faces[0], "gx")
        y_low, y_high = exchange(dir_faces[3], dir_faces[2], "gy")
        z_low, z_high = exchange(dir_faces[5], dir_faces[4], "gz")
        halos = (x_low, x_high, y_low, y_high, z_low, z_high)
        residual, step_dir, potential, dir_faces = run_sweep(
            first_coef[sweep - 1], second_coef[sweep - 1], step_dir, residual, potential, faces, diagonal, inverse, halos
        )
    return (heart_next, jnp.transpose(potential, (1, 2, 0, 3)))


def solution(mesh):
    in_specs = (
        P(None, "gx", "gy", "gz"),
        P("gx", "gy", "gz"),
        P(),
        P(),
        P(),
        P(),
        P(),
        P("gx", "gy", "gz"),
        P("gx", "gy", "gz"),
        P("gx", "gy", "gz"),
        P(),
    )
    out_specs = (P(None, "gx", "gy", "gz"), P("gx", "gy", None, "gz"))
    return jax.shard_map(local, mesh=mesh, in_specs=in_specs, out_specs=out_specs, check_vma=False)
```

```python
import jax
import jax.numpy as jnp
from jax import lax
from jax.sharding import PartitionSpec as P
from jax.experimental import pallas as pl
from jax.experimental.pallas import tpu as pltpu
import functools

STEPS = 4
SWEEPS = 4


DT_HEART = 0.05
SIGMA_HEART = 1.0
SCREEN = 0.05
LOW_EDGE = 0.1
HIGH_EDGE = 1.9


def chebyshev_weights(sweep_count):
    spectrum_mid = 0.5 * (HIGH_EDGE + LOW_EDGE)
    half_width = 0.5 * (HIGH_EDGE - LOW_EDGE)
    half_ratio = spectrum_mid / half_width
    rho_old = 1.0 / half_ratio
    first_coef = []
    second_coef = []
    for sweep in range(1, sweep_count):
        rho_new = 1.0 / (2.0 * half_ratio - rho_old)
        first_coef.append(rho_new * rho_old)
        second_coef.append(2.0 * rho_new / half_width)
        rho_old = rho_new
    return (spectrum_mid, first_coef, second_coef)


def face_halos(block, axis, dim):
    top = lax.index_in_dim(block, block.shape[dim] - 1, axis=dim, keepdims=False)
    bottom = lax.index_in_dim(block, 0, axis=dim, keepdims=False)
    return exchange(top, bottom, axis)


def shifted(block, low, high, dim):
    n = block.shape[dim]
    low = jnp.expand_dims(low, dim)
    high = jnp.expand_dims(high, dim)
    minus = jnp.concatenate([low, lax.slice_in_dim(block, 0, n - 1, axis=dim)], axis=dim)
    plus = jnp.concatenate([lax.slice_in_dim(block, 1, n, axis=dim), high], axis=dim)
    return minus, plus


def membrane(voltage, gate_state, cell_type, gate_half, gate_slope, gate_tau, conduct, reversal):
    gate_count = gate_half.shape[0]
    lead_shape = (-1,) + (1,) * voltage.ndim
    gate_sign = jnp.where(jnp.arange(gate_count) % 2 == 0, 1.0, -1.0).astype(jnp.float32)
    exponent = (gate_sign / gate_slope).reshape(lead_shape) * (
        voltage[None] - gate_half.reshape(lead_shape)
    )
    steady = jax.nn.sigmoid(exponent)
    time_const = gate_tau.reshape(lead_shape) * (0.5 + steady)
    gate_state = steady + (gate_state - steady) * jnp.exp(-DT_HEART / time_const)
    weight = jnp.zeros(gate_state[0::2].shape, jnp.float32)
    for cell_kind in range(conduct.shape[0]):
        weight = weight + jnp.where(
            cell_type[None] == cell_kind, conduct[cell_kind].reshape(lead_shape), 0.0
        )
    ion_current = jnp.sum(
        weight
        * gate_state[0::2]
        * gate_state[1::2]
        * (voltage[None] - reversal.reshape(lead_shape)),
        axis=0,
    )
    return (gate_state, ion_current)


def faces_of(block, dim):
    top = lax.index_in_dim(block, block.shape[dim] - 1, axis=dim, keepdims=False)
    bottom = lax.index_in_dim(block, 0, axis=dim, keepdims=False)
    return top, bottom


def heart_laplace(voltage, riders=None):
    parts = []
    carried = []
    for index, (axis, dim) in enumerate((("gx", 0), ("gy", 1), ("gz", 2))):
        pairs = [faces_of(voltage, dim)]
        if riders is not None:
            pairs.append(riders[index])
        got = exchange_group(pairs, axis)
        minus, plus = shifted(voltage, got[0][0], got[0][1], dim)
        parts.append((plus, minus))
        carried.append(got[1:])
    total = parts[0][0] + parts[0][1]
    total = total + parts[1][0] + parts[1][1]
    total = total + parts[2][0] + parts[2][1]
    return total - 6.0 * voltage, carried


def exchange(top, bottom, axis):
    count = lax.axis_size(axis)
    if count == 2:
        index = lax.axis_index(axis)
        got = lax.ppermute(jnp.where(index == 0, top, bottom), axis, [(0, 1), (1, 0)])
        zero = jnp.zeros_like(got)
        return jnp.where(index == 1, got, zero), jnp.where(index == 0, got, zero)
    forward = [(i, i + 1) for i in range(count - 1)]
    backward = [(i + 1, i) for i in range(count - 1)]
    return lax.ppermute(top, axis, forward), lax.ppermute(bottom, axis, backward)


def exchange_group(pairs, axis):
    if len(pairs) == 1:
        return [exchange(pairs[0][0], pairs[0][1], axis)]
    top = jnp.concatenate([item.reshape(-1) for item, _ in pairs])
    bottom = jnp.concatenate([item.reshape(-1) for _, item in pairs])
    low, high = exchange(top, bottom, axis)
    result = []
    offset = 0
    for item, _ in pairs:
        size = item.size
        result.append((low[offset:offset + size].reshape(item.shape), high[offset:offset + size].reshape(item.shape)))
        offset += size
    return result


def write_faces(x, value, columns, xf_lo, xf_hi, yf_lo, yf_hi, zf_lo, zf_hi):
    nx = yf_lo.shape[1]
    ny, nz = value.shape
    half = nz // 2
    lane = lax.broadcasted_iota(jnp.int32, (ny, nz), 1)

    @pl.when(x == 0)
    def _():
        xf_lo[0] = value

    @pl.when(x == nx - 1)
    def _():
        xf_hi[0] = value

    yf_lo[0, x] = value[0:1, :]
    yf_hi[0, x] = value[ny - 1:ny, :]
    columns = jnp.where(lane == x, jnp.broadcast_to(value[:, 0:1], (ny, nz)), columns)
    columns = jnp.where(lane == half + x, jnp.broadcast_to(value[:, nz - 1:nz], (ny, nz)), columns)
    return columns


def finish_faces(columns, xf_lo, xf_hi, yf_lo, yf_hi, zf_lo, zf_hi):
    nx = yf_lo.shape[1]
    half = columns.shape[1] // 2
    flipped = columns.T
    zf_lo[0] = flipped[0:nx, :]
    zf_hi[0] = flipped[half:half + nx, :]


def sweep_kernel(first, second, d_ref, r_ref, p_ref, fxp, fxm, fyp, fym, fzp, fzm, dg_ref, inv_ref,
                 xlo, xhi, ylo, yhi, zlo, zhi, r_out, d_out, p_out, *face_out):
    nx, ny, nz = d_ref.shape[1], d_ref.shape[2], d_ref.shape[3]
    row = lax.broadcasted_iota(jnp.int32, (ny, nz), 0)
    lane = lax.broadcasted_iota(jnp.int32, (ny, nz), 1)
    blank = jnp.zeros((nz - nx, ny), jnp.float32)
    low_cols = jnp.concatenate([zlo[0], blank], axis=0).T
    high_rows = zhi[0]
    high_cols = jnp.concatenate([high_rows[1:nx], blank, high_rows[0:1]], axis=0).T

    def body(x, carry):
        centre = d_ref[0, x]
        below = d_ref[0, jnp.maximum(x - 1, 0)]
        above = d_ref[0, jnp.minimum(x + 1, nx - 1)]
        x_minus = jnp.where(x == 0, xlo[0], below)
        x_plus = jnp.where(x == nx - 1, xhi[0], above)
        y_minus = jnp.where(row == 0, ylo[0, x], pltpu.roll(centre, 1, 0))
        y_plus = jnp.where(row == ny - 1, yhi[0, x], pltpu.roll(centre, ny - 1, 0))
        turn = lax.rem(nz - x, nz)
        z_minus = jnp.where(lane == 0, pltpu.roll(low_cols, turn, 1), pltpu.roll(centre, 1, 1))
        z_plus = jnp.where(lane == nz - 1, pltpu.roll(high_cols, turn, 1), pltpu.roll(centre, nz - 1, 1))
        beside = fxp[x] * x_plus + fxm[x] * x_minus
        beside = beside + fyp[x] * y_plus + fym[x] * y_minus
        beside = beside + fzp[x] * z_plus + fzm[x] * z_minus
        diag = dg_ref[x]
        residual = r_ref[0, x] - (diag * centre - beside)
        step_dir = first * centre + second * (residual * inv_ref[x])
        r_out[0, x] = residual
        d_out[0, x] = step_dir
        p_out[0, x] = p_ref[0, x] + step_dir
        return write_faces(x, step_dir, carry, *face_out)

    columns = lax.fori_loop(0, nx, body, jnp.zeros((ny, nz), jnp.float32), unroll=2)
    finish_faces(columns, *face_out)


def initial_kernel(mid, rows_ref, recv_ref, inv_ref, r_out, d_out, *face_out):
    nx, ny, nz = r_out.shape[1], r_out.shape[2], r_out.shape[3]
    slots = rows_ref.shape[0]
    r_out[...] = jnp.zeros(r_out.shape, jnp.float32)

    def place(k, carry):
        row = rows_ref[k]

        @pl.when(row < nx * ny)
        def _():
            r_out[0, row // ny, pl.ds(row % ny, 1), :] = recv_ref[0, pl.ds(k, 1), :]

        return carry

    lax.fori_loop(0, slots, place, 0)

    def body(x, carry):
        step_dir = r_out[0, x] * inv_ref[x] * (1.0 / mid)
        d_out[0, x] = step_dir
        return write_faces(x, step_dir, carry, *face_out)

    columns = lax.fori_loop(0, nx, body, jnp.zeros((ny, nz), jnp.float32), unroll=2)
    finish_faces(columns, *face_out)


def specs(shape):
    steps, nx, ny, nz = shape
    full = pl.BlockSpec((1, nx, ny, nz), lambda s: (s, 0, 0, 0))
    fixed = pl.BlockSpec((nx, ny, nz), lambda s: (0, 0, 0))
    x_face = pl.BlockSpec((1, ny, nz), lambda s: (s, 0, 0))
    y_face = pl.BlockSpec((1, nx, 1, nz), lambda s: (s, 0, 0, 0))
    z_face = pl.BlockSpec((1, nx, ny), lambda s: (s, 0, 0))
    face_specs = [x_face, x_face, y_face, y_face, z_face, z_face]
    face_shapes = [
        jax.ShapeDtypeStruct((steps, ny, nz), jnp.float32),
        jax.ShapeDtypeStruct((steps, ny, nz), jnp.float32),
        jax.ShapeDtypeStruct((steps, nx, 1, nz), jnp.float32),
        jax.ShapeDtypeStruct((steps, nx, 1, nz), jnp.float32),
        jax.ShapeDtypeStruct((steps, nx, ny), jnp.float32),
        jax.ShapeDtypeStruct((steps, nx, ny), jnp.float32),
    ]
    return full, fixed, face_specs, face_shapes


def run_initial(mid, recv_rows, received, inverse):
    steps, slots, nz = received.shape
    nx, ny = inverse.shape[0], inverse.shape[1]
    shape4 = (steps, nx, ny, nz)
    full, fixed, face_specs, face_shapes = specs(shape4)
    shape = jax.ShapeDtypeStruct(shape4, jnp.float32)
    size = steps * nx * ny * nz
    rows_spec = pl.BlockSpec(memory_space=pltpu.SMEM)
    recv_spec = pl.BlockSpec((1, slots, nz), lambda s: (s, 0, 0))
    outs = pl.pallas_call(
        functools.partial(initial_kernel, mid),
        grid=(steps,),
        in_specs=[rows_spec, recv_spec, fixed],
        out_specs=[full, full] + face_specs,
        out_shape=[shape, shape] + face_shapes,
        cost_estimate=pl.CostEstimate(flops=2 * size, transcendentals=0, bytes_accessed=8 * size + 4 * size // steps + 4 * received.size),
        name="chebyshev_start",
    )(recv_rows, received, inverse)
    return outs[0], outs[1], outs[2:]


def run_sweep(first, second, step_dir, residual, potential, faces, diagonal, inverse, halos):
    full, fixed, face_specs, face_shapes = specs(step_dir.shape)
    steps, nx, ny, nz = step_dir.shape
    x_face, y_face = face_specs[0], face_specs[2]
    shape = jax.ShapeDtypeStruct(step_dir.shape, jnp.float32)
    size = step_dir.size
    outs = pl.pallas_call(
        functools.partial(sweep_kernel, first, second),
        grid=(steps,),
        in_specs=[full, full, full] + [fixed] * 8 + [x_face, x_face, y_face, y_face, face_specs[4], face_specs[4]],
        out_specs=[full, full, full] + face_specs,
        out_shape=[shape, shape, shape] + face_shapes,
        cost_estimate=pl.CostEstimate(flops=30 * size, transcendentals=0, bytes_accessed=4 * 7 * size + 4 * 7 * size // steps),
        name="chebyshev_sweep",
    )(step_dir, residual, potential, *faces, diagonal, inverse, *halos)
    return outs[0], outs[1], outs[2], outs[3:]


def local(
    heart_state,
    cell_type,
    gate_half,
    gate_slope,
    gate_tau,
    conduct,
    reversal,
    block_device,
    block_row,
    tissue,
    tissue_sigma,
):
    voltage = heart_state[0]
    gate_state = heart_state[1:]
    heart_x, heart_y, row_len = voltage.shape
    blocks = heart_x * heart_y
    devices = lax.axis_size("gx") * lax.axis_size("gy") * lax.axis_size("gz")
    capacity = 3 * blocks // devices
    slots = devices * capacity
    torso_x, torso_y, torso_z = tissue.shape
    torso_rows = torso_x * torso_y

    dest_dev = block_device.reshape(blocks)
    dest_row = block_row.reshape(blocks)
    one_hot = (dest_dev[:, None] == jnp.arange(devices, dtype=jnp.int32)[None, :]).astype(jnp.int32)
    running = jnp.cumsum(one_hot, axis=0) - 1
    slot_rank = jnp.sum(running * one_hot, axis=1)
    slot_index = dest_dev * capacity + slot_rank
    slot_match = slot_index[None, :] == jnp.arange(slots, dtype=jnp.int32)[:, None]
    slot_used = jnp.any(slot_match, axis=1)
    slot_block = jnp.argmax(slot_match, axis=1).astype(jnp.int32)
    send_rows = jnp.where(slot_used, dest_row[slot_block], torso_rows)
    recv_rows = lax.all_to_all(
        send_rows.reshape(devices, capacity), ("gx", "gy", "gz"), 0, 0, tiled=True
    ).reshape(slots)

    sigma = []
    for dim_index in range(3):
        value = jnp.zeros(tissue.shape, jnp.float32)
        for tissue_kind in range(tissue_sigma.shape[0]):
            value = value + jnp.where(tissue == tissue_kind, tissue_sigma[tissue_kind, dim_index], 0.0)
        sigma.append(value)
    riders = [faces_of(sigma[dim_index], dim_index) for dim_index in range(3)]

    currents = []
    for time_step in range(STEPS):
        gate_state, ion_current = membrane(
            voltage, gate_state, cell_type, gate_half, gate_slope, gate_tau, conduct, reversal
        )
        laplace, carried = heart_laplace(voltage, riders if time_step == 0 else None)
        if time_step == 0:
            sigma_halos = [item[0] for item in carried]
        current = SIGMA_HEART * laplace
        currents.append(current)
        voltage = voltage + DT_HEART * (current - ion_current)
    heart_next = jnp.concatenate([voltage[None], gate_state], axis=0)

    payload = jnp.stack([item.reshape(blocks, row_len) for item in currents], axis=0)
    send_values = jnp.where(slot_used[None, :, None], jnp.take(payload, slot_block, axis=1), 0.0)
    received = lax.all_to_all(
        send_values.reshape(STEPS, devices, capacity, row_len),
        ("gx", "gy", "gz"),
        1,
        1,
        tiled=True,
    ).reshape(STEPS, slots, row_len)

    faces = []
    for dim_index in range(3):
        low, high = sigma_halos[dim_index]
        minus, plus = shifted(sigma[dim_index], low, high, dim_index)
        faces.append(0.5 * (sigma[dim_index] + plus))
        faces.append(0.5 * (sigma[dim_index] + minus))
    diagonal = SCREEN + faces[0] + faces[1] + faces[2] + faces[3] + faces[4] + faces[5]

    spectrum_mid, first_coef, second_coef = chebyshev_weights(SWEEPS)
    inverse = 1.0 / diagonal
    residual, step_dir, dir_faces = run_initial(spectrum_mid, recv_rows, received, inverse)
    potential = step_dir
    for sweep in range(1, SWEEPS):
        x_low, x_high = exchange(dir_faces[1], dir_faces[0], "gx")
        y_low, y_high = exchange(dir_faces[3], dir_faces[2], "gy")
        z_low, z_high = exchange(dir_faces[5], dir_faces[4], "gz")
        halos = (x_low, x_high, y_low, y_high, z_low, z_high)
        residual, step_dir, potential, dir_faces = run_sweep(
            first_coef[sweep - 1], second_coef[sweep - 1], step_dir, residual, potential, faces, diagonal, inverse, halos
        )
    return (heart_next, jnp.transpose(potential, (1, 2, 0, 3)))


def solution(mesh):
    in_specs = (
        P(None, "gx", "gy", "gz"),
        P("gx", "gy", "gz"),
        P(),
        P(),
        P(),
        P(),
        P(),
        P("gx", "gy", "gz"),
        P("gx", "gy", "gz"),
        P("gx", "gy", "gz"),
        P(),
    )
    out_specs = (P(None, "gx", "gy", "gz"), P("gx", "gy", None, "gz"))
    return jax.shard_map(local, mesh=mesh, in_specs=in_specs, out_specs=out_specs, check_vma=False)
```

```python
import jax
import jax.numpy as jnp
from jax import lax
from jax.sharding import PartitionSpec as P
from jax.experimental import pallas as pl
from jax.experimental.pallas import tpu as pltpu
import functools

STEPS = 4
SWEEPS = 4


DT_HEART = 0.05
SIGMA_HEART = 1.0
SCREEN = 0.05
LOW_EDGE = 0.1
HIGH_EDGE = 1.9


def chebyshev_weights(sweep_count):
    spectrum_mid = 0.5 * (HIGH_EDGE + LOW_EDGE)
    half_width = 0.5 * (HIGH_EDGE - LOW_EDGE)
    half_ratio = spectrum_mid / half_width
    rho_old = 1.0 / half_ratio
    first_coef = []
    second_coef = []
    for sweep in range(1, sweep_count):
        rho_new = 1.0 / (2.0 * half_ratio - rho_old)
        first_coef.append(rho_new * rho_old)
        second_coef.append(2.0 * rho_new / half_width)
        rho_old = rho_new
    return (spectrum_mid, first_coef, second_coef)


def face_halos(block, axis, dim):
    top = lax.index_in_dim(block, block.shape[dim] - 1, axis=dim, keepdims=False)
    bottom = lax.index_in_dim(block, 0, axis=dim, keepdims=False)
    return exchange(top, bottom, axis)


def shifted(block, low, high, dim):
    n = block.shape[dim]
    low = jnp.expand_dims(low, dim)
    high = jnp.expand_dims(high, dim)
    minus = jnp.concatenate([low, lax.slice_in_dim(block, 0, n - 1, axis=dim)], axis=dim)
    plus = jnp.concatenate([lax.slice_in_dim(block, 1, n, axis=dim), high], axis=dim)
    return minus, plus


def membrane(voltage, gate_state, cell_type, gate_half, gate_slope, gate_tau, conduct, reversal):
    gate_count = gate_half.shape[0]
    lead_shape = (-1,) + (1,) * voltage.ndim
    gate_sign = jnp.where(jnp.arange(gate_count) % 2 == 0, 1.0, -1.0).astype(jnp.float32)
    exponent = (gate_sign / gate_slope).reshape(lead_shape) * (
        voltage[None] - gate_half.reshape(lead_shape)
    )
    steady = jax.nn.sigmoid(exponent)
    time_const = gate_tau.reshape(lead_shape) * (0.5 + steady)
    gate_state = steady + (gate_state - steady) * jnp.exp(-DT_HEART / time_const)
    weight = jnp.zeros(gate_state[0::2].shape, jnp.float32)
    for cell_kind in range(conduct.shape[0]):
        weight = weight + jnp.where(
            cell_type[None] == cell_kind, conduct[cell_kind].reshape(lead_shape), 0.0
        )
    ion_current = jnp.sum(
        weight
        * gate_state[0::2]
        * gate_state[1::2]
        * (voltage[None] - reversal.reshape(lead_shape)),
        axis=0,
    )
    return (gate_state, ion_current)


def faces_of(block, dim):
    top = lax.index_in_dim(block, block.shape[dim] - 1, axis=dim, keepdims=False)
    bottom = lax.index_in_dim(block, 0, axis=dim, keepdims=False)
    return top, bottom


def heart_laplace(voltage, riders=None):
    parts = []
    carried = []
    for index, (axis, dim) in enumerate((("gx", 0), ("gy", 1), ("gz", 2))):
        pairs = [faces_of(voltage, dim)]
        if riders is not None:
            pairs.append(riders[index])
        got = exchange_group(pairs, axis)
        minus, plus = shifted(voltage, got[0][0], got[0][1], dim)
        parts.append((plus, minus))
        carried.append(got[1:])
    total = parts[0][0] + parts[0][1]
    total = total + parts[1][0] + parts[1][1]
    total = total + parts[2][0] + parts[2][1]
    return total - 6.0 * voltage, carried


def exchange(top, bottom, axis):
    count = lax.axis_size(axis)
    if count == 2:
        index = lax.axis_index(axis)
        got = lax.ppermute(jnp.where(index == 0, top, bottom), axis, [(0, 1), (1, 0)])
        zero = jnp.zeros_like(got)
        return jnp.where(index == 1, got, zero), jnp.where(index == 0, got, zero)
    forward = [(i, i + 1) for i in range(count - 1)]
    backward = [(i + 1, i) for i in range(count - 1)]
    return lax.ppermute(top, axis, forward), lax.ppermute(bottom, axis, backward)


def exchange_group(pairs, axis):
    if len(pairs) == 1:
        return [exchange(pairs[0][0], pairs[0][1], axis)]
    top = jnp.concatenate([item.reshape(-1) for item, _ in pairs])
    bottom = jnp.concatenate([item.reshape(-1) for _, item in pairs])
    low, high = exchange(top, bottom, axis)
    result = []
    offset = 0
    for item, _ in pairs:
        size = item.size
        result.append((low[offset:offset + size].reshape(item.shape), high[offset:offset + size].reshape(item.shape)))
        offset += size
    return result


def group_faces(x, g, step, columns, lane, xf_lo, xf_hi, yf_lo, yf_hi):
    nx = yf_lo.shape[1]
    groups = xf_lo.shape[1] // 8
    nz = step.shape[1]
    half = nz // 2
    rows = pl.ds(8 * g, 8)

    if g == 0:
        yf_lo[0, x] = step[0:1, :]
    if g == groups - 1:
        yf_hi[0, x] = step[7:8, :]
    columns = jnp.where(lane == x, jnp.broadcast_to(step[:, 0:1], step.shape), columns)
    return jnp.where(lane == half + x, jnp.broadcast_to(step[:, nz - 1:nz], step.shape), columns)


def finish_faces(d_out, xf_lo, xf_hi, col_scr, zf_lo, zf_hi):
    nx = zf_lo.shape[1]
    xf_lo[0] = d_out[0, 0]
    xf_hi[0] = d_out[0, nx - 1]
    half = col_scr.shape[1] // 2
    flipped = col_scr[...].T
    zf_lo[0] = flipped[0:nx, :]
    zf_hi[0] = flipped[half:half + nx, :]


def sweep_kernel(first, second, d_ref, r_ref, p_ref, fxp, fxm, fyp, fym, fzp, fzm, dg_ref, inv_ref,
                 xlo, xhi, ylo, yhi, zlo, zhi, r_out, d_out, p_out, xf_lo, xf_hi, yf_lo, yf_hi,
                 zf_lo, zf_hi, low_scr, high_scr, col_scr):
    nx, ny, nz = d_ref.shape[1], d_ref.shape[2], d_ref.shape[3]
    groups = ny // 8
    sub = lax.broadcasted_iota(jnp.int32, (8, nz), 0)
    lane = lax.broadcasted_iota(jnp.int32, (8, nz), 1)
    blank = jnp.zeros((nz - nx, ny), jnp.float32)
    low_scr[...] = jnp.concatenate([zlo[0], blank], axis=0).T
    high_rows = zhi[0]
    high_scr[...] = jnp.concatenate([high_rows[1:nx], blank, high_rows[0:1]], axis=0).T
    col_scr[...] = jnp.zeros(col_scr.shape, jnp.float32)

    def body(x, carry):
        turn = lax.rem(nz - x, nz)
        below = jnp.maximum(x - 1, 0)
        above = jnp.minimum(x + 1, nx - 1)
        cs = [d_ref[0, x, pl.ds(8 * g, 8), :] for g in range(groups)]
        r1 = [pltpu.roll(c, 1, 0) for c in cs]
        r7 = [pltpu.roll(c, 7, 0) for c in cs]
        for g in range(groups):
            rows = pl.ds(8 * g, 8)
            centre = cs[g]
            x_minus = jnp.where(x == 0, xlo[0, rows], d_ref[0, below, rows])
            x_plus = jnp.where(x == nx - 1, xhi[0, rows], d_ref[0, above, rows])
            up = ylo[0, x] if g == 0 else r1[g - 1]
            down = yhi[0, x] if g == groups - 1 else r7[g + 1]
            y_minus = jnp.where(sub == 0, up, r1[g])
            y_plus = jnp.where(sub == 7, down, r7[g])
            z_minus = jnp.where(lane == 0, pltpu.roll(low_scr[rows], turn, 1), pltpu.roll(centre, 1, 1))
            z_plus = jnp.where(lane == nz - 1, pltpu.roll(high_scr[rows], turn, 1), pltpu.roll(centre, nz - 1, 1))
            beside = fxp[x, rows] * x_plus + fxm[x, rows] * x_minus
            beside = beside + fyp[x, rows] * y_plus + fym[x, rows] * y_minus
            beside = beside + fzp[x, rows] * z_plus + fzm[x, rows] * z_minus
            residual = r_ref[0, x, rows] - (dg_ref[x, rows] * centre - beside)
            step_dir = first * centre + second * (residual * inv_ref[x, rows])
            r_out[0, x, rows] = residual
            d_out[0, x, rows] = step_dir
            p_out[0, x, rows] = p_ref[0, x, rows] + step_dir
            col_scr[rows] = group_faces(x, g, step_dir, col_scr[rows], lane, xf_lo, xf_hi, yf_lo, yf_hi)
        return carry

    lax.fori_loop(0, nx, body, 0)
    finish_faces(d_out, xf_lo, xf_hi, col_scr, zf_lo, zf_hi)


def initial_kernel(mid, r_ref, inv_ref, d_out, xf_lo, xf_hi, yf_lo, yf_hi, zf_lo, zf_hi, col_scr):
    nx, ny, nz = r_ref.shape[1], r_ref.shape[2], r_ref.shape[3]
    groups = ny // 8
    lane = lax.broadcasted_iota(jnp.int32, (8, nz), 1)
    col_scr[...] = jnp.zeros(col_scr.shape, jnp.float32)

    def body(x, carry):
        for g in range(groups):
            rows = pl.ds(8 * g, 8)
            step_dir = r_ref[0, x, rows] * inv_ref[x, rows] * (1.0 / mid)
            d_out[0, x, rows] = step_dir
            col_scr[rows] = group_faces(x, g, step_dir, col_scr[rows], lane, xf_lo, xf_hi, yf_lo, yf_hi)
        return carry

    lax.fori_loop(0, nx, body, 0)
    finish_faces(d_out, xf_lo, xf_hi, col_scr, zf_lo, zf_hi)


def specs(shape):
    steps, nx, ny, nz = shape
    full = pl.BlockSpec((1, nx, ny, nz), lambda s: (s, 0, 0, 0))
    fixed = pl.BlockSpec((nx, ny, nz), lambda s: (0, 0, 0))
    x_face = pl.BlockSpec((1, ny, nz), lambda s: (s, 0, 0))
    y_face = pl.BlockSpec((1, nx, 1, nz), lambda s: (s, 0, 0, 0))
    z_face = pl.BlockSpec((1, nx, ny), lambda s: (s, 0, 0))
    face_specs = [x_face, x_face, y_face, y_face, z_face, z_face]
    face_shapes = [
        jax.ShapeDtypeStruct((steps, ny, nz), jnp.float32),
        jax.ShapeDtypeStruct((steps, ny, nz), jnp.float32),
        jax.ShapeDtypeStruct((steps, nx, 1, nz), jnp.float32),
        jax.ShapeDtypeStruct((steps, nx, 1, nz), jnp.float32),
        jax.ShapeDtypeStruct((steps, nx, ny), jnp.float32),
        jax.ShapeDtypeStruct((steps, nx, ny), jnp.float32),
    ]
    return full, fixed, face_specs, face_shapes


def run_initial(mid, source, inverse):
    full, fixed, face_specs, face_shapes = specs(source.shape)
    shape = jax.ShapeDtypeStruct(source.shape, jnp.float32)
    size = source.size
    outs = pl.pallas_call(
        functools.partial(initial_kernel, mid),
        grid=(source.shape[0],),
        in_specs=[full, fixed],
        out_specs=[full] + face_specs,
        out_shape=[shape] + face_shapes,
        cost_estimate=pl.CostEstimate(flops=2 * size, transcendentals=0, bytes_accessed=8 * size + 4 * size // source.shape[0]),
        scratch_shapes=[pltpu.VMEM((source.shape[2], source.shape[3]), jnp.float32)],
        name="chebyshev_start",
    )(source, inverse)
    return outs[0], outs[1:]


def run_sweep(first, second, step_dir, residual, potential, faces, diagonal, inverse, halos):
    full, fixed, face_specs, face_shapes = specs(step_dir.shape)
    steps, nx, ny, nz = step_dir.shape
    x_face, y_face = face_specs[0], face_specs[2]
    shape = jax.ShapeDtypeStruct(step_dir.shape, jnp.float32)
    size = step_dir.size
    outs = pl.pallas_call(
        functools.partial(sweep_kernel, first, second),
        grid=(steps,),
        in_specs=[full, full, full] + [fixed] * 8 + [x_face, x_face, y_face, y_face, face_specs[4], face_specs[4]],
        out_specs=[full, full, full] + face_specs,
        out_shape=[shape, shape, shape] + face_shapes,
        cost_estimate=pl.CostEstimate(flops=30 * size, transcendentals=0, bytes_accessed=4 * 7 * size + 4 * 7 * size // steps),
        scratch_shapes=[pltpu.VMEM((ny, nz), jnp.float32)] * 3,
        name="chebyshev_sweep",
    )(step_dir, residual, potential, *faces, diagonal, inverse, *halos)
    return outs[0], outs[1], outs[2], outs[3:]


def local(
    heart_state,
    cell_type,
    gate_half,
    gate_slope,
    gate_tau,
    conduct,
    reversal,
    block_device,
    block_row,
    tissue,
    tissue_sigma,
):
    voltage = heart_state[0]
    gate_state = heart_state[1:]
    heart_x, heart_y, row_len = voltage.shape
    blocks = heart_x * heart_y
    devices = lax.axis_size("gx") * lax.axis_size("gy") * lax.axis_size("gz")
    capacity = 3 * blocks // devices
    slots = devices * capacity
    torso_x, torso_y, torso_z = tissue.shape
    torso_rows = torso_x * torso_y

    dest_dev = block_device.reshape(blocks)
    dest_row = block_row.reshape(blocks)
    one_hot = (dest_dev[:, None] == jnp.arange(devices, dtype=jnp.int32)[None, :]).astype(jnp.int32)
    running = jnp.cumsum(one_hot, axis=0) - 1
    slot_rank = jnp.sum(running * one_hot, axis=1)
    slot_index = dest_dev * capacity + slot_rank
    slot_match = slot_index[None, :] == jnp.arange(slots, dtype=jnp.int32)[:, None]
    slot_used = jnp.any(slot_match, axis=1)
    slot_block = jnp.argmax(slot_match, axis=1).astype(jnp.int32)
    send_rows = jnp.where(slot_used, dest_row[slot_block], torso_rows)
    recv_rows = lax.all_to_all(
        send_rows.reshape(devices, capacity), ("gx", "gy", "gz"), 0, 0, tiled=True
    ).reshape(slots)
    row_match = recv_rows[None, :] == jnp.arange(torso_rows, dtype=jnp.int32)[:, None]
    row_used = jnp.any(row_match, axis=1)
    row_slot = jnp.argmax(row_match, axis=1).astype(jnp.int32)

    sigma = []
    for dim_index in range(3):
        value = jnp.zeros(tissue.shape, jnp.float32)
        for tissue_kind in range(tissue_sigma.shape[0]):
            value = value + jnp.where(tissue == tissue_kind, tissue_sigma[tissue_kind, dim_index], 0.0)
        sigma.append(value)
    riders = [faces_of(sigma[dim_index], dim_index) for dim_index in range(3)]

    currents = []
    for time_step in range(STEPS):
        gate_state, ion_current = membrane(
            voltage, gate_state, cell_type, gate_half, gate_slope, gate_tau, conduct, reversal
        )
        laplace, carried = heart_laplace(voltage, riders if time_step == 0 else None)
        if time_step == 0:
            sigma_halos = [item[0] for item in carried]
        current = SIGMA_HEART * laplace
        currents.append(current)
        voltage = voltage + DT_HEART * (current - ion_current)
    heart_next = jnp.concatenate([voltage[None], gate_state], axis=0)

    payload = jnp.stack([item.reshape(blocks, row_len) for item in currents], axis=0)
    send_values = jnp.where(slot_used[None, :, None], jnp.take(payload, slot_block, axis=1), 0.0)
    received = lax.all_to_all(
        send_values.reshape(STEPS, devices, capacity, row_len),
        ("gx", "gy", "gz"),
        1,
        1,
        tiled=True,
    ).reshape(STEPS, slots, row_len)
    source = jnp.where(row_used[None, :, None], jnp.take(received, row_slot, axis=1), 0.0)
    source = source.reshape(STEPS, torso_x, torso_y, torso_z)

    faces = []
    for dim_index in range(3):
        low, high = sigma_halos[dim_index]
        minus, plus = shifted(sigma[dim_index], low, high, dim_index)
        faces.append(0.5 * (sigma[dim_index] + plus))
        faces.append(0.5 * (sigma[dim_index] + minus))
    diagonal = SCREEN + faces[0] + faces[1] + faces[2] + faces[3] + faces[4] + faces[5]

    spectrum_mid, first_coef, second_coef = chebyshev_weights(SWEEPS)
    residual = source
    inverse = 1.0 / diagonal
    step_dir, dir_faces = run_initial(spectrum_mid, residual, inverse)
    potential = step_dir
    for sweep in range(1, SWEEPS):
        x_low, x_high = exchange(dir_faces[1], dir_faces[0], "gx")
        y_low, y_high = exchange(dir_faces[3], dir_faces[2], "gy")
        z_low, z_high = exchange(dir_faces[5], dir_faces[4], "gz")
        halos = (x_low, x_high, y_low, y_high, z_low, z_high)
        residual, step_dir, potential, dir_faces = run_sweep(
            first_coef[sweep - 1], second_coef[sweep - 1], step_dir, residual, potential, faces, diagonal, inverse, halos
        )
    return (heart_next, jnp.transpose(potential, (1, 2, 0, 3)))


def solution(mesh):
    in_specs = (
        P(None, "gx", "gy", "gz"),
        P("gx", "gy", "gz"),
        P(),
        P(),
        P(),
        P(),
        P(),
        P("gx", "gy", "gz"),
        P("gx", "gy", "gz"),
        P("gx", "gy", "gz"),
        P(),
    )
    out_specs = (P(None, "gx", "gy", "gz"), P("gx", "gy", None, "gz"))
    return jax.shard_map(local, mesh=mesh, in_specs=in_specs, out_specs=out_specs, check_vma=False)
```

```python
import jax
import jax.numpy as jnp
from jax import lax
from jax.sharding import PartitionSpec as P
from jax.experimental import pallas as pl
from jax.experimental.pallas import tpu as pltpu
import functools

STEPS = 4
SWEEPS = 4


DT_HEART = 0.05
SIGMA_HEART = 1.0
SCREEN = 0.05
LOW_EDGE = 0.1
HIGH_EDGE = 1.9


def chebyshev_weights(sweep_count):
    spectrum_mid = 0.5 * (HIGH_EDGE + LOW_EDGE)
    half_width = 0.5 * (HIGH_EDGE - LOW_EDGE)
    half_ratio = spectrum_mid / half_width
    rho_old = 1.0 / half_ratio
    first_coef = []
    second_coef = []
    for sweep in range(1, sweep_count):
        rho_new = 1.0 / (2.0 * half_ratio - rho_old)
        first_coef.append(rho_new * rho_old)
        second_coef.append(2.0 * rho_new / half_width)
        rho_old = rho_new
    return (spectrum_mid, first_coef, second_coef)


def face_halos(block, axis, dim):
    top = lax.index_in_dim(block, block.shape[dim] - 1, axis=dim, keepdims=False)
    bottom = lax.index_in_dim(block, 0, axis=dim, keepdims=False)
    return exchange(top, bottom, axis)


def shifted(block, low, high, dim):
    n = block.shape[dim]
    low = jnp.expand_dims(low, dim)
    high = jnp.expand_dims(high, dim)
    minus = jnp.concatenate([low, lax.slice_in_dim(block, 0, n - 1, axis=dim)], axis=dim)
    plus = jnp.concatenate([lax.slice_in_dim(block, 1, n, axis=dim), high], axis=dim)
    return minus, plus


def membrane(voltage, gate_state, cell_type, gate_half, gate_slope, gate_tau, conduct, reversal):
    gate_count = gate_half.shape[0]
    lead_shape = (-1,) + (1,) * voltage.ndim
    gate_sign = jnp.where(jnp.arange(gate_count) % 2 == 0, 1.0, -1.0).astype(jnp.float32)
    exponent = (gate_sign / gate_slope).reshape(lead_shape) * (
        voltage[None] - gate_half.reshape(lead_shape)
    )
    steady = jax.nn.sigmoid(exponent)
    time_const = gate_tau.reshape(lead_shape) * (0.5 + steady)
    gate_state = steady + (gate_state - steady) * jnp.exp(-DT_HEART / time_const)
    weight = jnp.zeros(gate_state[0::2].shape, jnp.float32)
    for cell_kind in range(conduct.shape[0]):
        weight = weight + jnp.where(
            cell_type[None] == cell_kind, conduct[cell_kind].reshape(lead_shape), 0.0
        )
    ion_current = jnp.sum(
        weight
        * gate_state[0::2]
        * gate_state[1::2]
        * (voltage[None] - reversal.reshape(lead_shape)),
        axis=0,
    )
    return (gate_state, ion_current)


def faces_of(block, dim):
    top = lax.index_in_dim(block, block.shape[dim] - 1, axis=dim, keepdims=False)
    bottom = lax.index_in_dim(block, 0, axis=dim, keepdims=False)
    return top, bottom


def heart_laplace(voltage, riders=None):
    parts = []
    carried = []
    for index, (axis, dim) in enumerate((("gx", 0), ("gy", 1), ("gz", 2))):
        pairs = [faces_of(voltage, dim)]
        if riders is not None:
            pairs.append(riders[index])
        got = exchange_group(pairs, axis)
        minus, plus = shifted(voltage, got[0][0], got[0][1], dim)
        parts.append((plus, minus))
        carried.append(got[1:])
    total = parts[0][0] + parts[0][1]
    total = total + parts[1][0] + parts[1][1]
    total = total + parts[2][0] + parts[2][1]
    return total - 6.0 * voltage, carried


def exchange(top, bottom, axis):
    count = lax.axis_size(axis)
    if count == 2:
        index = lax.axis_index(axis)
        got = lax.ppermute(jnp.where(index == 0, top, bottom), axis, [(0, 1), (1, 0)])
        zero = jnp.zeros_like(got)
        return jnp.where(index == 1, got, zero), jnp.where(index == 0, got, zero)
    forward = [(i, i + 1) for i in range(count - 1)]
    backward = [(i + 1, i) for i in range(count - 1)]
    return lax.ppermute(top, axis, forward), lax.ppermute(bottom, axis, backward)


def exchange_group(pairs, axis):
    if len(pairs) == 1:
        return [exchange(pairs[0][0], pairs[0][1], axis)]
    top = jnp.concatenate([item.reshape(-1) for item, _ in pairs])
    bottom = jnp.concatenate([item.reshape(-1) for _, item in pairs])
    low, high = exchange(top, bottom, axis)
    result = []
    offset = 0
    for item, _ in pairs:
        size = item.size
        result.append((low[offset:offset + size].reshape(item.shape), high[offset:offset + size].reshape(item.shape)))
        offset += size
    return result


def write_faces(x, value, columns, xf_lo, xf_hi, yf_lo, yf_hi, zf_lo, zf_hi):
    nx = yf_lo.shape[1]
    ny, nz = value.shape
    half = nz // 2
    lane = lax.broadcasted_iota(jnp.int32, (ny, nz), 1)

    @pl.when(x == 0)
    def _():
        xf_lo[0] = value

    @pl.when(x == nx - 1)
    def _():
        xf_hi[0] = value

    yf_lo[0, x] = value[0:1, :]
    yf_hi[0, x] = value[ny - 1:ny, :]
    columns = jnp.where(lane == x, jnp.broadcast_to(value[:, 0:1], (ny, nz)), columns)
    columns = jnp.where(lane == half + x, jnp.broadcast_to(value[:, nz - 1:nz], (ny, nz)), columns)
    return columns


def finish_faces(columns, xf_lo, xf_hi, yf_lo, yf_hi, zf_lo, zf_hi):
    nx = yf_lo.shape[1]
    half = columns.shape[1] // 2
    flipped = columns.T
    zf_lo[0] = flipped[0:nx, :]
    zf_hi[0] = flipped[half:half + nx, :]


def sweep_kernel(first, second, final, d_ref, r_ref, p_ref, fxp, fxm, fyp, fym, fzp, fzm, dg_ref, inv_ref,
                 xlo, xhi, ylo, yhi, zlo, zhi, r_out, d_out, p_out, *face_out):
    snapshot = pl.program_id(0)
    nx, ny, nz = d_ref.shape[1], d_ref.shape[2], d_ref.shape[3]
    row = lax.broadcasted_iota(jnp.int32, (ny, nz), 0)
    lane = lax.broadcasted_iota(jnp.int32, (ny, nz), 1)
    blank = jnp.zeros((nz - nx, ny), jnp.float32)
    low_cols = jnp.concatenate([zlo[0], blank], axis=0).T
    high_rows = zhi[0]
    high_cols = jnp.concatenate([high_rows[1:nx], blank, high_rows[0:1]], axis=0).T

    def body(x, carry):
        centre = d_ref[0, x]
        below = d_ref[0, jnp.maximum(x - 1, 0)]
        above = d_ref[0, jnp.minimum(x + 1, nx - 1)]
        x_minus = jnp.where(x == 0, xlo[0], below)
        x_plus = jnp.where(x == nx - 1, xhi[0], above)
        y_minus = jnp.where(row == 0, ylo[0, x], pltpu.roll(centre, 1, 0))
        y_plus = jnp.where(row == ny - 1, yhi[0, x], pltpu.roll(centre, ny - 1, 0))
        turn = lax.rem(nz - x, nz)
        z_minus = jnp.where(lane == 0, pltpu.roll(low_cols, turn, 1), pltpu.roll(centre, 1, 1))
        z_plus = jnp.where(lane == nz - 1, pltpu.roll(high_cols, turn, 1), pltpu.roll(centre, nz - 1, 1))
        beside = fxp[x] * x_plus + fxm[x] * x_minus
        beside = beside + fyp[x] * y_plus + fym[x] * y_minus
        beside = beside + fzp[x] * z_plus + fzm[x] * z_minus
        diag = dg_ref[x]
        residual = r_ref[0, x] - (diag * centre - beside)
        step_dir = first * centre + second * (residual * inv_ref[x])
        r_out[0, x] = residual
        d_out[0, x] = step_dir
        if final:
            p_out[x, :, snapshot, :] = p_ref[0, x] + step_dir
        else:
            p_out[0, x] = p_ref[0, x] + step_dir
        return write_faces(x, step_dir, carry, *face_out)

    columns = lax.fori_loop(0, nx, body, jnp.zeros((ny, nz), jnp.float32), unroll=2)
    finish_faces(columns, *face_out)


def initial_kernel(mid, r_ref, inv_ref, d_out, *face_out):
    nx, ny, nz = r_ref.shape[1], r_ref.shape[2], r_ref.shape[3]

    def body(x, carry):
        step_dir = r_ref[0, x] * inv_ref[x] * (1.0 / mid)
        d_out[0, x] = step_dir
        return write_faces(x, step_dir, carry, *face_out)

    columns = lax.fori_loop(0, nx, body, jnp.zeros((ny, nz), jnp.float32), unroll=2)
    finish_faces(columns, *face_out)


def specs(shape):
    steps, nx, ny, nz = shape
    full = pl.BlockSpec((1, nx, ny, nz), lambda s: (s, 0, 0, 0))
    fixed = pl.BlockSpec((nx, ny, nz), lambda s: (0, 0, 0))
    x_face = pl.BlockSpec((1, ny, nz), lambda s: (s, 0, 0))
    y_face = pl.BlockSpec((1, nx, 1, nz), lambda s: (s, 0, 0, 0))
    z_face = pl.BlockSpec((1, nx, ny), lambda s: (s, 0, 0))
    face_specs = [x_face, x_face, y_face, y_face, z_face, z_face]
    face_shapes = [
        jax.ShapeDtypeStruct((steps, ny, nz), jnp.float32),
        jax.ShapeDtypeStruct((steps, ny, nz), jnp.float32),
        jax.ShapeDtypeStruct((steps, nx, 1, nz), jnp.float32),
        jax.ShapeDtypeStruct((steps, nx, 1, nz), jnp.float32),
        jax.ShapeDtypeStruct((steps, nx, ny), jnp.float32),
        jax.ShapeDtypeStruct((steps, nx, ny), jnp.float32),
    ]
    return full, fixed, face_specs, face_shapes


def run_initial(mid, source, inverse):
    full, fixed, face_specs, face_shapes = specs(source.shape)
    shape = jax.ShapeDtypeStruct(source.shape, jnp.float32)
    size = source.size
    outs = pl.pallas_call(
        functools.partial(initial_kernel, mid),
        grid=(source.shape[0],),
        in_specs=[full, fixed],
        out_specs=[full] + face_specs,
        out_shape=[shape] + face_shapes,
        cost_estimate=pl.CostEstimate(flops=2 * size, transcendentals=0, bytes_accessed=8 * size + 4 * size // source.shape[0]),
        name="chebyshev_start",
    )(source, inverse)
    return outs[0], outs[1:]


def run_sweep(first, second, step_dir, residual, potential, faces, diagonal, inverse, halos, final=False):
    full, fixed, face_specs, face_shapes = specs(step_dir.shape)
    steps, nx, ny, nz = step_dir.shape
    x_face, y_face = face_specs[0], face_specs[2]
    shape = jax.ShapeDtypeStruct(step_dir.shape, jnp.float32)
    if final:
        out_spec = pl.BlockSpec((nx, ny, steps, nz), lambda s: (0, 0, 0, 0))
        out_shape = jax.ShapeDtypeStruct((nx, ny, steps, nz), jnp.float32)
    else:
        out_spec, out_shape = full, shape
    size = step_dir.size
    outs = pl.pallas_call(
        functools.partial(sweep_kernel, first, second, final),
        grid=(steps,),
        in_specs=[full, full, full] + [fixed] * 8 + [x_face, x_face, y_face, y_face, face_specs[4], face_specs[4]],
        out_specs=[full, full, out_spec] + face_specs,
        out_shape=[shape, shape, out_shape] + face_shapes,
        cost_estimate=pl.CostEstimate(flops=30 * size, transcendentals=0, bytes_accessed=4 * 7 * size + 4 * 7 * size // steps),
        name="chebyshev_sweep",
    )(step_dir, residual, potential, *faces, diagonal, inverse, *halos)
    return outs[0], outs[1], outs[2], outs[3:]


def local(
    heart_state,
    cell_type,
    gate_half,
    gate_slope,
    gate_tau,
    conduct,
    reversal,
    block_device,
    block_row,
    tissue,
    tissue_sigma,
):
    voltage = heart_state[0]
    gate_state = heart_state[1:]
    heart_x, heart_y, row_len = voltage.shape
    blocks = heart_x * heart_y
    devices = lax.axis_size("gx") * lax.axis_size("gy") * lax.axis_size("gz")
    capacity = 3 * blocks // devices
    slots = devices * capacity
    torso_x, torso_y, torso_z = tissue.shape
    torso_rows = torso_x * torso_y

    dest_dev = block_device.reshape(blocks)
    dest_row = block_row.reshape(blocks)
    one_hot = (dest_dev[:, None] == jnp.arange(devices, dtype=jnp.int32)[None, :]).astype(jnp.int32)
    running = jnp.cumsum(one_hot, axis=0) - 1
    slot_rank = jnp.sum(running * one_hot, axis=1)
    slot_index = dest_dev * capacity + slot_rank
    slot_match = slot_index[None, :] == jnp.arange(slots, dtype=jnp.int32)[:, None]
    slot_used = jnp.any(slot_match, axis=1)
    slot_block = jnp.argmax(slot_match, axis=1).astype(jnp.int32)
    send_rows = jnp.where(slot_used, dest_row[slot_block], torso_rows)
    recv_rows = lax.all_to_all(
        send_rows.reshape(devices, capacity), ("gx", "gy", "gz"), 0, 0, tiled=True
    ).reshape(slots)
    row_match = recv_rows[None, :] == jnp.arange(torso_rows, dtype=jnp.int32)[:, None]
    row_used = jnp.any(row_match, axis=1)
    row_slot = jnp.argmax(row_match, axis=1).astype(jnp.int32)

    sigma = []
    for dim_index in range(3):
        value = jnp.zeros(tissue.shape, jnp.float32)
        for tissue_kind in range(tissue_sigma.shape[0]):
            value = value + jnp.where(tissue == tissue_kind, tissue_sigma[tissue_kind, dim_index], 0.0)
        sigma.append(value)
    riders = [faces_of(sigma[dim_index], dim_index) for dim_index in range(3)]

    currents = []
    for time_step in range(STEPS):
        gate_state, ion_current = membrane(
            voltage, gate_state, cell_type, gate_half, gate_slope, gate_tau, conduct, reversal
        )
        laplace, carried = heart_laplace(voltage, riders if time_step == 0 else None)
        if time_step == 0:
            sigma_halos = [item[0] for item in carried]
        current = SIGMA_HEART * laplace
        currents.append(current)
        voltage = voltage + DT_HEART * (current - ion_current)
    heart_next = jnp.concatenate([voltage[None], gate_state], axis=0)

    payload = jnp.stack([item.reshape(blocks, row_len) for item in currents], axis=0)
    send_values = jnp.where(slot_used[None, :, None], jnp.take(payload, slot_block, axis=1), 0.0)
    received = lax.all_to_all(
        send_values.reshape(STEPS, devices, capacity, row_len),
        ("gx", "gy", "gz"),
        1,
        1,
        tiled=True,
    ).reshape(STEPS, slots, row_len)
    source = jnp.where(row_used[None, :, None], jnp.take(received, row_slot, axis=1), 0.0)
    source = source.reshape(STEPS, torso_x, torso_y, torso_z)

    faces = []
    for dim_index in range(3):
        low, high = sigma_halos[dim_index]
        minus, plus = shifted(sigma[dim_index], low, high, dim_index)
        faces.append(0.5 * (sigma[dim_index] + plus))
        faces.append(0.5 * (sigma[dim_index] + minus))
    diagonal = SCREEN + faces[0] + faces[1] + faces[2] + faces[3] + faces[4] + faces[5]

    spectrum_mid, first_coef, second_coef = chebyshev_weights(SWEEPS)
    residual = source
    inverse = 1.0 / diagonal
    step_dir, dir_faces = run_initial(spectrum_mid, residual, inverse)
    potential = step_dir
    for sweep in range(1, SWEEPS):
        x_low, x_high = exchange(dir_faces[1], dir_faces[0], "gx")
        y_low, y_high = exchange(dir_faces[3], dir_faces[2], "gy")
        z_low, z_high = exchange(dir_faces[5], dir_faces[4], "gz")
        halos = (x_low, x_high, y_low, y_high, z_low, z_high)
        residual, step_dir, potential, dir_faces = run_sweep(
            first_coef[sweep - 1], second_coef[sweep - 1], step_dir, residual, potential, faces, diagonal, inverse, halos,
            final=sweep == SWEEPS - 1,
        )
    return (heart_next, potential)


def solution(mesh):
    in_specs = (
        P(None, "gx", "gy", "gz"),
        P("gx", "gy", "gz"),
        P(),
        P(),
        P(),
        P(),
        P(),
        P("gx", "gy", "gz"),
        P("gx", "gy", "gz"),
        P("gx", "gy", "gz"),
        P(),
    )
    out_specs = (P(None, "gx", "gy", "gz"), P("gx", "gy", None, "gz"))
    return jax.shard_map(local, mesh=mesh, in_specs=in_specs, out_specs=out_specs, check_vma=False)
```

```python
import jax
import jax.numpy as jnp
from jax import lax
from jax.sharding import PartitionSpec as P
from jax.experimental import pallas as pl
from jax.experimental.pallas import tpu as pltpu
import functools

STEPS = 4
SWEEPS = 4


DT_HEART = 0.05
SIGMA_HEART = 1.0
SCREEN = 0.05
LOW_EDGE = 0.1
HIGH_EDGE = 1.9


def chebyshev_weights(sweep_count):
    spectrum_mid = 0.5 * (HIGH_EDGE + LOW_EDGE)
    half_width = 0.5 * (HIGH_EDGE - LOW_EDGE)
    half_ratio = spectrum_mid / half_width
    rho_old = 1.0 / half_ratio
    first_coef = []
    second_coef = []
    for sweep in range(1, sweep_count):
        rho_new = 1.0 / (2.0 * half_ratio - rho_old)
        first_coef.append(rho_new * rho_old)
        second_coef.append(2.0 * rho_new / half_width)
        rho_old = rho_new
    return (spectrum_mid, first_coef, second_coef)


def face_halos(block, axis, dim):
    top = lax.index_in_dim(block, block.shape[dim] - 1, axis=dim, keepdims=False)
    bottom = lax.index_in_dim(block, 0, axis=dim, keepdims=False)
    return exchange(top, bottom, axis)


def shifted(block, low, high, dim):
    n = block.shape[dim]
    low = jnp.expand_dims(low, dim)
    high = jnp.expand_dims(high, dim)
    minus = jnp.concatenate([low, lax.slice_in_dim(block, 0, n - 1, axis=dim)], axis=dim)
    plus = jnp.concatenate([lax.slice_in_dim(block, 1, n, axis=dim), high], axis=dim)
    return minus, plus


def membrane(voltage, gate_state, cell_type, gate_half, gate_slope, gate_tau, conduct, reversal):
    gate_count = gate_half.shape[0]
    lead_shape = (-1,) + (1,) * voltage.ndim
    gate_sign = jnp.where(jnp.arange(gate_count) % 2 == 0, 1.0, -1.0).astype(jnp.float32)
    exponent = (gate_sign / gate_slope).reshape(lead_shape) * (
        voltage[None] - gate_half.reshape(lead_shape)
    )
    steady = jax.nn.sigmoid(exponent)
    time_const = gate_tau.reshape(lead_shape) * (0.5 + steady)
    gate_state = steady + (gate_state - steady) * jnp.exp(-DT_HEART / time_const)
    weight = jnp.zeros(gate_state[0::2].shape, jnp.float32)
    for cell_kind in range(conduct.shape[0]):
        weight = weight + jnp.where(
            cell_type[None] == cell_kind, conduct[cell_kind].reshape(lead_shape), 0.0
        )
    ion_current = jnp.sum(
        weight
        * gate_state[0::2]
        * gate_state[1::2]
        * (voltage[None] - reversal.reshape(lead_shape)),
        axis=0,
    )
    return (gate_state, ion_current)


def faces_of(block, dim):
    top = lax.index_in_dim(block, block.shape[dim] - 1, axis=dim, keepdims=False)
    bottom = lax.index_in_dim(block, 0, axis=dim, keepdims=False)
    return top, bottom


def heart_laplace(voltage, riders=None):
    parts = []
    carried = []
    for index, (axis, dim) in enumerate((("gx", 0), ("gy", 1), ("gz", 2))):
        pairs = [faces_of(voltage, dim)]
        if riders is not None:
            pairs.append(riders[index])
        got = exchange_group(pairs, axis)
        minus, plus = shifted(voltage, got[0][0], got[0][1], dim)
        parts.append((plus, minus))
        carried.append(got[1:])
    total = parts[0][0] + parts[0][1]
    total = total + parts[1][0] + parts[1][1]
    total = total + parts[2][0] + parts[2][1]
    return total - 6.0 * voltage, carried


def exchange(top, bottom, axis):
    count = lax.axis_size(axis)
    if count == 2:
        index = lax.axis_index(axis)
        got = lax.ppermute(jnp.where(index == 0, top, bottom), axis, [(0, 1), (1, 0)])
        zero = jnp.zeros_like(got)
        return jnp.where(index == 1, got, zero), jnp.where(index == 0, got, zero)
    forward = [(i, i + 1) for i in range(count - 1)]
    backward = [(i + 1, i) for i in range(count - 1)]
    return lax.ppermute(top, axis, forward), lax.ppermute(bottom, axis, backward)


def exchange_group(pairs, axis):
    if len(pairs) == 1:
        return [exchange(pairs[0][0], pairs[0][1], axis)]
    top = jnp.concatenate([item.reshape(-1) for item, _ in pairs])
    bottom = jnp.concatenate([item.reshape(-1) for _, item in pairs])
    low, high = exchange(top, bottom, axis)
    result = []
    offset = 0
    for item, _ in pairs:
        size = item.size
        result.append((low[offset:offset + size].reshape(item.shape), high[offset:offset + size].reshape(item.shape)))
        offset += size
    return result


def write_faces(x, value, columns, xf_lo, xf_hi, yf_lo, yf_hi, zf_lo, zf_hi):
    nx = yf_lo.shape[1]
    ny, nz = value.shape
    half = nz // 2
    lane = lax.broadcasted_iota(jnp.int32, (ny, nz), 1)

    @pl.when(x == 0)
    def _():
        xf_lo[0] = value

    @pl.when(x == nx - 1)
    def _():
        xf_hi[0] = value

    yf_lo[0, x] = value[0:1, :]
    yf_hi[0, x] = value[ny - 1:ny, :]
    columns = jnp.where(lane == x, jnp.broadcast_to(value[:, 0:1], (ny, nz)), columns)
    columns = jnp.where(lane == half + x, jnp.broadcast_to(value[:, nz - 1:nz], (ny, nz)), columns)
    return columns


def finish_faces(columns, xf_lo, xf_hi, yf_lo, yf_hi, zf_lo, zf_hi):
    nx = yf_lo.shape[1]
    half = columns.shape[1] // 2
    flipped = columns.T
    zf_lo[0] = flipped[0:nx, :]
    zf_hi[0] = flipped[half:half + nx, :]


def sweep_kernel(first, second, final, d_ref, r_ref, p_ref, fxp, fxm, fyp, fym, fzp, fzm, dg_ref, inv_ref,
                 xlo, xhi, ylo, yhi, zlo, zhi, r_out, d_out, p_out, *face_out):
    snapshot = pl.program_id(0)
    nx, ny, nz = d_ref.shape[1], d_ref.shape[2], d_ref.shape[3]
    row = lax.broadcasted_iota(jnp.int32, (ny, nz), 0)
    lane = lax.broadcasted_iota(jnp.int32, (ny, nz), 1)
    blank = jnp.zeros((nz - nx, ny), jnp.float32)
    low_cols = jnp.concatenate([zlo[0], blank], axis=0).T
    high_rows = zhi[0]
    high_cols = jnp.concatenate([high_rows[1:nx], blank, high_rows[0:1]], axis=0).T

    def body(x, carry):
        centre = d_ref[0, x]
        below = d_ref[0, jnp.maximum(x - 1, 0)]
        above = d_ref[0, jnp.minimum(x + 1, nx - 1)]
        x_minus = jnp.where(x == 0, xlo[0], below)
        x_plus = jnp.where(x == nx - 1, xhi[0], above)
        y_minus = jnp.where(row == 0, ylo[0, x], pltpu.roll(centre, 1, 0))
        y_plus = jnp.where(row == ny - 1, yhi[0, x], pltpu.roll(centre, ny - 1, 0))
        turn = lax.rem(nz - x, nz)
        z_minus = jnp.where(lane == 0, pltpu.roll(low_cols, turn, 1), pltpu.roll(centre, 1, 1))
        z_plus = jnp.where(lane == nz - 1, pltpu.roll(high_cols, turn, 1), pltpu.roll(centre, nz - 1, 1))
        beside = fxp[x] * x_plus + fxm[x] * x_minus
        beside = beside + fyp[x] * y_plus + fym[x] * y_minus
        beside = beside + fzp[x] * z_plus + fzm[x] * z_minus
        diag = dg_ref[x]
        residual = r_ref[0, x] - (diag * centre - beside)
        step_dir = first * centre + second * (residual * inv_ref[x])
        r_out[0, x] = residual
        d_out[0, x] = step_dir
        if final:
            p_out[x, :, snapshot, :] = p_ref[0, x] + step_dir
        else:
            p_out[0, x] = p_ref[0, x] + step_dir
        return write_faces(x, step_dir, carry, *face_out)

    columns = lax.fori_loop(0, nx, body, jnp.zeros((ny, nz), jnp.float32), unroll=2)
    finish_faces(columns, *face_out)


def initial_kernel(mid, r_ref, inv_ref, d_out, *face_out):
    nx, ny, nz = r_ref.shape[1], r_ref.shape[2], r_ref.shape[3]

    def body(x, carry):
        step_dir = r_ref[0, x] * inv_ref[x] * (1.0 / mid)
        d_out[0, x] = step_dir
        return write_faces(x, step_dir, carry, *face_out)

    columns = lax.fori_loop(0, nx, body, jnp.zeros((ny, nz), jnp.float32), unroll=2)
    finish_faces(columns, *face_out)


def specs(shape):
    steps, nx, ny, nz = shape
    full = pl.BlockSpec((1, nx, ny, nz), lambda s: (s, 0, 0, 0))
    fixed = pl.BlockSpec((nx, ny, nz), lambda s: (0, 0, 0))
    x_face = pl.BlockSpec((1, ny, nz), lambda s: (s, 0, 0))
    y_face = pl.BlockSpec((1, nx, 1, nz), lambda s: (s, 0, 0, 0))
    z_face = pl.BlockSpec((1, nx, ny), lambda s: (s, 0, 0))
    face_specs = [x_face, x_face, y_face, y_face, z_face, z_face]
    face_shapes = [
        jax.ShapeDtypeStruct((steps, ny, nz), jnp.float32),
        jax.ShapeDtypeStruct((steps, ny, nz), jnp.float32),
        jax.ShapeDtypeStruct((steps, nx, 1, nz), jnp.float32),
        jax.ShapeDtypeStruct((steps, nx, 1, nz), jnp.float32),
        jax.ShapeDtypeStruct((steps, nx, ny), jnp.float32),
        jax.ShapeDtypeStruct((steps, nx, ny), jnp.float32),
    ]
    return full, fixed, face_specs, face_shapes


def run_initial(mid, source, inverse):
    full, fixed, face_specs, face_shapes = specs(source.shape)
    shape = jax.ShapeDtypeStruct(source.shape, jnp.float32)
    size = source.size
    outs = pl.pallas_call(
        functools.partial(initial_kernel, mid),
        grid=(source.shape[0],),
        in_specs=[full, fixed],
        out_specs=[full] + face_specs,
        out_shape=[shape] + face_shapes,
        cost_estimate=pl.CostEstimate(flops=2 * size, transcendentals=0, bytes_accessed=8 * size + 4 * size // source.shape[0]),
        name="chebyshev_start",
    )(source, inverse)
    return outs[0], outs[1:]


def run_sweep(first, second, step_dir, residual, potential, faces, diagonal, inverse, halos, final=False):
    full, fixed, face_specs, face_shapes = specs(step_dir.shape)
    steps, nx, ny, nz = step_dir.shape
    x_face, y_face = face_specs[0], face_specs[2]
    shape = jax.ShapeDtypeStruct(step_dir.shape, jnp.float32)
    if final:
        out_spec = pl.BlockSpec((nx, ny, steps, nz), lambda s: (0, 0, 0, 0))
        out_shape = jax.ShapeDtypeStruct((nx, ny, steps, nz), jnp.float32)
    else:
        out_spec, out_shape = full, shape
    size = step_dir.size
    outs = pl.pallas_call(
        functools.partial(sweep_kernel, first, second, final),
        grid=(steps,),
        in_specs=[full, full, full] + [fixed] * 8 + [x_face, x_face, y_face, y_face, face_specs[4], face_specs[4]],
        out_specs=[full, full, out_spec] + face_specs,
        out_shape=[shape, shape, out_shape] + face_shapes,
        cost_estimate=pl.CostEstimate(flops=30 * size, transcendentals=0, bytes_accessed=4 * 7 * size + 4 * 7 * size // steps),
        name="chebyshev_sweep",
    )(step_dir, residual, potential, *faces, diagonal, inverse, *halos)
    return outs[0], outs[1], outs[2], outs[3:]


def heart_kernel(kinds, coef, v_ref, g_ref, ct_ref, xlo, xhi, ylo, yhi, zlo, zhi,
                 g_out, c_out, v_out, xf_lo, xf_hi, yf_lo, yf_hi, zf_lo, zf_hi):
    i = pl.program_id(0)
    hx, hy, row = v_ref.shape
    gates = g_ref.shape[0]
    channels = gates // 2
    sub = lax.broadcasted_iota(jnp.int32, (hy, row), 0)
    lane = lax.broadcasted_iota(jnp.int32, (hy, row), 1)
    centre = v_ref[i]
    below = v_ref[jnp.maximum(i - 1, 0)]
    above = v_ref[jnp.minimum(i + 1, hx - 1)]
    x_minus = jnp.where(i == 0, xlo[...], below)
    x_plus = jnp.where(i == hx - 1, xhi[...], above)
    y_minus = jnp.where(sub == 0, ylo[i], pltpu.roll(centre, 1, 0))
    y_plus = jnp.where(sub == hy - 1, yhi[i], pltpu.roll(centre, hy - 1, 0))
    z_minus = jnp.where(lane == 0, pltpu.roll(zlo[...], lax.rem(row - i, row), 1), pltpu.roll(centre, 1, 1))
    z_plus = jnp.where(lane == row - 1, pltpu.roll(zhi[...], lax.rem(row - 1 - i + row, row), 1), pltpu.roll(centre, row - 1, 1))
    total = x_plus + x_minus
    total = total + y_plus + y_minus
    total = total + z_plus + z_minus
    current = SIGMA_HEART * (total - 6.0 * centre)
    cell = ct_ref[0]
    ion = None
    for channel in range(channels):
        updated = []
        for gate in (2 * channel, 2 * channel + 1):
            exponent = coef[gate] * (centre - coef[gates + gate])
            steady = 1.0 / (1.0 + jnp.exp(-exponent))
            time_const = coef[2 * gates + gate] * (0.5 + steady)
            value = steady + (g_ref[gate, 0] - steady) * jnp.exp(-DT_HEART / time_const)
            g_out[gate, 0] = value
            updated.append(value)
        weight = jnp.zeros((hy, row), jnp.float32)
        for kind in range(kinds):
            weight = weight + jnp.where(cell == kind, coef[3 * gates + kind * channels + channel], 0.0)
        term = weight * updated[0] * updated[1] * (centre - coef[3 * gates + kinds * channels + channel])
        ion = term if ion is None else ion + term
    new_v = centre + DT_HEART * (current - ion)
    c_out[0] = current
    v_out[0] = new_v

    @pl.when(i == 0)
    def _():
        xf_lo[...] = new_v
        zf_lo[...] = jnp.zeros(zf_lo.shape, jnp.float32)
        zf_hi[...] = jnp.zeros(zf_hi.shape, jnp.float32)

    @pl.when(i == hx - 1)
    def _():
        xf_hi[...] = new_v

    yf_lo[i] = new_v[0:1, :]
    yf_hi[i] = new_v[hy - 1:hy, :]
    zf_lo[...] = jnp.where(lane == i, jnp.broadcast_to(new_v[:, 0:1], (hy, row)), zf_lo[...])
    zf_hi[...] = jnp.where(lane == i, jnp.broadcast_to(new_v[:, row - 1:row], (hy, row)), zf_hi[...])


def heart_step(coef, kinds, voltage, gate_state, cell_type, halos):
    hx, hy, row = voltage.shape
    gates = gate_state.shape[0]
    whole = lambda shape: pl.BlockSpec(shape, lambda i: (0,) * len(shape))
    slab = pl.BlockSpec((1, hy, row), lambda i: (i, 0, 0))
    gate_slab = pl.BlockSpec((gates, 1, hy, row), lambda i: (0, i, 0, 0))
    plane = whole((hy, row))
    rows = whole((hx, 1, row))
    f32 = lambda shape: jax.ShapeDtypeStruct(shape, jnp.float32)
    size = voltage.size
    return pl.pallas_call(
        functools.partial(heart_kernel, kinds),
        grid=(hx,),
        in_specs=[pl.BlockSpec(memory_space=pltpu.SMEM), whole((hx, hy, row)), gate_slab, slab,
                  plane, plane, rows, rows, plane, plane],
        out_specs=[gate_slab, slab, slab, plane, plane, rows, rows, plane, plane],
        out_shape=[f32(gate_state.shape), f32(voltage.shape), f32(voltage.shape),
                   f32((hy, row)), f32((hy, row)), f32((hx, 1, row)), f32((hx, 1, row)),
                   f32((hy, row)), f32((hy, row))],
        cost_estimate=pl.CostEstimate(flops=40 * gates * size, transcendentals=3 * gates * size,
                                      bytes_accessed=4 * (2 * gates + 5) * size),
        name="heart_step",
    )(coef, voltage, gate_state, cell_type, *halos)


def voltage_faces(voltage):
    hx, hy, row = voltage.shape
    pad = jnp.zeros((hy, row - hx), jnp.float32)
    return (
        voltage[0], voltage[hx - 1],
        voltage[:, 0:1, :], voltage[:, hy - 1:hy, :],
        jnp.concatenate([voltage[:, :, 0].T, pad], axis=1),
        jnp.concatenate([voltage[:, :, row - 1].T, pad], axis=1),
    )


def local(
    heart_state,
    cell_type,
    gate_half,
    gate_slope,
    gate_tau,
    conduct,
    reversal,
    block_device,
    block_row,
    tissue,
    tissue_sigma,
):
    voltage = heart_state[0]
    gate_state = heart_state[1:]
    heart_x, heart_y, row_len = voltage.shape
    blocks = heart_x * heart_y
    devices = lax.axis_size("gx") * lax.axis_size("gy") * lax.axis_size("gz")
    capacity = 3 * blocks // devices
    slots = devices * capacity
    torso_x, torso_y, torso_z = tissue.shape
    torso_rows = torso_x * torso_y

    dest_dev = block_device.reshape(blocks)
    dest_row = block_row.reshape(blocks)
    one_hot = (dest_dev[:, None] == jnp.arange(devices, dtype=jnp.int32)[None, :]).astype(jnp.int32)
    running = jnp.cumsum(one_hot, axis=0) - 1
    slot_rank = jnp.sum(running * one_hot, axis=1)
    slot_index = dest_dev * capacity + slot_rank
    slot_match = slot_index[None, :] == jnp.arange(slots, dtype=jnp.int32)[:, None]
    slot_used = jnp.any(slot_match, axis=1)
    slot_block = jnp.argmax(slot_match, axis=1).astype(jnp.int32)
    send_rows = jnp.where(slot_used, dest_row[slot_block], torso_rows)
    recv_rows = lax.all_to_all(
        send_rows.reshape(devices, capacity), ("gx", "gy", "gz"), 0, 0, tiled=True
    ).reshape(slots)
    row_match = recv_rows[None, :] == jnp.arange(torso_rows, dtype=jnp.int32)[:, None]
    row_used = jnp.any(row_match, axis=1)
    row_slot = jnp.argmax(row_match, axis=1).astype(jnp.int32)

    sigma = []
    for dim_index in range(3):
        value = jnp.zeros(tissue.shape, jnp.float32)
        for tissue_kind in range(tissue_sigma.shape[0]):
            value = value + jnp.where(tissue == tissue_kind, tissue_sigma[tissue_kind, dim_index], 0.0)
        sigma.append(value)
    riders = [faces_of(sigma[dim_index], dim_index) for dim_index in range(3)]

    gate_count = gate_half.shape[0]
    gate_sign = jnp.where(jnp.arange(gate_count) % 2 == 0, 1.0, -1.0).astype(jnp.float32)
    coef = jnp.concatenate(
        [gate_sign / gate_slope, gate_half, gate_tau, conduct.reshape(-1), reversal]
    ).astype(jnp.float32)
    kinds = conduct.shape[0]
    faces_now = voltage_faces(voltage)
    currents = []
    for time_step in range(STEPS):
        halos = []
        for index, axis in enumerate(("gx", "gy", "gz")):
            pairs = [(faces_now[2 * index + 1], faces_now[2 * index])]
            if time_step == 0:
                pairs.append(riders[index])
            got = exchange_group(pairs, axis)
            halos.extend(got[0])
            if time_step == 0:
                if index == 0:
                    sigma_halos = []
                sigma_halos.append(got[1])
        outs = heart_step(coef, kinds, voltage, gate_state, cell_type, halos)
        gate_state, current, voltage = outs[0], outs[1], outs[2]
        faces_now = outs[3:]
        currents.append(current)
    heart_next = jnp.concatenate([voltage[None], gate_state], axis=0)

    payload = jnp.stack([item.reshape(blocks, row_len) for item in currents], axis=0)
    send_values = jnp.where(slot_used[None, :, None], jnp.take(payload, slot_block, axis=1), 0.0)
    received = lax.all_to_all(
        send_values.reshape(STEPS, devices, capacity, row_len),
        ("gx", "gy", "gz"),
        1,
        1,
        tiled=True,
    ).reshape(STEPS, slots, row_len)
    source = jnp.where(row_used[None, :, None], jnp.take(received, row_slot, axis=1), 0.0)
    source = source.reshape(STEPS, torso_x, torso_y, torso_z)

    faces = []
    for dim_index in range(3):
        low, high = sigma_halos[dim_index]
        minus, plus = shifted(sigma[dim_index], low, high, dim_index)
        faces.append(0.5 * (sigma[dim_index] + plus))
        faces.append(0.5 * (sigma[dim_index] + minus))
    diagonal = SCREEN + faces[0] + faces[1] + faces[2] + faces[3] + faces[4] + faces[5]

    spectrum_mid, first_coef, second_coef = chebyshev_weights(SWEEPS)
    residual = source
    inverse = 1.0 / diagonal
    step_dir, dir_faces = run_initial(spectrum_mid, residual, inverse)
    potential = step_dir
    for sweep in range(1, SWEEPS):
        x_low, x_high = exchange(dir_faces[1], dir_faces[0], "gx")
        y_low, y_high = exchange(dir_faces[3], dir_faces[2], "gy")
        z_low, z_high = exchange(dir_faces[5], dir_faces[4], "gz")
        halos = (x_low, x_high, y_low, y_high, z_low, z_high)
        residual, step_dir, potential, dir_faces = run_sweep(
            first_coef[sweep - 1], second_coef[sweep - 1], step_dir, residual, potential, faces, diagonal, inverse, halos,
            final=sweep == SWEEPS - 1,
        )
    return (heart_next, potential)


def solution(mesh):
    in_specs = (
        P(None, "gx", "gy", "gz"),
        P("gx", "gy", "gz"),
        P(),
        P(),
        P(),
        P(),
        P(),
        P("gx", "gy", "gz"),
        P("gx", "gy", "gz"),
        P("gx", "gy", "gz"),
        P(),
    )
    out_specs = (P(None, "gx", "gy", "gz"), P("gx", "gy", None, "gz"))
    return jax.shard_map(local, mesh=mesh, in_specs=in_specs, out_specs=out_specs, check_vma=False)
```

```python
import jax
import jax.numpy as jnp
from jax import lax
from jax.sharding import PartitionSpec as P
from jax.experimental import pallas as pl
from jax.experimental.pallas import tpu as pltpu
import functools

STEPS = 4
SWEEPS = 4


DT_HEART = 0.05
SIGMA_HEART = 1.0
SCREEN = 0.05
LOW_EDGE = 0.1
HIGH_EDGE = 1.9


def chebyshev_weights(sweep_count):
    spectrum_mid = 0.5 * (HIGH_EDGE + LOW_EDGE)
    half_width = 0.5 * (HIGH_EDGE - LOW_EDGE)
    half_ratio = spectrum_mid / half_width
    rho_old = 1.0 / half_ratio
    first_coef = []
    second_coef = []
    for sweep in range(1, sweep_count):
        rho_new = 1.0 / (2.0 * half_ratio - rho_old)
        first_coef.append(rho_new * rho_old)
        second_coef.append(2.0 * rho_new / half_width)
        rho_old = rho_new
    return (spectrum_mid, first_coef, second_coef)


def face_halos(block, axis, dim):
    top = lax.index_in_dim(block, block.shape[dim] - 1, axis=dim, keepdims=False)
    bottom = lax.index_in_dim(block, 0, axis=dim, keepdims=False)
    return exchange(top, bottom, axis)


def shifted(block, low, high, dim):
    n = block.shape[dim]
    low = jnp.expand_dims(low, dim)
    high = jnp.expand_dims(high, dim)
    minus = jnp.concatenate([low, lax.slice_in_dim(block, 0, n - 1, axis=dim)], axis=dim)
    plus = jnp.concatenate([lax.slice_in_dim(block, 1, n, axis=dim), high], axis=dim)
    return minus, plus


def membrane(voltage, gate_state, cell_type, gate_half, gate_slope, gate_tau, conduct, reversal):
    gate_count = gate_half.shape[0]
    lead_shape = (-1,) + (1,) * voltage.ndim
    gate_sign = jnp.where(jnp.arange(gate_count) % 2 == 0, 1.0, -1.0).astype(jnp.float32)
    exponent = (gate_sign / gate_slope).reshape(lead_shape) * (
        voltage[None] - gate_half.reshape(lead_shape)
    )
    steady = jax.nn.sigmoid(exponent)
    time_const = gate_tau.reshape(lead_shape) * (0.5 + steady)
    gate_state = steady + (gate_state - steady) * jnp.exp(-DT_HEART / time_const)
    weight = jnp.zeros(gate_state[0::2].shape, jnp.float32)
    for cell_kind in range(conduct.shape[0]):
        weight = weight + jnp.where(
            cell_type[None] == cell_kind, conduct[cell_kind].reshape(lead_shape), 0.0
        )
    ion_current = jnp.sum(
        weight
        * gate_state[0::2]
        * gate_state[1::2]
        * (voltage[None] - reversal.reshape(lead_shape)),
        axis=0,
    )
    return (gate_state, ion_current)


def faces_of(block, dim):
    top = lax.index_in_dim(block, block.shape[dim] - 1, axis=dim, keepdims=False)
    bottom = lax.index_in_dim(block, 0, axis=dim, keepdims=False)
    return top, bottom


def heart_laplace(voltage, riders=None):
    parts = []
    carried = []
    for index, (axis, dim) in enumerate((("gx", 0), ("gy", 1), ("gz", 2))):
        pairs = [faces_of(voltage, dim)]
        if riders is not None:
            pairs.append(riders[index])
        got = exchange_group(pairs, axis)
        minus, plus = shifted(voltage, got[0][0], got[0][1], dim)
        parts.append((plus, minus))
        carried.append(got[1:])
    total = parts[0][0] + parts[0][1]
    total = total + parts[1][0] + parts[1][1]
    total = total + parts[2][0] + parts[2][1]
    return total - 6.0 * voltage, carried


def exchange(top, bottom, axis):
    count = lax.axis_size(axis)
    if count == 2:
        index = lax.axis_index(axis)
        got = lax.ppermute(jnp.where(index == 0, top, bottom), axis, [(0, 1), (1, 0)])
        zero = jnp.zeros_like(got)
        return jnp.where(index == 1, got, zero), jnp.where(index == 0, got, zero)
    forward = [(i, i + 1) for i in range(count - 1)]
    backward = [(i + 1, i) for i in range(count - 1)]
    return lax.ppermute(top, axis, forward), lax.ppermute(bottom, axis, backward)


def exchange_group(pairs, axis):
    if len(pairs) == 1:
        return [exchange(pairs[0][0], pairs[0][1], axis)]
    top = jnp.concatenate([item.reshape(-1) for item, _ in pairs])
    bottom = jnp.concatenate([item.reshape(-1) for _, item in pairs])
    low, high = exchange(top, bottom, axis)
    result = []
    offset = 0
    for item, _ in pairs:
        size = item.size
        result.append((low[offset:offset + size].reshape(item.shape), high[offset:offset + size].reshape(item.shape)))
        offset += size
    return result


def write_faces(x, value, columns, xf_lo, xf_hi, yf_lo, yf_hi, zf_lo, zf_hi):
    nx = yf_lo.shape[1]
    ny, nz = value.shape
    half = nz // 2
    lane = lax.broadcasted_iota(jnp.int32, (ny, nz), 1)

    @pl.when(x == 0)
    def _():
        xf_lo[0] = value

    @pl.when(x == nx - 1)
    def _():
        xf_hi[0] = value

    yf_lo[0, x] = value[0:1, :]
    yf_hi[0, x] = value[ny - 1:ny, :]
    columns = jnp.where(lane == x, jnp.broadcast_to(value[:, 0:1], (ny, nz)), columns)
    columns = jnp.where(lane == half + x, jnp.broadcast_to(value[:, nz - 1:nz], (ny, nz)), columns)
    return columns


def finish_faces(columns, xf_lo, xf_hi, yf_lo, yf_hi, zf_lo, zf_hi):
    nx = yf_lo.shape[1]
    half = columns.shape[1] // 2
    flipped = columns.T
    zf_lo[0] = flipped[0:nx, :]
    zf_hi[0] = flipped[half:half + nx, :]


def sweep_kernel(first, second, final, d_ref, r_ref, p_ref, fxp, fxm, fyp, fym, fzp, fzm, dg_ref, inv_ref,
                 xlo, xhi, ylo, yhi, zlo, zhi, r_out, d_out, p_out, *face_out):
    snapshot = pl.program_id(0)
    nx, ny, nz = d_ref.shape[1], d_ref.shape[2], d_ref.shape[3]
    row = lax.broadcasted_iota(jnp.int32, (ny, nz), 0)
    lane = lax.broadcasted_iota(jnp.int32, (ny, nz), 1)
    blank = jnp.zeros((nz - nx, ny), jnp.float32)
    low_cols = jnp.concatenate([zlo[0], blank], axis=0).T
    high_rows = zhi[0]
    high_cols = jnp.concatenate([high_rows[1:nx], blank, high_rows[0:1]], axis=0).T

    def body(x, carry):
        centre = d_ref[0, x]
        below = d_ref[0, jnp.maximum(x - 1, 0)]
        above = d_ref[0, jnp.minimum(x + 1, nx - 1)]
        x_minus = jnp.where(x == 0, xlo[0], below)
        x_plus = jnp.where(x == nx - 1, xhi[0], above)
        y_minus = jnp.where(row == 0, ylo[0, x], pltpu.roll(centre, 1, 0))
        y_plus = jnp.where(row == ny - 1, yhi[0, x], pltpu.roll(centre, ny - 1, 0))
        turn = lax.rem(nz - x, nz)
        z_minus = jnp.where(lane == 0, pltpu.roll(low_cols, turn, 1), pltpu.roll(centre, 1, 1))
        z_plus = jnp.where(lane == nz - 1, pltpu.roll(high_cols, turn, 1), pltpu.roll(centre, nz - 1, 1))
        beside = fxp[x] * x_plus + fxm[x] * x_minus
        beside = beside + fyp[x] * y_plus + fym[x] * y_minus
        beside = beside + fzp[x] * z_plus + fzm[x] * z_minus
        diag = dg_ref[x]
        residual = r_ref[0, x] - (diag * centre - beside)
        step_dir = first * centre + second * (residual * inv_ref[x])
        r_out[0, x] = residual
        d_out[0, x] = step_dir
        if final:
            p_out[x, :, snapshot, :] = p_ref[0, x] + step_dir
        else:
            p_out[0, x] = p_ref[0, x] + step_dir
        return write_faces(x, step_dir, carry, *face_out)

    columns = lax.fori_loop(0, nx, body, jnp.zeros((ny, nz), jnp.float32), unroll=2)
    finish_faces(columns, *face_out)


def initial_kernel(mid, r_ref, inv_ref, d_out, *face_out):
    nx, ny, nz = r_ref.shape[1], r_ref.shape[2], r_ref.shape[3]

    def body(x, carry):
        step_dir = r_ref[0, x] * inv_ref[x] * (1.0 / mid)
        d_out[0, x] = step_dir
        return write_faces(x, step_dir, carry, *face_out)

    columns = lax.fori_loop(0, nx, body, jnp.zeros((ny, nz), jnp.float32), unroll=2)
    finish_faces(columns, *face_out)


def specs(shape):
    steps, nx, ny, nz = shape
    full = pl.BlockSpec((1, nx, ny, nz), lambda s: (s, 0, 0, 0))
    fixed = pl.BlockSpec((nx, ny, nz), lambda s: (0, 0, 0))
    x_face = pl.BlockSpec((1, ny, nz), lambda s: (s, 0, 0))
    y_face = pl.BlockSpec((1, nx, 1, nz), lambda s: (s, 0, 0, 0))
    z_face = pl.BlockSpec((1, nx, ny), lambda s: (s, 0, 0))
    face_specs = [x_face, x_face, y_face, y_face, z_face, z_face]
    face_shapes = [
        jax.ShapeDtypeStruct((steps, ny, nz), jnp.float32),
        jax.ShapeDtypeStruct((steps, ny, nz), jnp.float32),
        jax.ShapeDtypeStruct((steps, nx, 1, nz), jnp.float32),
        jax.ShapeDtypeStruct((steps, nx, 1, nz), jnp.float32),
        jax.ShapeDtypeStruct((steps, nx, ny), jnp.float32),
        jax.ShapeDtypeStruct((steps, nx, ny), jnp.float32),
    ]
    return full, fixed, face_specs, face_shapes


def run_initial(mid, source, inverse):
    full, fixed, face_specs, face_shapes = specs(source.shape)
    shape = jax.ShapeDtypeStruct(source.shape, jnp.float32)
    size = source.size
    outs = pl.pallas_call(
        functools.partial(initial_kernel, mid),
        grid=(source.shape[0],),
        in_specs=[full, fixed],
        out_specs=[full] + face_specs,
        out_shape=[shape] + face_shapes,
        cost_estimate=pl.CostEstimate(flops=2 * size, transcendentals=0, bytes_accessed=8 * size + 4 * size // source.shape[0]),
        name="chebyshev_start",
    )(source, inverse)
    return outs[0], outs[1:]


def run_sweep(first, second, step_dir, residual, potential, faces, diagonal, inverse, halos, final=False):
    full, fixed, face_specs, face_shapes = specs(step_dir.shape)
    steps, nx, ny, nz = step_dir.shape
    x_face, y_face = face_specs[0], face_specs[2]
    shape = jax.ShapeDtypeStruct(step_dir.shape, jnp.float32)
    if final:
        out_spec = pl.BlockSpec((nx, ny, steps, nz), lambda s: (0, 0, 0, 0))
        out_shape = jax.ShapeDtypeStruct((nx, ny, steps, nz), jnp.float32)
    else:
        out_spec, out_shape = full, shape
    size = step_dir.size
    outs = pl.pallas_call(
        functools.partial(sweep_kernel, first, second, final),
        grid=(steps,),
        in_specs=[full, full, full] + [fixed] * 8 + [x_face, x_face, y_face, y_face, face_specs[4], face_specs[4]],
        out_specs=[full, full, out_spec] + face_specs,
        out_shape=[shape, shape, out_shape] + face_shapes,
        cost_estimate=pl.CostEstimate(flops=30 * size, transcendentals=0, bytes_accessed=4 * 7 * size + 4 * 7 * size // steps),
        name="chebyshev_sweep",
    )(step_dir, residual, potential, *faces, diagonal, inverse, *halos)
    return outs[0], outs[1], outs[2], outs[3:]


def sigma_kernel(sigma_ref, t_ref, sx, sy, sz, x_lo, x_hi, y_lo, y_hi, z_lo, z_hi):
    nx, ny, nz = t_ref.shape
    kinds = sigma_ref.shape[0] // 3
    half = nz // 2
    lane = lax.broadcasted_iota(jnp.int32, (ny, nz), 1)

    def body(x, columns):
        cls = t_ref[x]
        values = []
        for dim_index in range(3):
            value = jnp.zeros((ny, nz), jnp.float32)
            for kind in range(kinds):
                value = value + jnp.where(cls == kind, sigma_ref[3 * kind + dim_index], 0.0)
            values.append(value)
        sx[x] = values[0]
        sy[x] = values[1]
        sz[x] = values[2]
        y_lo[pl.ds(x, 1), :] = values[1][0:1, :]
        y_hi[pl.ds(x, 1), :] = values[1][ny - 1:ny, :]
        columns = jnp.where(lane == x, jnp.broadcast_to(values[2][:, 0:1], (ny, nz)), columns)
        return jnp.where(lane == half + x, jnp.broadcast_to(values[2][:, nz - 1:nz], (ny, nz)), columns)

    columns = lax.fori_loop(0, nx, body, jnp.zeros((ny, nz), jnp.float32))
    x_lo[...] = sx[0]
    x_hi[...] = sx[nx - 1]
    flipped = columns.T
    z_lo[...] = flipped[0:nx, :]
    z_hi[...] = flipped[half:half + nx, :]


def conductivity(tissue, tissue_sigma):
    nx, ny, nz = tissue.shape
    vmem = pl.BlockSpec(memory_space=pltpu.VMEM)
    f32 = lambda shape: jax.ShapeDtypeStruct(shape, jnp.float32)
    outs = pl.pallas_call(
        sigma_kernel,
        in_specs=[pl.BlockSpec(memory_space=pltpu.SMEM), vmem],
        out_specs=[vmem] * 9,
        out_shape=[f32(tissue.shape)] * 3 + [f32((ny, nz))] * 2 + [f32((nx, nz))] * 2 + [f32((nx, ny))] * 2,
        cost_estimate=pl.CostEstimate(flops=24 * tissue.size, transcendentals=0, bytes_accessed=16 * tissue.size),
        name="tissue_conductivity",
    )(tissue_sigma.reshape(-1).astype(jnp.float32), tissue)
    sigma = list(outs[0:3])
    riders = [(outs[4], outs[3]), (outs[6], outs[5]), (outs[8], outs[7])]
    return sigma, riders


def local(
    heart_state,
    cell_type,
    gate_half,
    gate_slope,
    gate_tau,
    conduct,
    reversal,
    block_device,
    block_row,
    tissue,
    tissue_sigma,
):
    voltage = heart_state[0]
    gate_state = heart_state[1:]
    heart_x, heart_y, row_len = voltage.shape
    blocks = heart_x * heart_y
    devices = lax.axis_size("gx") * lax.axis_size("gy") * lax.axis_size("gz")
    capacity = 3 * blocks // devices
    slots = devices * capacity
    torso_x, torso_y, torso_z = tissue.shape
    torso_rows = torso_x * torso_y

    dest_dev = block_device.reshape(blocks)
    dest_row = block_row.reshape(blocks)
    one_hot = (dest_dev[:, None] == jnp.arange(devices, dtype=jnp.int32)[None, :]).astype(jnp.int32)
    running = jnp.cumsum(one_hot, axis=0) - 1
    slot_rank = jnp.sum(running * one_hot, axis=1)
    slot_index = dest_dev * capacity + slot_rank
    slot_match = slot_index[None, :] == jnp.arange(slots, dtype=jnp.int32)[:, None]
    slot_used = jnp.any(slot_match, axis=1)
    slot_block = jnp.argmax(slot_match, axis=1).astype(jnp.int32)
    send_rows = jnp.where(slot_used, dest_row[slot_block], torso_rows)
    recv_rows = lax.all_to_all(
        send_rows.reshape(devices, capacity), ("gx", "gy", "gz"), 0, 0, tiled=True
    ).reshape(slots)
    row_match = recv_rows[None, :] == jnp.arange(torso_rows, dtype=jnp.int32)[:, None]
    row_used = jnp.any(row_match, axis=1)
    row_slot = jnp.argmax(row_match, axis=1).astype(jnp.int32)

    sigma, riders = conductivity(tissue, tissue_sigma)

    currents = []
    for time_step in range(STEPS):
        gate_state, ion_current = membrane(
            voltage, gate_state, cell_type, gate_half, gate_slope, gate_tau, conduct, reversal
        )
        laplace, carried = heart_laplace(voltage, riders if time_step == 0 else None)
        if time_step == 0:
            sigma_halos = [item[0] for item in carried]
        current = SIGMA_HEART * laplace
        currents.append(current)
        voltage = voltage + DT_HEART * (current - ion_current)
    heart_next = jnp.concatenate([voltage[None], gate_state], axis=0)

    payload = jnp.stack([item.reshape(blocks, row_len) for item in currents], axis=0)
    send_values = jnp.where(slot_used[None, :, None], jnp.take(payload, slot_block, axis=1), 0.0)
    received = lax.all_to_all(
        send_values.reshape(STEPS, devices, capacity, row_len),
        ("gx", "gy", "gz"),
        1,
        1,
        tiled=True,
    ).reshape(STEPS, slots, row_len)
    source = jnp.where(row_used[None, :, None], jnp.take(received, row_slot, axis=1), 0.0)
    source = source.reshape(STEPS, torso_x, torso_y, torso_z)

    faces = []
    for dim_index in range(3):
        low, high = sigma_halos[dim_index]
        minus, plus = shifted(sigma[dim_index], low, high, dim_index)
        faces.append(0.5 * (sigma[dim_index] + plus))
        faces.append(0.5 * (sigma[dim_index] + minus))
    diagonal = SCREEN + faces[0] + faces[1] + faces[2] + faces[3] + faces[4] + faces[5]

    spectrum_mid, first_coef, second_coef = chebyshev_weights(SWEEPS)
    residual = source
    inverse = 1.0 / diagonal
    step_dir, dir_faces = run_initial(spectrum_mid, residual, inverse)
    potential = step_dir
    for sweep in range(1, SWEEPS):
        x_low, x_high = exchange(dir_faces[1], dir_faces[0], "gx")
        y_low, y_high = exchange(dir_faces[3], dir_faces[2], "gy")
        z_low, z_high = exchange(dir_faces[5], dir_faces[4], "gz")
        halos = (x_low, x_high, y_low, y_high, z_low, z_high)
        residual, step_dir, potential, dir_faces = run_sweep(
            first_coef[sweep - 1], second_coef[sweep - 1], step_dir, residual, potential, faces, diagonal, inverse, halos,
            final=sweep == SWEEPS - 1,
        )
    return (heart_next, potential)


def solution(mesh):
    in_specs = (
        P(None, "gx", "gy", "gz"),
        P("gx", "gy", "gz"),
        P(),
        P(),
        P(),
        P(),
        P(),
        P("gx", "gy", "gz"),
        P("gx", "gy", "gz"),
        P("gx", "gy", "gz"),
        P(),
    )
    out_specs = (P(None, "gx", "gy", "gz"), P("gx", "gy", None, "gz"))
    return jax.shard_map(local, mesh=mesh, in_specs=in_specs, out_specs=out_specs, check_vma=False)
```

```python
import jax
import jax.numpy as jnp
from jax import lax
from jax.sharding import PartitionSpec as P
from jax.experimental import pallas as pl
from jax.experimental.pallas import tpu as pltpu
import functools

STEPS = 4
SWEEPS = 4


DT_HEART = 0.05
SIGMA_HEART = 1.0
SCREEN = 0.05
LOW_EDGE = 0.1
HIGH_EDGE = 1.9


def chebyshev_weights(sweep_count):
    spectrum_mid = 0.5 * (HIGH_EDGE + LOW_EDGE)
    half_width = 0.5 * (HIGH_EDGE - LOW_EDGE)
    half_ratio = spectrum_mid / half_width
    rho_old = 1.0 / half_ratio
    first_coef = []
    second_coef = []
    for sweep in range(1, sweep_count):
        rho_new = 1.0 / (2.0 * half_ratio - rho_old)
        first_coef.append(rho_new * rho_old)
        second_coef.append(2.0 * rho_new / half_width)
        rho_old = rho_new
    return (spectrum_mid, first_coef, second_coef)


def face_halos(block, axis, dim):
    top = lax.index_in_dim(block, block.shape[dim] - 1, axis=dim, keepdims=False)
    bottom = lax.index_in_dim(block, 0, axis=dim, keepdims=False)
    return exchange(top, bottom, axis)


def shifted(block, low, high, dim):
    n = block.shape[dim]
    low = jnp.expand_dims(low, dim)
    high = jnp.expand_dims(high, dim)
    minus = jnp.concatenate([low, lax.slice_in_dim(block, 0, n - 1, axis=dim)], axis=dim)
    plus = jnp.concatenate([lax.slice_in_dim(block, 1, n, axis=dim), high], axis=dim)
    return minus, plus


def membrane(voltage, gate_state, cell_type, gate_half, gate_slope, gate_tau, conduct, reversal):
    gate_count = gate_half.shape[0]
    lead_shape = (-1,) + (1,) * voltage.ndim
    gate_sign = jnp.where(jnp.arange(gate_count) % 2 == 0, 1.0, -1.0).astype(jnp.float32)
    exponent = (gate_sign / gate_slope).reshape(lead_shape) * (
        voltage[None] - gate_half.reshape(lead_shape)
    )
    steady = jax.nn.sigmoid(exponent)
    time_const = gate_tau.reshape(lead_shape) * (0.5 + steady)
    gate_state = steady + (gate_state - steady) * jnp.exp(-DT_HEART / time_const)
    weight = jnp.zeros(gate_state[0::2].shape, jnp.float32)
    for cell_kind in range(conduct.shape[0]):
        weight = weight + jnp.where(
            cell_type[None] == cell_kind, conduct[cell_kind].reshape(lead_shape), 0.0
        )
    ion_current = jnp.sum(
        weight
        * gate_state[0::2]
        * gate_state[1::2]
        * (voltage[None] - reversal.reshape(lead_shape)),
        axis=0,
    )
    return (gate_state, ion_current)


def faces_of(block, dim):
    top = lax.index_in_dim(block, block.shape[dim] - 1, axis=dim, keepdims=False)
    bottom = lax.index_in_dim(block, 0, axis=dim, keepdims=False)
    return top, bottom


def heart_laplace(voltage, riders=None):
    parts = []
    carried = []
    for index, (axis, dim) in enumerate((("gx", 0), ("gy", 1), ("gz", 2))):
        pairs = [faces_of(voltage, dim)]
        if riders is not None:
            pairs.append(riders[index])
        got = exchange_group(pairs, axis)
        minus, plus = shifted(voltage, got[0][0], got[0][1], dim)
        parts.append((plus, minus))
        carried.append(got[1:])
    total = parts[0][0] + parts[0][1]
    total = total + parts[1][0] + parts[1][1]
    total = total + parts[2][0] + parts[2][1]
    return total - 6.0 * voltage, carried


def exchange(top, bottom, axis):
    count = lax.axis_size(axis)
    if count == 2:
        index = lax.axis_index(axis)
        got = lax.ppermute(jnp.where(index == 0, top, bottom), axis, [(0, 1), (1, 0)])
        zero = jnp.zeros_like(got)
        return jnp.where(index == 1, got, zero), jnp.where(index == 0, got, zero)
    forward = [(i, i + 1) for i in range(count - 1)]
    backward = [(i + 1, i) for i in range(count - 1)]
    return lax.ppermute(top, axis, forward), lax.ppermute(bottom, axis, backward)


def exchange_group(pairs, axis):
    if len(pairs) == 1:
        return [exchange(pairs[0][0], pairs[0][1], axis)]
    top = jnp.concatenate([item.reshape(-1) for item, _ in pairs])
    bottom = jnp.concatenate([item.reshape(-1) for _, item in pairs])
    low, high = exchange(top, bottom, axis)
    result = []
    offset = 0
    for item, _ in pairs:
        size = item.size
        result.append((low[offset:offset + size].reshape(item.shape), high[offset:offset + size].reshape(item.shape)))
        offset += size
    return result


def write_faces(x, value, columns, xf_lo, xf_hi, yf_lo, yf_hi, zf_lo, zf_hi):
    nx = yf_lo.shape[1]
    ny, nz = value.shape
    half = nz // 2
    lane = lax.broadcasted_iota(jnp.int32, (ny, nz), 1)

    @pl.when(x == 0)
    def _():
        xf_lo[0] = value

    @pl.when(x == nx - 1)
    def _():
        xf_hi[0] = value

    yf_lo[0, x] = value[0:1, :]
    yf_hi[0, x] = value[ny - 1:ny, :]
    columns = jnp.where(lane == x, jnp.broadcast_to(value[:, 0:1], (ny, nz)), columns)
    columns = jnp.where(lane == half + x, jnp.broadcast_to(value[:, nz - 1:nz], (ny, nz)), columns)
    return columns


def finish_faces(columns, xf_lo, xf_hi, yf_lo, yf_hi, zf_lo, zf_hi):
    nx = yf_lo.shape[1]
    half = columns.shape[1] // 2
    flipped = columns.T
    zf_lo[0] = flipped[0:nx, :]
    zf_hi[0] = flipped[half:half + nx, :]


def sweep_kernel(final, coef_ref, d_ref, r_ref, p_ref, fxp, fxm, fyp, fym, fzp, fzm, dg_ref, inv_ref,
                 xlo, xhi, ylo, yhi, zlo, zhi, r_out, d_out, p_out, *face_out):
    snapshot = pl.program_id(0)
    first = coef_ref[0]
    second = coef_ref[1]
    nx, ny, nz = d_ref.shape[1], d_ref.shape[2], d_ref.shape[3]
    row = lax.broadcasted_iota(jnp.int32, (ny, nz), 0)
    lane = lax.broadcasted_iota(jnp.int32, (ny, nz), 1)
    blank = jnp.zeros((nz - nx, ny), jnp.float32)
    low_cols = jnp.concatenate([zlo[0], blank], axis=0).T
    high_rows = zhi[0]
    high_cols = jnp.concatenate([high_rows[1:nx], blank, high_rows[0:1]], axis=0).T

    def body(x, carry):
        centre = d_ref[0, x]
        below = d_ref[0, jnp.maximum(x - 1, 0)]
        above = d_ref[0, jnp.minimum(x + 1, nx - 1)]
        x_minus = jnp.where(x == 0, xlo[0], below)
        x_plus = jnp.where(x == nx - 1, xhi[0], above)
        y_minus = jnp.where(row == 0, ylo[0, x], pltpu.roll(centre, 1, 0))
        y_plus = jnp.where(row == ny - 1, yhi[0, x], pltpu.roll(centre, ny - 1, 0))
        turn = lax.rem(nz - x, nz)
        z_minus = jnp.where(lane == 0, pltpu.roll(low_cols, turn, 1), pltpu.roll(centre, 1, 1))
        z_plus = jnp.where(lane == nz - 1, pltpu.roll(high_cols, turn, 1), pltpu.roll(centre, nz - 1, 1))
        beside = fxp[x] * x_plus + fxm[x] * x_minus
        beside = beside + fyp[x] * y_plus + fym[x] * y_minus
        beside = beside + fzp[x] * z_plus + fzm[x] * z_minus
        diag = dg_ref[x]
        residual = r_ref[0, x] - (diag * centre - beside)
        step_dir = first * centre + second * (residual * inv_ref[x])
        r_out[0, x] = residual
        d_out[0, x] = step_dir
        if final:
            p_out[x, :, snapshot, :] = p_ref[0, x] + step_dir
        else:
            p_out[0, x] = p_ref[0, x] + step_dir
        return write_faces(x, step_dir, carry, *face_out)

    columns = lax.fori_loop(0, nx, body, jnp.zeros((ny, nz), jnp.float32), unroll=4)
    finish_faces(columns, *face_out)


def initial_kernel(mid, r_ref, inv_ref, d_out, *face_out):
    nx, ny, nz = r_ref.shape[1], r_ref.shape[2], r_ref.shape[3]

    def body(x, carry):
        step_dir = r_ref[0, x] * inv_ref[x] * (1.0 / mid)
        d_out[0, x] = step_dir
        return write_faces(x, step_dir, carry, *face_out)

    columns = lax.fori_loop(0, nx, body, jnp.zeros((ny, nz), jnp.float32), unroll=2)
    finish_faces(columns, *face_out)


def specs(shape):
    steps, nx, ny, nz = shape
    full = pl.BlockSpec((1, nx, ny, nz), lambda s: (s, 0, 0, 0))
    fixed = pl.BlockSpec((nx, ny, nz), lambda s: (0, 0, 0))
    x_face = pl.BlockSpec((1, ny, nz), lambda s: (s, 0, 0))
    y_face = pl.BlockSpec((1, nx, 1, nz), lambda s: (s, 0, 0, 0))
    z_face = pl.BlockSpec((1, nx, ny), lambda s: (s, 0, 0))
    face_specs = [x_face, x_face, y_face, y_face, z_face, z_face]
    face_shapes = [
        jax.ShapeDtypeStruct((steps, ny, nz), jnp.float32),
        jax.ShapeDtypeStruct((steps, ny, nz), jnp.float32),
        jax.ShapeDtypeStruct((steps, nx, 1, nz), jnp.float32),
        jax.ShapeDtypeStruct((steps, nx, 1, nz), jnp.float32),
        jax.ShapeDtypeStruct((steps, nx, ny), jnp.float32),
        jax.ShapeDtypeStruct((steps, nx, ny), jnp.float32),
    ]
    return full, fixed, face_specs, face_shapes


def run_initial(mid, source, inverse):
    full, fixed, face_specs, face_shapes = specs(source.shape)
    shape = jax.ShapeDtypeStruct(source.shape, jnp.float32)
    size = source.size
    outs = pl.pallas_call(
        functools.partial(initial_kernel, mid),
        grid=(source.shape[0],),
        in_specs=[full, fixed],
        out_specs=[full] + face_specs,
        out_shape=[shape] + face_shapes,
        cost_estimate=pl.CostEstimate(flops=2 * size, transcendentals=0, bytes_accessed=8 * size + 4 * size // source.shape[0]),
        name="chebyshev_start",
    )(source, inverse)
    return outs[0], outs[1:]


def run_sweep(first, second, step_dir, residual, potential, faces, diagonal, inverse, halos, final=False):
    full, fixed, face_specs, face_shapes = specs(step_dir.shape)
    steps, nx, ny, nz = step_dir.shape
    x_face, y_face = face_specs[0], face_specs[2]
    shape = jax.ShapeDtypeStruct(step_dir.shape, jnp.float32)
    if final:
        out_spec = pl.BlockSpec((nx, ny, steps, nz), lambda s: (0, 0, 0, 0))
        out_shape = jax.ShapeDtypeStruct((nx, ny, steps, nz), jnp.float32)
    else:
        out_spec, out_shape = full, shape
    size = step_dir.size
    outs = pl.pallas_call(
        functools.partial(sweep_kernel, final),
        grid=(steps,),
        in_specs=[pl.BlockSpec(memory_space=pltpu.SMEM), full, full, full] + [fixed] * 8 + [x_face, x_face, y_face, y_face, face_specs[4], face_specs[4]],
        out_specs=[full, full, out_spec] + face_specs,
        out_shape=[shape, shape, out_shape] + face_shapes,
        cost_estimate=pl.CostEstimate(flops=30 * size, transcendentals=0, bytes_accessed=4 * 7 * size + 4 * 7 * size // steps),
        name="chebyshev_sweep",
    )(jnp.array([first, second], jnp.float32), step_dir, residual, potential, *faces, diagonal, inverse, *halos)
    return outs[0], outs[1], outs[2], outs[3:]


def local(
    heart_state,
    cell_type,
    gate_half,
    gate_slope,
    gate_tau,
    conduct,
    reversal,
    block_device,
    block_row,
    tissue,
    tissue_sigma,
):
    voltage = heart_state[0]
    gate_state = heart_state[1:]
    heart_x, heart_y, row_len = voltage.shape
    blocks = heart_x * heart_y
    devices = lax.axis_size("gx") * lax.axis_size("gy") * lax.axis_size("gz")
    capacity = 3 * blocks // devices
    slots = devices * capacity
    torso_x, torso_y, torso_z = tissue.shape
    torso_rows = torso_x * torso_y

    dest_dev = block_device.reshape(blocks)
    dest_row = block_row.reshape(blocks)
    one_hot = (dest_dev[:, None] == jnp.arange(devices, dtype=jnp.int32)[None, :]).astype(jnp.int32)
    running = jnp.cumsum(one_hot, axis=0) - 1
    slot_rank = jnp.sum(running * one_hot, axis=1)
    slot_index = dest_dev * capacity + slot_rank
    slot_match = slot_index[None, :] == jnp.arange(slots, dtype=jnp.int32)[:, None]
    slot_used = jnp.any(slot_match, axis=1)
    slot_block = jnp.argmax(slot_match, axis=1).astype(jnp.int32)
    send_rows = jnp.where(slot_used, dest_row[slot_block], torso_rows)
    recv_rows = lax.all_to_all(
        send_rows.reshape(devices, capacity), ("gx", "gy", "gz"), 0, 0, tiled=True
    ).reshape(slots)
    row_match = recv_rows[None, :] == jnp.arange(torso_rows, dtype=jnp.int32)[:, None]
    row_used = jnp.any(row_match, axis=1)
    row_slot = jnp.argmax(row_match, axis=1).astype(jnp.int32)

    sigma = []
    for dim_index in range(3):
        value = jnp.zeros(tissue.shape, jnp.float32)
        for tissue_kind in range(tissue_sigma.shape[0]):
            value = value + jnp.where(tissue == tissue_kind, tissue_sigma[tissue_kind, dim_index], 0.0)
        sigma.append(value)
    riders = [faces_of(sigma[dim_index], dim_index) for dim_index in range(3)]

    currents = []
    for time_step in range(STEPS):
        gate_state, ion_current = membrane(
            voltage, gate_state, cell_type, gate_half, gate_slope, gate_tau, conduct, reversal
        )
        laplace, carried = heart_laplace(voltage, riders if time_step == 0 else None)
        if time_step == 0:
            sigma_halos = [item[0] for item in carried]
        current = SIGMA_HEART * laplace
        currents.append(current)
        voltage = voltage + DT_HEART * (current - ion_current)
    heart_next = jnp.concatenate([voltage[None], gate_state], axis=0)

    payload = jnp.stack([item.reshape(blocks, row_len) for item in currents], axis=0)
    send_values = jnp.where(slot_used[None, :, None], jnp.take(payload, slot_block, axis=1), 0.0)
    received = lax.all_to_all(
        send_values.reshape(STEPS, devices, capacity, row_len),
        ("gx", "gy", "gz"),
        1,
        1,
        tiled=True,
    ).reshape(STEPS, slots, row_len)
    source = jnp.where(row_used[None, :, None], jnp.take(received, row_slot, axis=1), 0.0)
    source = source.reshape(STEPS, torso_x, torso_y, torso_z)

    faces = []
    for dim_index in range(3):
        low, high = sigma_halos[dim_index]
        minus, plus = shifted(sigma[dim_index], low, high, dim_index)
        faces.append(0.5 * (sigma[dim_index] + plus))
        faces.append(0.5 * (sigma[dim_index] + minus))
    diagonal = SCREEN + faces[0] + faces[1] + faces[2] + faces[3] + faces[4] + faces[5]

    spectrum_mid, first_coef, second_coef = chebyshev_weights(SWEEPS)
    residual = source
    inverse = 1.0 / diagonal
    step_dir, dir_faces = run_initial(spectrum_mid, residual, inverse)
    potential = step_dir
    for sweep in range(1, SWEEPS):
        x_low, x_high = exchange(dir_faces[1], dir_faces[0], "gx")
        y_low, y_high = exchange(dir_faces[3], dir_faces[2], "gy")
        z_low, z_high = exchange(dir_faces[5], dir_faces[4], "gz")
        halos = (x_low, x_high, y_low, y_high, z_low, z_high)
        residual, step_dir, potential, dir_faces = run_sweep(
            first_coef[sweep - 1], second_coef[sweep - 1], step_dir, residual, potential, faces, diagonal, inverse, halos,
            final=sweep == SWEEPS - 1,
        )
    return (heart_next, potential)


def solution(mesh):
    in_specs = (
        P(None, "gx", "gy", "gz"),
        P("gx", "gy", "gz"),
        P(),
        P(),
        P(),
        P(),
        P(),
        P("gx", "gy", "gz"),
        P("gx", "gy", "gz"),
        P("gx", "gy", "gz"),
        P(),
    )
    out_specs = (P(None, "gx", "gy", "gz"), P("gx", "gy", None, "gz"))
    return jax.shard_map(local, mesh=mesh, in_specs=in_specs, out_specs=out_specs, check_vma=False)
```

```python
import jax
import jax.numpy as jnp
from jax import lax
from jax.sharding import PartitionSpec as P
from jax.experimental import pallas as pl
from jax.experimental.pallas import tpu as pltpu
import functools

STEPS = 4
SWEEPS = 4


DT_HEART = 0.05
SIGMA_HEART = 1.0
SCREEN = 0.05
LOW_EDGE = 0.1
HIGH_EDGE = 1.9


def chebyshev_weights(sweep_count):
    spectrum_mid = 0.5 * (HIGH_EDGE + LOW_EDGE)
    half_width = 0.5 * (HIGH_EDGE - LOW_EDGE)
    half_ratio = spectrum_mid / half_width
    rho_old = 1.0 / half_ratio
    first_coef = []
    second_coef = []
    for sweep in range(1, sweep_count):
        rho_new = 1.0 / (2.0 * half_ratio - rho_old)
        first_coef.append(rho_new * rho_old)
        second_coef.append(2.0 * rho_new / half_width)
        rho_old = rho_new
    return (spectrum_mid, first_coef, second_coef)


def face_halos(block, axis, dim):
    top = lax.index_in_dim(block, block.shape[dim] - 1, axis=dim, keepdims=False)
    bottom = lax.index_in_dim(block, 0, axis=dim, keepdims=False)
    return exchange(top, bottom, axis)


def shifted(block, low, high, dim):
    n = block.shape[dim]
    low = jnp.expand_dims(low, dim)
    high = jnp.expand_dims(high, dim)
    minus = jnp.concatenate([low, lax.slice_in_dim(block, 0, n - 1, axis=dim)], axis=dim)
    plus = jnp.concatenate([lax.slice_in_dim(block, 1, n, axis=dim), high], axis=dim)
    return minus, plus


def membrane(voltage, gate_state, cell_type, gate_half, gate_slope, gate_tau, conduct, reversal):
    gate_count = gate_half.shape[0]
    lead_shape = (-1,) + (1,) * voltage.ndim
    gate_sign = jnp.where(jnp.arange(gate_count) % 2 == 0, 1.0, -1.0).astype(jnp.float32)
    exponent = (gate_sign / gate_slope).reshape(lead_shape) * (
        voltage[None] - gate_half.reshape(lead_shape)
    )
    steady = jax.nn.sigmoid(exponent)
    time_const = gate_tau.reshape(lead_shape) * (0.5 + steady)
    gate_state = steady + (gate_state - steady) * jnp.exp(-DT_HEART / time_const)
    weight = jnp.zeros(gate_state[0::2].shape, jnp.float32)
    for cell_kind in range(conduct.shape[0]):
        weight = weight + jnp.where(
            cell_type[None] == cell_kind, conduct[cell_kind].reshape(lead_shape), 0.0
        )
    ion_current = jnp.sum(
        weight
        * gate_state[0::2]
        * gate_state[1::2]
        * (voltage[None] - reversal.reshape(lead_shape)),
        axis=0,
    )
    return (gate_state, ion_current)


def faces_of(block, dim):
    top = lax.index_in_dim(block, block.shape[dim] - 1, axis=dim, keepdims=False)
    bottom = lax.index_in_dim(block, 0, axis=dim, keepdims=False)
    return top, bottom


def heart_laplace(voltage, riders=None):
    parts = []
    carried = []
    for index, (axis, dim) in enumerate((("gx", 0), ("gy", 1), ("gz", 2))):
        pairs = [faces_of(voltage, dim)]
        if riders is not None:
            pairs.append(riders[index])
        got = exchange_group(pairs, axis)
        minus, plus = shifted(voltage, got[0][0], got[0][1], dim)
        parts.append((plus, minus))
        carried.append(got[1:])
    total = parts[0][0] + parts[0][1]
    total = total + parts[1][0] + parts[1][1]
    total = total + parts[2][0] + parts[2][1]
    return total - 6.0 * voltage, carried


def exchange(top, bottom, axis):
    count = lax.axis_size(axis)
    if count == 2:
        index = lax.axis_index(axis)
        got = lax.ppermute(jnp.where(index == 0, top, bottom), axis, [(0, 1), (1, 0)])
        zero = jnp.zeros_like(got)
        return jnp.where(index == 1, got, zero), jnp.where(index == 0, got, zero)
    forward = [(i, i + 1) for i in range(count - 1)]
    backward = [(i + 1, i) for i in range(count - 1)]
    return lax.ppermute(top, axis, forward), lax.ppermute(bottom, axis, backward)


def exchange_group(pairs, axis):
    if len(pairs) == 1:
        return [exchange(pairs[0][0], pairs[0][1], axis)]
    top = jnp.concatenate([item.reshape(-1) for item, _ in pairs])
    bottom = jnp.concatenate([item.reshape(-1) for _, item in pairs])
    low, high = exchange(top, bottom, axis)
    result = []
    offset = 0
    for item, _ in pairs:
        size = item.size
        result.append((low[offset:offset + size].reshape(item.shape), high[offset:offset + size].reshape(item.shape)))
        offset += size
    return result


def write_faces(x, value, columns, xf_lo, xf_hi, yf_lo, yf_hi, zf_lo, zf_hi):
    nx = yf_lo.shape[1]
    ny, nz = value.shape
    half = nz // 2
    lane = lax.broadcasted_iota(jnp.int32, (ny, nz), 1)

    @pl.when(x == 0)
    def _():
        xf_lo[0] = value

    @pl.when(x == nx - 1)
    def _():
        xf_hi[0] = value

    yf_lo[0, x] = value[0:1, :]
    yf_hi[0, x] = value[ny - 1:ny, :]
    columns = jnp.where(lane == x, jnp.broadcast_to(value[:, 0:1], (ny, nz)), columns)
    columns = jnp.where(lane == half + x, jnp.broadcast_to(value[:, nz - 1:nz], (ny, nz)), columns)
    return columns


def finish_faces(columns, xf_lo, xf_hi, yf_lo, yf_hi, zf_lo, zf_hi):
    nx = yf_lo.shape[1]
    half = columns.shape[1] // 2
    flipped = columns.T
    zf_lo[0] = flipped[0:nx, :]
    zf_hi[0] = flipped[half:half + nx, :]


def sweep_kernel(final, coef_ref, d_ref, r_ref, p_ref, fxp, fxm, fyp, fym, fzp, fzm, dg_ref, inv_ref,
                 xlo, xhi, ylo, yhi, zlo, zhi, r_out, d_out, p_out, *face_out):
    snapshot = pl.program_id(0)
    first = coef_ref[0]
    second = coef_ref[1]
    nx, ny, nz = d_ref.shape[1], d_ref.shape[2], d_ref.shape[3]
    row = lax.broadcasted_iota(jnp.int32, (ny, nz), 0)
    lane = lax.broadcasted_iota(jnp.int32, (ny, nz), 1)
    blank = jnp.zeros((nz - nx, ny), jnp.float32)
    low_cols = jnp.concatenate([zlo[0], blank], axis=0).T
    high_rows = zhi[0]
    high_cols = jnp.concatenate([high_rows[1:nx], blank, high_rows[0:1]], axis=0).T

    def body(x, carry):
        centre = d_ref[0, x]
        below = d_ref[0, jnp.maximum(x - 1, 0)]
        above = d_ref[0, jnp.minimum(x + 1, nx - 1)]
        x_minus = jnp.where(x == 0, xlo[0], below)
        x_plus = jnp.where(x == nx - 1, xhi[0], above)
        y_minus = jnp.where(row == 0, ylo[0, x], pltpu.roll(centre, 1, 0))
        y_plus = jnp.where(row == ny - 1, yhi[0, x], pltpu.roll(centre, ny - 1, 0))
        turn = lax.rem(nz - x, nz)
        z_minus = jnp.where(lane == 0, pltpu.roll(low_cols, turn, 1), pltpu.roll(centre, 1, 1))
        z_plus = jnp.where(lane == nz - 1, pltpu.roll(high_cols, turn, 1), pltpu.roll(centre, nz - 1, 1))
        beside = fxp[x] * x_plus + fxm[x] * x_minus
        beside = beside + fyp[x] * y_plus + fym[x] * y_minus
        beside = beside + fzp[x] * z_plus + fzm[x] * z_minus
        diag = dg_ref[x]
        residual = r_ref[0, x] - (diag * centre - beside)
        step_dir = first * centre + second * (residual * inv_ref[x])
        r_out[0, x] = residual
        d_out[0, x] = step_dir
        if final:
            p_out[x, :, snapshot, :] = p_ref[0, x] + step_dir
        else:
            p_out[0, x] = p_ref[0, x] + step_dir
        return write_faces(x, step_dir, carry, *face_out)

    columns = lax.fori_loop(0, nx, body, jnp.zeros((ny, nz), jnp.float32), unroll=8)
    finish_faces(columns, *face_out)


def initial_kernel(mid, r_ref, inv_ref, d_out, *face_out):
    nx, ny, nz = r_ref.shape[1], r_ref.shape[2], r_ref.shape[3]

    def body(x, carry):
        step_dir = r_ref[0, x] * inv_ref[x] * (1.0 / mid)
        d_out[0, x] = step_dir
        return write_faces(x, step_dir, carry, *face_out)

    columns = lax.fori_loop(0, nx, body, jnp.zeros((ny, nz), jnp.float32), unroll=4)
    finish_faces(columns, *face_out)


def specs(shape):
    steps, nx, ny, nz = shape
    full = pl.BlockSpec((1, nx, ny, nz), lambda s: (s, 0, 0, 0))
    fixed = pl.BlockSpec((nx, ny, nz), lambda s: (0, 0, 0))
    x_face = pl.BlockSpec((1, ny, nz), lambda s: (s, 0, 0))
    y_face = pl.BlockSpec((1, nx, 1, nz), lambda s: (s, 0, 0, 0))
    z_face = pl.BlockSpec((1, nx, ny), lambda s: (s, 0, 0))
    face_specs = [x_face, x_face, y_face, y_face, z_face, z_face]
    face_shapes = [
        jax.ShapeDtypeStruct((steps, ny, nz), jnp.float32),
        jax.ShapeDtypeStruct((steps, ny, nz), jnp.float32),
        jax.ShapeDtypeStruct((steps, nx, 1, nz), jnp.float32),
        jax.ShapeDtypeStruct((steps, nx, 1, nz), jnp.float32),
        jax.ShapeDtypeStruct((steps, nx, ny), jnp.float32),
        jax.ShapeDtypeStruct((steps, nx, ny), jnp.float32),
    ]
    return full, fixed, face_specs, face_shapes


def run_initial(mid, source, inverse):
    full, fixed, face_specs, face_shapes = specs(source.shape)
    shape = jax.ShapeDtypeStruct(source.shape, jnp.float32)
    size = source.size
    outs = pl.pallas_call(
        functools.partial(initial_kernel, mid),
        grid=(source.shape[0],),
        in_specs=[full, fixed],
        out_specs=[full] + face_specs,
        out_shape=[shape] + face_shapes,
        cost_estimate=pl.CostEstimate(flops=2 * size, transcendentals=0, bytes_accessed=8 * size + 4 * size // source.shape[0]),
        name="chebyshev_start",
    )(source, inverse)
    return outs[0], outs[1:]


def run_sweep(first, second, step_dir, residual, potential, faces, diagonal, inverse, halos, final=False):
    full, fixed, face_specs, face_shapes = specs(step_dir.shape)
    steps, nx, ny, nz = step_dir.shape
    x_face, y_face = face_specs[0], face_specs[2]
    shape = jax.ShapeDtypeStruct(step_dir.shape, jnp.float32)
    if final:
        out_spec = pl.BlockSpec((nx, ny, steps, nz), lambda s: (0, 0, 0, 0))
        out_shape = jax.ShapeDtypeStruct((nx, ny, steps, nz), jnp.float32)
    else:
        out_spec, out_shape = full, shape
    size = step_dir.size
    outs = pl.pallas_call(
        functools.partial(sweep_kernel, final),
        grid=(steps,),
        in_specs=[pl.BlockSpec(memory_space=pltpu.SMEM), full, full, full] + [fixed] * 8 + [x_face, x_face, y_face, y_face, face_specs[4], face_specs[4]],
        out_specs=[full, full, out_spec] + face_specs,
        out_shape=[shape, shape, out_shape] + face_shapes,
        cost_estimate=pl.CostEstimate(flops=30 * size, transcendentals=0, bytes_accessed=4 * 7 * size + 4 * 7 * size // steps),
        name="chebyshev_sweep",
    )(jnp.array([first, second], jnp.float32), step_dir, residual, potential, *faces, diagonal, inverse, *halos)
    return outs[0], outs[1], outs[2], outs[3:]


def local(
    heart_state,
    cell_type,
    gate_half,
    gate_slope,
    gate_tau,
    conduct,
    reversal,
    block_device,
    block_row,
    tissue,
    tissue_sigma,
):
    voltage = heart_state[0]
    gate_state = heart_state[1:]
    heart_x, heart_y, row_len = voltage.shape
    blocks = heart_x * heart_y
    devices = lax.axis_size("gx") * lax.axis_size("gy") * lax.axis_size("gz")
    capacity = 3 * blocks // devices
    slots = devices * capacity
    torso_x, torso_y, torso_z = tissue.shape
    torso_rows = torso_x * torso_y

    dest_dev = block_device.reshape(blocks)
    dest_row = block_row.reshape(blocks)
    one_hot = (dest_dev[:, None] == jnp.arange(devices, dtype=jnp.int32)[None, :]).astype(jnp.int32)
    running = jnp.cumsum(one_hot, axis=0) - 1
    slot_rank = jnp.sum(running * one_hot, axis=1)
    slot_index = dest_dev * capacity + slot_rank
    slot_match = slot_index[None, :] == jnp.arange(slots, dtype=jnp.int32)[:, None]
    slot_used = jnp.any(slot_match, axis=1)
    slot_block = jnp.argmax(slot_match, axis=1).astype(jnp.int32)
    send_rows = jnp.where(slot_used, dest_row[slot_block], torso_rows)
    recv_rows = lax.all_to_all(
        send_rows.reshape(devices, capacity), ("gx", "gy", "gz"), 0, 0, tiled=True
    ).reshape(slots)
    row_match = recv_rows[None, :] == jnp.arange(torso_rows, dtype=jnp.int32)[:, None]
    row_used = jnp.any(row_match, axis=1)
    row_slot = jnp.argmax(row_match, axis=1).astype(jnp.int32)

    sigma = []
    for dim_index in range(3):
        value = jnp.zeros(tissue.shape, jnp.float32)
        for tissue_kind in range(tissue_sigma.shape[0]):
            value = value + jnp.where(tissue == tissue_kind, tissue_sigma[tissue_kind, dim_index], 0.0)
        sigma.append(value)
    riders = [faces_of(sigma[dim_index], dim_index) for dim_index in range(3)]

    currents = []
    for time_step in range(STEPS):
        gate_state, ion_current = membrane(
            voltage, gate_state, cell_type, gate_half, gate_slope, gate_tau, conduct, reversal
        )
        laplace, carried = heart_laplace(voltage, riders if time_step == 0 else None)
        if time_step == 0:
            sigma_halos = [item[0] for item in carried]
        current = SIGMA_HEART * laplace
        currents.append(current)
        voltage = voltage + DT_HEART * (current - ion_current)
    heart_next = jnp.concatenate([voltage[None], gate_state], axis=0)

    payload = jnp.stack([item.reshape(blocks, row_len) for item in currents], axis=0)
    send_values = jnp.where(slot_used[None, :, None], jnp.take(payload, slot_block, axis=1), 0.0)
    received = lax.all_to_all(
        send_values.reshape(STEPS, devices, capacity, row_len),
        ("gx", "gy", "gz"),
        1,
        1,
        tiled=True,
    ).reshape(STEPS, slots, row_len)
    source = jnp.where(row_used[None, :, None], jnp.take(received, row_slot, axis=1), 0.0)
    source = source.reshape(STEPS, torso_x, torso_y, torso_z)

    faces = []
    for dim_index in range(3):
        low, high = sigma_halos[dim_index]
        minus, plus = shifted(sigma[dim_index], low, high, dim_index)
        faces.append(0.5 * (sigma[dim_index] + plus))
        faces.append(0.5 * (sigma[dim_index] + minus))
    diagonal = SCREEN + faces[0] + faces[1] + faces[2] + faces[3] + faces[4] + faces[5]

    spectrum_mid, first_coef, second_coef = chebyshev_weights(SWEEPS)
    residual = source
    inverse = 1.0 / diagonal
    step_dir, dir_faces = run_initial(spectrum_mid, residual, inverse)
    potential = step_dir
    for sweep in range(1, SWEEPS):
        x_low, x_high = exchange(dir_faces[1], dir_faces[0], "gx")
        y_low, y_high = exchange(dir_faces[3], dir_faces[2], "gy")
        z_low, z_high = exchange(dir_faces[5], dir_faces[4], "gz")
        halos = (x_low, x_high, y_low, y_high, z_low, z_high)
        residual, step_dir, potential, dir_faces = run_sweep(
            first_coef[sweep - 1], second_coef[sweep - 1], step_dir, residual, potential, faces, diagonal, inverse, halos,
            final=sweep == SWEEPS - 1,
        )
    return (heart_next, potential)


def solution(mesh):
    in_specs = (
        P(None, "gx", "gy", "gz"),
        P("gx", "gy", "gz"),
        P(),
        P(),
        P(),
        P(),
        P(),
        P("gx", "gy", "gz"),
        P("gx", "gy", "gz"),
        P("gx", "gy", "gz"),
        P(),
    )
    out_specs = (P(None, "gx", "gy", "gz"), P("gx", "gy", None, "gz"))
    return jax.shard_map(local, mesh=mesh, in_specs=in_specs, out_specs=out_specs, check_vma=False)
```

```python
import jax
import jax.numpy as jnp
from jax import lax
from jax.sharding import PartitionSpec as P
from jax.experimental import pallas as pl
from jax.experimental.pallas import tpu as pltpu
import functools

STEPS = 4
SWEEPS = 4


DT_HEART = 0.05
SIGMA_HEART = 1.0
SCREEN = 0.05
LOW_EDGE = 0.1
HIGH_EDGE = 1.9


def chebyshev_weights(sweep_count):
    spectrum_mid = 0.5 * (HIGH_EDGE + LOW_EDGE)
    half_width = 0.5 * (HIGH_EDGE - LOW_EDGE)
    half_ratio = spectrum_mid / half_width
    rho_old = 1.0 / half_ratio
    first_coef = []
    second_coef = []
    for sweep in range(1, sweep_count):
        rho_new = 1.0 / (2.0 * half_ratio - rho_old)
        first_coef.append(rho_new * rho_old)
        second_coef.append(2.0 * rho_new / half_width)
        rho_old = rho_new
    return (spectrum_mid, first_coef, second_coef)


def face_halos(block, axis, dim):
    top = lax.index_in_dim(block, block.shape[dim] - 1, axis=dim, keepdims=False)
    bottom = lax.index_in_dim(block, 0, axis=dim, keepdims=False)
    return exchange(top, bottom, axis)


def shifted(block, low, high, dim):
    n = block.shape[dim]
    low = jnp.expand_dims(low, dim)
    high = jnp.expand_dims(high, dim)
    minus = jnp.concatenate([low, lax.slice_in_dim(block, 0, n - 1, axis=dim)], axis=dim)
    plus = jnp.concatenate([lax.slice_in_dim(block, 1, n, axis=dim), high], axis=dim)
    return minus, plus


def membrane(voltage, gate_state, cell_type, gate_half, gate_slope, gate_tau, conduct, reversal):
    gate_count = gate_half.shape[0]
    lead_shape = (-1,) + (1,) * voltage.ndim
    gate_sign = jnp.where(jnp.arange(gate_count) % 2 == 0, 1.0, -1.0).astype(jnp.float32)
    exponent = (gate_sign / gate_slope).reshape(lead_shape) * (
        voltage[None] - gate_half.reshape(lead_shape)
    )
    steady = jax.nn.sigmoid(exponent)
    time_const = gate_tau.reshape(lead_shape) * (0.5 + steady)
    gate_state = steady + (gate_state - steady) * jnp.exp(-DT_HEART / time_const)
    weight = jnp.zeros(gate_state[0::2].shape, jnp.float32)
    for cell_kind in range(conduct.shape[0]):
        weight = weight + jnp.where(
            cell_type[None] == cell_kind, conduct[cell_kind].reshape(lead_shape), 0.0
        )
    ion_current = jnp.sum(
        weight
        * gate_state[0::2]
        * gate_state[1::2]
        * (voltage[None] - reversal.reshape(lead_shape)),
        axis=0,
    )
    return (gate_state, ion_current)


def faces_of(block, dim):
    top = lax.index_in_dim(block, block.shape[dim] - 1, axis=dim, keepdims=False)
    bottom = lax.index_in_dim(block, 0, axis=dim, keepdims=False)
    return top, bottom


def heart_laplace(voltage, riders=None):
    parts = []
    carried = []
    for index, (axis, dim) in enumerate((("gx", 0), ("gy", 1), ("gz", 2))):
        pairs = [faces_of(voltage, dim)]
        if riders is not None:
            pairs.append(riders[index])
        got = exchange_group(pairs, axis)
        minus, plus = shifted(voltage, got[0][0], got[0][1], dim)
        parts.append((plus, minus))
        carried.append(got[1:])
    total = parts[0][0] + parts[0][1]
    total = total + parts[1][0] + parts[1][1]
    total = total + parts[2][0] + parts[2][1]
    return total - 6.0 * voltage, carried


def exchange(top, bottom, axis):
    count = lax.axis_size(axis)
    if count == 2:
        index = lax.axis_index(axis)
        got = lax.ppermute(jnp.where(index == 0, top, bottom), axis, [(0, 1), (1, 0)])
        zero = jnp.zeros_like(got)
        return jnp.where(index == 1, got, zero), jnp.where(index == 0, got, zero)
    forward = [(i, i + 1) for i in range(count - 1)]
    backward = [(i + 1, i) for i in range(count - 1)]
    return lax.ppermute(top, axis, forward), lax.ppermute(bottom, axis, backward)


def exchange_group(pairs, axis):
    if len(pairs) == 1:
        return [exchange(pairs[0][0], pairs[0][1], axis)]
    top = jnp.concatenate([item.reshape(-1) for item, _ in pairs])
    bottom = jnp.concatenate([item.reshape(-1) for _, item in pairs])
    low, high = exchange(top, bottom, axis)
    result = []
    offset = 0
    for item, _ in pairs:
        size = item.size
        result.append((low[offset:offset + size].reshape(item.shape), high[offset:offset + size].reshape(item.shape)))
        offset += size
    return result


def write_faces(x, value, columns, xf_lo, xf_hi, yf_lo, yf_hi, zf_lo, zf_hi):
    nx = yf_lo.shape[1]
    ny, nz = value.shape
    half = nz // 2
    lane = lax.broadcasted_iota(jnp.int32, (ny, nz), 1)

    @pl.when(x == 0)
    def _():
        xf_lo[0] = value

    @pl.when(x == nx - 1)
    def _():
        xf_hi[0] = value

    yf_lo[0, x] = value[0:1, :]
    yf_hi[0, x] = value[ny - 1:ny, :]
    columns = jnp.where(lane == x, pltpu.roll(value, x, 1), columns)
    columns = jnp.where(lane == half + x, pltpu.roll(value, lax.rem(half + x + 1, nz), 1), columns)
    return columns


def finish_faces(columns, xf_lo, xf_hi, yf_lo, yf_hi, zf_lo, zf_hi):
    nx = yf_lo.shape[1]
    half = columns.shape[1] // 2
    flipped = columns.T
    zf_lo[0] = flipped[0:nx, :]
    zf_hi[0] = flipped[half:half + nx, :]


def sweep_kernel(final, coef_ref, d_ref, r_ref, p_ref, fxp, fxm, fyp, fym, fzp, fzm, dg_ref, inv_ref,
                 xlo, xhi, ylo, yhi, zlo, zhi, r_out, d_out, p_out, *face_out):
    snapshot = pl.program_id(0)
    first = coef_ref[0]
    second = coef_ref[1]
    nx, ny, nz = d_ref.shape[1], d_ref.shape[2], d_ref.shape[3]
    row = lax.broadcasted_iota(jnp.int32, (ny, nz), 0)
    lane = lax.broadcasted_iota(jnp.int32, (ny, nz), 1)
    blank = jnp.zeros((nz - nx, ny), jnp.float32)
    low_cols = jnp.concatenate([zlo[0], blank], axis=0).T
    high_rows = zhi[0]
    high_cols = jnp.concatenate([high_rows[1:nx], blank, high_rows[0:1]], axis=0).T

    def body(x, carry):
        centre = d_ref[0, x]
        below = d_ref[0, jnp.maximum(x - 1, 0)]
        above = d_ref[0, jnp.minimum(x + 1, nx - 1)]
        x_minus = jnp.where(x == 0, xlo[0], below)
        x_plus = jnp.where(x == nx - 1, xhi[0], above)
        y_minus = jnp.where(row == 0, ylo[0, x], pltpu.roll(centre, 1, 0))
        y_plus = jnp.where(row == ny - 1, yhi[0, x], pltpu.roll(centre, ny - 1, 0))
        turn = lax.rem(nz - x, nz)
        z_minus = jnp.where(lane == 0, pltpu.roll(low_cols, turn, 1), pltpu.roll(centre, 1, 1))
        z_plus = jnp.where(lane == nz - 1, pltpu.roll(high_cols, turn, 1), pltpu.roll(centre, nz - 1, 1))
        beside = fxp[x] * x_plus + fxm[x] * x_minus
        beside = beside + fyp[x] * y_plus + fym[x] * y_minus
        beside = beside + fzp[x] * z_plus + fzm[x] * z_minus
        diag = dg_ref[x]
        residual = r_ref[0, x] - (diag * centre - beside)
        step_dir = first * centre + second * (residual * inv_ref[x])
        r_out[0, x] = residual
        d_out[0, x] = step_dir
        if final:
            p_out[x, :, snapshot, :] = p_ref[0, x] + step_dir
        else:
            p_out[0, x] = p_ref[0, x] + step_dir
        return write_faces(x, step_dir, carry, *face_out)

    columns = lax.fori_loop(0, nx, body, jnp.zeros((ny, nz), jnp.float32), unroll=8)
    finish_faces(columns, *face_out)


def initial_kernel(mid, r_ref, inv_ref, d_out, *face_out):
    nx, ny, nz = r_ref.shape[1], r_ref.shape[2], r_ref.shape[3]

    def body(x, carry):
        step_dir = r_ref[0, x] * inv_ref[x] * (1.0 / mid)
        d_out[0, x] = step_dir
        return write_faces(x, step_dir, carry, *face_out)

    columns = lax.fori_loop(0, nx, body, jnp.zeros((ny, nz), jnp.float32), unroll=4)
    finish_faces(columns, *face_out)


def specs(shape):
    steps, nx, ny, nz = shape
    full = pl.BlockSpec((1, nx, ny, nz), lambda s: (s, 0, 0, 0))
    fixed = pl.BlockSpec((nx, ny, nz), lambda s: (0, 0, 0))
    x_face = pl.BlockSpec((1, ny, nz), lambda s: (s, 0, 0))
    y_face = pl.BlockSpec((1, nx, 1, nz), lambda s: (s, 0, 0, 0))
    z_face = pl.BlockSpec((1, nx, ny), lambda s: (s, 0, 0))
    face_specs = [x_face, x_face, y_face, y_face, z_face, z_face]
    face_shapes = [
        jax.ShapeDtypeStruct((steps, ny, nz), jnp.float32),
        jax.ShapeDtypeStruct((steps, ny, nz), jnp.float32),
        jax.ShapeDtypeStruct((steps, nx, 1, nz), jnp.float32),
        jax.ShapeDtypeStruct((steps, nx, 1, nz), jnp.float32),
        jax.ShapeDtypeStruct((steps, nx, ny), jnp.float32),
        jax.ShapeDtypeStruct((steps, nx, ny), jnp.float32),
    ]
    return full, fixed, face_specs, face_shapes


def run_initial(mid, source, inverse):
    full, fixed, face_specs, face_shapes = specs(source.shape)
    shape = jax.ShapeDtypeStruct(source.shape, jnp.float32)
    size = source.size
    outs = pl.pallas_call(
        functools.partial(initial_kernel, mid),
        grid=(source.shape[0],),
        in_specs=[full, fixed],
        out_specs=[full] + face_specs,
        out_shape=[shape] + face_shapes,
        cost_estimate=pl.CostEstimate(flops=2 * size, transcendentals=0, bytes_accessed=8 * size + 4 * size // source.shape[0]),
        name="chebyshev_start",
    )(source, inverse)
    return outs[0], outs[1:]


def run_sweep(first, second, step_dir, residual, potential, faces, diagonal, inverse, halos, final=False):
    full, fixed, face_specs, face_shapes = specs(step_dir.shape)
    steps, nx, ny, nz = step_dir.shape
    x_face, y_face = face_specs[0], face_specs[2]
    shape = jax.ShapeDtypeStruct(step_dir.shape, jnp.float32)
    if final:
        out_spec = pl.BlockSpec((nx, ny, steps, nz), lambda s: (0, 0, 0, 0))
        out_shape = jax.ShapeDtypeStruct((nx, ny, steps, nz), jnp.float32)
    else:
        out_spec, out_shape = full, shape
    size = step_dir.size
    outs = pl.pallas_call(
        functools.partial(sweep_kernel, final),
        grid=(steps,),
        in_specs=[pl.BlockSpec(memory_space=pltpu.SMEM), full, full, full] + [fixed] * 8 + [x_face, x_face, y_face, y_face, face_specs[4], face_specs[4]],
        out_specs=[full, full, out_spec] + face_specs,
        out_shape=[shape, shape, out_shape] + face_shapes,
        cost_estimate=pl.CostEstimate(flops=30 * size, transcendentals=0, bytes_accessed=4 * 7 * size + 4 * 7 * size // steps),
        name="chebyshev_sweep",
    )(jnp.array([first, second], jnp.float32), step_dir, residual, potential, *faces, diagonal, inverse, *halos)
    return outs[0], outs[1], outs[2], outs[3:]


def local(
    heart_state,
    cell_type,
    gate_half,
    gate_slope,
    gate_tau,
    conduct,
    reversal,
    block_device,
    block_row,
    tissue,
    tissue_sigma,
):
    voltage = heart_state[0]
    gate_state = heart_state[1:]
    heart_x, heart_y, row_len = voltage.shape
    blocks = heart_x * heart_y
    devices = lax.axis_size("gx") * lax.axis_size("gy") * lax.axis_size("gz")
    capacity = 3 * blocks // devices
    slots = devices * capacity
    torso_x, torso_y, torso_z = tissue.shape
    torso_rows = torso_x * torso_y

    dest_dev = block_device.reshape(blocks)
    dest_row = block_row.reshape(blocks)
    one_hot = (dest_dev[:, None] == jnp.arange(devices, dtype=jnp.int32)[None, :]).astype(jnp.int32)
    running = jnp.cumsum(one_hot, axis=0) - 1
    slot_rank = jnp.sum(running * one_hot, axis=1)
    slot_index = dest_dev * capacity + slot_rank
    slot_match = slot_index[None, :] == jnp.arange(slots, dtype=jnp.int32)[:, None]
    slot_used = jnp.any(slot_match, axis=1)
    slot_block = jnp.argmax(slot_match, axis=1).astype(jnp.int32)
    send_rows = jnp.where(slot_used, dest_row[slot_block], torso_rows)
    recv_rows = lax.all_to_all(
        send_rows.reshape(devices, capacity), ("gx", "gy", "gz"), 0, 0, tiled=True
    ).reshape(slots)
    row_match = recv_rows[None, :] == jnp.arange(torso_rows, dtype=jnp.int32)[:, None]
    row_used = jnp.any(row_match, axis=1)
    row_slot = jnp.argmax(row_match, axis=1).astype(jnp.int32)

    sigma = []
    for dim_index in range(3):
        value = jnp.zeros(tissue.shape, jnp.float32)
        for tissue_kind in range(tissue_sigma.shape[0]):
            value = value + jnp.where(tissue == tissue_kind, tissue_sigma[tissue_kind, dim_index], 0.0)
        sigma.append(value)
    riders = [faces_of(sigma[dim_index], dim_index) for dim_index in range(3)]

    currents = []
    for time_step in range(STEPS):
        gate_state, ion_current = membrane(
            voltage, gate_state, cell_type, gate_half, gate_slope, gate_tau, conduct, reversal
        )
        laplace, carried = heart_laplace(voltage, riders if time_step == 0 else None)
        if time_step == 0:
            sigma_halos = [item[0] for item in carried]
        current = SIGMA_HEART * laplace
        currents.append(current)
        voltage = voltage + DT_HEART * (current - ion_current)
    heart_next = jnp.concatenate([voltage[None], gate_state], axis=0)

    payload = jnp.stack([item.reshape(blocks, row_len) for item in currents], axis=0)
    send_values = jnp.where(slot_used[None, :, None], jnp.take(payload, slot_block, axis=1), 0.0)
    received = lax.all_to_all(
        send_values.reshape(STEPS, devices, capacity, row_len),
        ("gx", "gy", "gz"),
        1,
        1,
        tiled=True,
    ).reshape(STEPS, slots, row_len)
    source = jnp.where(row_used[None, :, None], jnp.take(received, row_slot, axis=1), 0.0)
    source = source.reshape(STEPS, torso_x, torso_y, torso_z)

    faces = []
    for dim_index in range(3):
        low, high = sigma_halos[dim_index]
        minus, plus = shifted(sigma[dim_index], low, high, dim_index)
        faces.append(0.5 * (sigma[dim_index] + plus))
        faces.append(0.5 * (sigma[dim_index] + minus))
    diagonal = SCREEN + faces[0] + faces[1] + faces[2] + faces[3] + faces[4] + faces[5]

    spectrum_mid, first_coef, second_coef = chebyshev_weights(SWEEPS)
    residual = source
    inverse = 1.0 / diagonal
    step_dir, dir_faces = run_initial(spectrum_mid, residual, inverse)
    potential = step_dir
    for sweep in range(1, SWEEPS):
        x_low, x_high = exchange(dir_faces[1], dir_faces[0], "gx")
        y_low, y_high = exchange(dir_faces[3], dir_faces[2], "gy")
        z_low, z_high = exchange(dir_faces[5], dir_faces[4], "gz")
        halos = (x_low, x_high, y_low, y_high, z_low, z_high)
        residual, step_dir, potential, dir_faces = run_sweep(
            first_coef[sweep - 1], second_coef[sweep - 1], step_dir, residual, potential, faces, diagonal, inverse, halos,
            final=sweep == SWEEPS - 1,
        )
    return (heart_next, potential)


def solution(mesh):
    in_specs = (
        P(None, "gx", "gy", "gz"),
        P("gx", "gy", "gz"),
        P(),
        P(),
        P(),
        P(),
        P(),
        P("gx", "gy", "gz"),
        P("gx", "gy", "gz"),
        P("gx", "gy", "gz"),
        P(),
    )
    out_specs = (P(None, "gx", "gy", "gz"), P("gx", "gy", None, "gz"))
    return jax.shard_map(local, mesh=mesh, in_specs=in_specs, out_specs=out_specs, check_vma=False)
```

```python
import jax
import jax.numpy as jnp
from jax import lax
from jax.sharding import PartitionSpec as P
from jax.experimental import pallas as pl
from jax.experimental.pallas import tpu as pltpu
import functools

STEPS = 4
SWEEPS = 4


DT_HEART = 0.05
SIGMA_HEART = 1.0
SCREEN = 0.05
LOW_EDGE = 0.1
HIGH_EDGE = 1.9


def chebyshev_weights(sweep_count):
    spectrum_mid = 0.5 * (HIGH_EDGE + LOW_EDGE)
    half_width = 0.5 * (HIGH_EDGE - LOW_EDGE)
    half_ratio = spectrum_mid / half_width
    rho_old = 1.0 / half_ratio
    first_coef = []
    second_coef = []
    for sweep in range(1, sweep_count):
        rho_new = 1.0 / (2.0 * half_ratio - rho_old)
        first_coef.append(rho_new * rho_old)
        second_coef.append(2.0 * rho_new / half_width)
        rho_old = rho_new
    return (spectrum_mid, first_coef, second_coef)


def face_halos(block, axis, dim):
    top = lax.index_in_dim(block, block.shape[dim] - 1, axis=dim, keepdims=False)
    bottom = lax.index_in_dim(block, 0, axis=dim, keepdims=False)
    return exchange(top, bottom, axis)


def shifted(block, low, high, dim):
    n = block.shape[dim]
    low = jnp.expand_dims(low, dim)
    high = jnp.expand_dims(high, dim)
    minus = jnp.concatenate([low, lax.slice_in_dim(block, 0, n - 1, axis=dim)], axis=dim)
    plus = jnp.concatenate([lax.slice_in_dim(block, 1, n, axis=dim), high], axis=dim)
    return minus, plus


def membrane(voltage, gate_state, cell_type, gate_half, gate_slope, gate_tau, conduct, reversal):
    gate_count = gate_half.shape[0]
    lead_shape = (-1,) + (1,) * voltage.ndim
    gate_sign = jnp.where(jnp.arange(gate_count) % 2 == 0, 1.0, -1.0).astype(jnp.float32)
    exponent = (gate_sign / gate_slope).reshape(lead_shape) * (
        voltage[None] - gate_half.reshape(lead_shape)
    )
    steady = jax.nn.sigmoid(exponent)
    time_const = gate_tau.reshape(lead_shape) * (0.5 + steady)
    gate_state = steady + (gate_state - steady) * jnp.exp(-DT_HEART / time_const)
    weight = jnp.zeros(gate_state[0::2].shape, jnp.float32)
    for cell_kind in range(conduct.shape[0]):
        weight = weight + jnp.where(
            cell_type[None] == cell_kind, conduct[cell_kind].reshape(lead_shape), 0.0
        )
    ion_current = jnp.sum(
        weight
        * gate_state[0::2]
        * gate_state[1::2]
        * (voltage[None] - reversal.reshape(lead_shape)),
        axis=0,
    )
    return (gate_state, ion_current)


def faces_of(block, dim):
    top = lax.index_in_dim(block, block.shape[dim] - 1, axis=dim, keepdims=False)
    bottom = lax.index_in_dim(block, 0, axis=dim, keepdims=False)
    return top, bottom


def heart_laplace(voltage, riders=None):
    parts = []
    carried = []
    for index, (axis, dim) in enumerate((("gx", 0), ("gy", 1), ("gz", 2))):
        pairs = [faces_of(voltage, dim)]
        if riders is not None:
            pairs.append(riders[index])
        got = exchange_group(pairs, axis)
        minus, plus = shifted(voltage, got[0][0], got[0][1], dim)
        parts.append((plus, minus))
        carried.append(got[1:])
    total = parts[0][0] + parts[0][1]
    total = total + parts[1][0] + parts[1][1]
    total = total + parts[2][0] + parts[2][1]
    return total - 6.0 * voltage, carried


def exchange(top, bottom, axis):
    count = lax.axis_size(axis)
    if count == 2:
        index = lax.axis_index(axis)
        got = lax.ppermute(jnp.where(index == 0, top, bottom), axis, [(0, 1), (1, 0)])
        zero = jnp.zeros_like(got)
        return jnp.where(index == 1, got, zero), jnp.where(index == 0, got, zero)
    forward = [(i, i + 1) for i in range(count - 1)]
    backward = [(i + 1, i) for i in range(count - 1)]
    return lax.ppermute(top, axis, forward), lax.ppermute(bottom, axis, backward)


def exchange_group(pairs, axis):
    if len(pairs) == 1:
        return [exchange(pairs[0][0], pairs[0][1], axis)]
    top = jnp.concatenate([item.reshape(-1) for item, _ in pairs])
    bottom = jnp.concatenate([item.reshape(-1) for _, item in pairs])
    low, high = exchange(top, bottom, axis)
    result = []
    offset = 0
    for item, _ in pairs:
        size = item.size
        result.append((low[offset:offset + size].reshape(item.shape), high[offset:offset + size].reshape(item.shape)))
        offset += size
    return result


def write_faces(x, value, columns, xf_lo, xf_hi, yf_lo, yf_hi, zf_lo, zf_hi):
    nx = yf_lo.shape[1]
    ny, nz = value.shape
    half = nz // 2
    lane = lax.broadcasted_iota(jnp.int32, (ny, nz), 1)

    @pl.when(x == 0)
    def _():
        xf_lo[0] = value

    @pl.when(x == nx - 1)
    def _():
        xf_hi[0] = value

    yf_lo[0, x] = value[0:1, :]
    yf_hi[0, x] = value[ny - 1:ny, :]
    columns = jnp.where(lane == x, pltpu.roll(value, x, 1), columns)
    columns = jnp.where(lane == half + x, pltpu.roll(value, lax.rem(half + x + 1, nz), 1), columns)
    return columns


def finish_faces(columns, xf_lo, xf_hi, yf_lo, yf_hi, zf_lo, zf_hi):
    nx = yf_lo.shape[1]
    half = columns.shape[1] // 2
    flipped = columns.T
    zf_lo[0] = flipped[0:nx, :]
    zf_hi[0] = flipped[half:half + nx, :]


def sweep_kernel(final, coef_ref, d_ref, r_ref, p_ref, fxp, fxm, fyp, fym, fzp, fzm, dg_ref, inv_ref,
                 xlo, xhi, ylo, yhi, zlo, zhi, r_out, d_out, p_out, *face_out):
    snapshot = pl.program_id(0)
    first = coef_ref[0]
    second = coef_ref[1]
    nx, ny, nz = d_ref.shape[1], d_ref.shape[2], d_ref.shape[3]
    row = lax.broadcasted_iota(jnp.int32, (ny, nz), 0)
    lane = lax.broadcasted_iota(jnp.int32, (ny, nz), 1)
    blank = jnp.zeros((nz - nx, ny), jnp.float32)
    low_cols = jnp.concatenate([zlo[0], blank], axis=0).T
    high_rows = zhi[0]
    high_cols = jnp.concatenate([high_rows[1:nx], blank, high_rows[0:1]], axis=0).T

    def body(x, carry):
        centre = d_ref[0, x]
        below = d_ref[0, jnp.maximum(x - 1, 0)]
        above = d_ref[0, jnp.minimum(x + 1, nx - 1)]
        x_minus = jnp.where(x == 0, xlo[0], below)
        x_plus = jnp.where(x == nx - 1, xhi[0], above)
        y_minus = jnp.where(row == 0, ylo[0, x], pltpu.roll(centre, 1, 0))
        y_plus = jnp.where(row == ny - 1, yhi[0, x], pltpu.roll(centre, ny - 1, 0))
        turn = lax.rem(nz - x, nz)
        z_minus = jnp.where(lane == 0, pltpu.roll(low_cols, turn, 1), pltpu.roll(centre, 1, 1))
        z_plus = jnp.where(lane == nz - 1, pltpu.roll(high_cols, turn, 1), pltpu.roll(centre, nz - 1, 1))
        beside = fxp[x] * x_plus + fxm[x] * x_minus
        beside = beside + fyp[x] * y_plus + fym[x] * y_minus
        beside = beside + fzp[x] * z_plus + fzm[x] * z_minus
        diag = dg_ref[x]
        residual = r_ref[0, x] - (diag * centre - beside)
        step_dir = first * centre + second * (residual * inv_ref[x])
        r_out[0, x] = residual
        d_out[0, x] = step_dir
        if final:
            p_out[x, :, snapshot, :] = p_ref[0, x] + step_dir
        else:
            p_out[0, x] = p_ref[0, x] + step_dir
        return write_faces(x, step_dir, carry, *face_out)

    columns = lax.fori_loop(0, nx, body, jnp.zeros((ny, nz), jnp.float32), unroll=16)
    finish_faces(columns, *face_out)


def initial_kernel(mid, r_ref, inv_ref, d_out, *face_out):
    nx, ny, nz = r_ref.shape[1], r_ref.shape[2], r_ref.shape[3]

    def body(x, carry):
        step_dir = r_ref[0, x] * inv_ref[x] * (1.0 / mid)
        d_out[0, x] = step_dir
        return write_faces(x, step_dir, carry, *face_out)

    columns = lax.fori_loop(0, nx, body, jnp.zeros((ny, nz), jnp.float32), unroll=4)
    finish_faces(columns, *face_out)


def specs(shape):
    steps, nx, ny, nz = shape
    full = pl.BlockSpec((1, nx, ny, nz), lambda s: (s, 0, 0, 0))
    fixed = pl.BlockSpec((nx, ny, nz), lambda s: (0, 0, 0))
    x_face = pl.BlockSpec((1, ny, nz), lambda s: (s, 0, 0))
    y_face = pl.BlockSpec((1, nx, 1, nz), lambda s: (s, 0, 0, 0))
    z_face = pl.BlockSpec((1, nx, ny), lambda s: (s, 0, 0))
    face_specs = [x_face, x_face, y_face, y_face, z_face, z_face]
    face_shapes = [
        jax.ShapeDtypeStruct((steps, ny, nz), jnp.float32),
        jax.ShapeDtypeStruct((steps, ny, nz), jnp.float32),
        jax.ShapeDtypeStruct((steps, nx, 1, nz), jnp.float32),
        jax.ShapeDtypeStruct((steps, nx, 1, nz), jnp.float32),
        jax.ShapeDtypeStruct((steps, nx, ny), jnp.float32),
        jax.ShapeDtypeStruct((steps, nx, ny), jnp.float32),
    ]
    return full, fixed, face_specs, face_shapes


def run_initial(mid, source, inverse):
    full, fixed, face_specs, face_shapes = specs(source.shape)
    shape = jax.ShapeDtypeStruct(source.shape, jnp.float32)
    size = source.size
    outs = pl.pallas_call(
        functools.partial(initial_kernel, mid),
        grid=(source.shape[0],),
        in_specs=[full, fixed],
        out_specs=[full] + face_specs,
        out_shape=[shape] + face_shapes,
        cost_estimate=pl.CostEstimate(flops=2 * size, transcendentals=0, bytes_accessed=8 * size + 4 * size // source.shape[0]),
        name="chebyshev_start",
    )(source, inverse)
    return outs[0], outs[1:]


def run_sweep(first, second, step_dir, residual, potential, faces, diagonal, inverse, halos, final=False):
    full, fixed, face_specs, face_shapes = specs(step_dir.shape)
    steps, nx, ny, nz = step_dir.shape
    x_face, y_face = face_specs[0], face_specs[2]
    shape = jax.ShapeDtypeStruct(step_dir.shape, jnp.float32)
    if final:
        out_spec = pl.BlockSpec((nx, ny, steps, nz), lambda s: (0, 0, 0, 0))
        out_shape = jax.ShapeDtypeStruct((nx, ny, steps, nz), jnp.float32)
    else:
        out_spec, out_shape = full, shape
    size = step_dir.size
    outs = pl.pallas_call(
        functools.partial(sweep_kernel, final),
        grid=(steps,),
        in_specs=[pl.BlockSpec(memory_space=pltpu.SMEM), full, full, full] + [fixed] * 8 + [x_face, x_face, y_face, y_face, face_specs[4], face_specs[4]],
        out_specs=[full, full, out_spec] + face_specs,
        out_shape=[shape, shape, out_shape] + face_shapes,
        cost_estimate=pl.CostEstimate(flops=30 * size, transcendentals=0, bytes_accessed=4 * 7 * size + 4 * 7 * size // steps),
        name="chebyshev_sweep",
    )(jnp.array([first, second], jnp.float32), step_dir, residual, potential, *faces, diagonal, inverse, *halos)
    return outs[0], outs[1], outs[2], outs[3:]


def local(
    heart_state,
    cell_type,
    gate_half,
    gate_slope,
    gate_tau,
    conduct,
    reversal,
    block_device,
    block_row,
    tissue,
    tissue_sigma,
):
    voltage = heart_state[0]
    gate_state = heart_state[1:]
    heart_x, heart_y, row_len = voltage.shape
    blocks = heart_x * heart_y
    devices = lax.axis_size("gx") * lax.axis_size("gy") * lax.axis_size("gz")
    capacity = 3 * blocks // devices
    slots = devices * capacity
    torso_x, torso_y, torso_z = tissue.shape
    torso_rows = torso_x * torso_y

    dest_dev = block_device.reshape(blocks)
    dest_row = block_row.reshape(blocks)
    one_hot = (dest_dev[:, None] == jnp.arange(devices, dtype=jnp.int32)[None, :]).astype(jnp.int32)
    running = jnp.cumsum(one_hot, axis=0) - 1
    slot_rank = jnp.sum(running * one_hot, axis=1)
    slot_index = dest_dev * capacity + slot_rank
    slot_match = slot_index[None, :] == jnp.arange(slots, dtype=jnp.int32)[:, None]
    slot_used = jnp.any(slot_match, axis=1)
    slot_block = jnp.argmax(slot_match, axis=1).astype(jnp.int32)
    send_rows = jnp.where(slot_used, dest_row[slot_block], torso_rows)
    recv_rows = lax.all_to_all(
        send_rows.reshape(devices, capacity), ("gx", "gy", "gz"), 0, 0, tiled=True
    ).reshape(slots)
    row_match = recv_rows[None, :] == jnp.arange(torso_rows, dtype=jnp.int32)[:, None]
    row_used = jnp.any(row_match, axis=1)
    row_slot = jnp.argmax(row_match, axis=1).astype(jnp.int32)

    sigma = []
    for dim_index in range(3):
        value = jnp.zeros(tissue.shape, jnp.float32)
        for tissue_kind in range(tissue_sigma.shape[0]):
            value = value + jnp.where(tissue == tissue_kind, tissue_sigma[tissue_kind, dim_index], 0.0)
        sigma.append(value)
    riders = [faces_of(sigma[dim_index], dim_index) for dim_index in range(3)]

    currents = []
    for time_step in range(STEPS):
        gate_state, ion_current = membrane(
            voltage, gate_state, cell_type, gate_half, gate_slope, gate_tau, conduct, reversal
        )
        laplace, carried = heart_laplace(voltage, riders if time_step == 0 else None)
        if time_step == 0:
            sigma_halos = [item[0] for item in carried]
        current = SIGMA_HEART * laplace
        currents.append(current)
        voltage = voltage + DT_HEART * (current - ion_current)
    heart_next = jnp.concatenate([voltage[None], gate_state], axis=0)

    payload = jnp.stack([item.reshape(blocks, row_len) for item in currents], axis=0)
    send_values = jnp.where(slot_used[None, :, None], jnp.take(payload, slot_block, axis=1), 0.0)
    received = lax.all_to_all(
        send_values.reshape(STEPS, devices, capacity, row_len),
        ("gx", "gy", "gz"),
        1,
        1,
        tiled=True,
    ).reshape(STEPS, slots, row_len)
    source = jnp.where(row_used[None, :, None], jnp.take(received, row_slot, axis=1), 0.0)
    source = source.reshape(STEPS, torso_x, torso_y, torso_z)

    faces = []
    for dim_index in range(3):
        low, high = sigma_halos[dim_index]
        minus, plus = shifted(sigma[dim_index], low, high, dim_index)
        faces.append(0.5 * (sigma[dim_index] + plus))
        faces.append(0.5 * (sigma[dim_index] + minus))
    diagonal = SCREEN + faces[0] + faces[1] + faces[2] + faces[3] + faces[4] + faces[5]

    spectrum_mid, first_coef, second_coef = chebyshev_weights(SWEEPS)
    residual = source
    inverse = 1.0 / diagonal
    step_dir, dir_faces = run_initial(spectrum_mid, residual, inverse)
    potential = step_dir
    for sweep in range(1, SWEEPS):
        x_low, x_high = exchange(dir_faces[1], dir_faces[0], "gx")
        y_low, y_high = exchange(dir_faces[3], dir_faces[2], "gy")
        z_low, z_high = exchange(dir_faces[5], dir_faces[4], "gz")
        halos = (x_low, x_high, y_low, y_high, z_low, z_high)
        residual, step_dir, potential, dir_faces = run_sweep(
            first_coef[sweep - 1], second_coef[sweep - 1], step_dir, residual, potential, faces, diagonal, inverse, halos,
            final=sweep == SWEEPS - 1,
        )
    return (heart_next, potential)


def solution(mesh):
    in_specs = (
        P(None, "gx", "gy", "gz"),
        P("gx", "gy", "gz"),
        P(),
        P(),
        P(),
        P(),
        P(),
        P("gx", "gy", "gz"),
        P("gx", "gy", "gz"),
        P("gx", "gy", "gz"),
        P(),
    )
    out_specs = (P(None, "gx", "gy", "gz"), P("gx", "gy", None, "gz"))
    return jax.shard_map(local, mesh=mesh, in_specs=in_specs, out_specs=out_specs, check_vma=False)
```

```python
import jax
import jax.numpy as jnp
from jax import lax
from jax.sharding import PartitionSpec as P
from jax.experimental import pallas as pl
from jax.experimental.pallas import tpu as pltpu
import functools

STEPS = 4
SWEEPS = 4


DT_HEART = 0.05
SIGMA_HEART = 1.0
SCREEN = 0.05
LOW_EDGE = 0.1
HIGH_EDGE = 1.9


def chebyshev_weights(sweep_count):
    spectrum_mid = 0.5 * (HIGH_EDGE + LOW_EDGE)
    half_width = 0.5 * (HIGH_EDGE - LOW_EDGE)
    half_ratio = spectrum_mid / half_width
    rho_old = 1.0 / half_ratio
    first_coef = []
    second_coef = []
    for sweep in range(1, sweep_count):
        rho_new = 1.0 / (2.0 * half_ratio - rho_old)
        first_coef.append(rho_new * rho_old)
        second_coef.append(2.0 * rho_new / half_width)
        rho_old = rho_new
    return (spectrum_mid, first_coef, second_coef)


def face_halos(block, axis, dim):
    top = lax.index_in_dim(block, block.shape[dim] - 1, axis=dim, keepdims=False)
    bottom = lax.index_in_dim(block, 0, axis=dim, keepdims=False)
    return exchange(top, bottom, axis)


def shifted(block, low, high, dim):
    n = block.shape[dim]
    low = jnp.expand_dims(low, dim)
    high = jnp.expand_dims(high, dim)
    minus = jnp.concatenate([low, lax.slice_in_dim(block, 0, n - 1, axis=dim)], axis=dim)
    plus = jnp.concatenate([lax.slice_in_dim(block, 1, n, axis=dim), high], axis=dim)
    return minus, plus


def membrane(voltage, gate_state, cell_type, gate_half, gate_slope, gate_tau, conduct, reversal):
    gate_count = gate_half.shape[0]
    lead_shape = (-1,) + (1,) * voltage.ndim
    gate_sign = jnp.where(jnp.arange(gate_count) % 2 == 0, 1.0, -1.0).astype(jnp.float32)
    exponent = (gate_sign / gate_slope).reshape(lead_shape) * (
        voltage[None] - gate_half.reshape(lead_shape)
    )
    steady = jax.nn.sigmoid(exponent)
    time_const = gate_tau.reshape(lead_shape) * (0.5 + steady)
    gate_state = steady + (gate_state - steady) * jnp.exp(-DT_HEART / time_const)
    weight = jnp.zeros(gate_state[0::2].shape, jnp.float32)
    for cell_kind in range(conduct.shape[0]):
        weight = weight + jnp.where(
            cell_type[None] == cell_kind, conduct[cell_kind].reshape(lead_shape), 0.0
        )
    ion_current = jnp.sum(
        weight
        * gate_state[0::2]
        * gate_state[1::2]
        * (voltage[None] - reversal.reshape(lead_shape)),
        axis=0,
    )
    return (gate_state, ion_current)


def faces_of(block, dim):
    top = lax.index_in_dim(block, block.shape[dim] - 1, axis=dim, keepdims=False)
    bottom = lax.index_in_dim(block, 0, axis=dim, keepdims=False)
    return top, bottom


def heart_laplace(voltage, riders=None):
    parts = []
    carried = []
    for index, (axis, dim) in enumerate((("gx", 0), ("gy", 1), ("gz", 2))):
        pairs = [faces_of(voltage, dim)]
        if riders is not None:
            pairs.append(riders[index])
        got = exchange_group(pairs, axis)
        minus, plus = shifted(voltage, got[0][0], got[0][1], dim)
        parts.append((plus, minus))
        carried.append(got[1:])
    total = parts[0][0] + parts[0][1]
    total = total + parts[1][0] + parts[1][1]
    total = total + parts[2][0] + parts[2][1]
    return total - 6.0 * voltage, carried


def exchange(top, bottom, axis):
    count = lax.axis_size(axis)
    if count == 2:
        index = lax.axis_index(axis)
        got = lax.ppermute(jnp.where(index == 0, top, bottom), axis, [(0, 1), (1, 0)])
        zero = jnp.zeros_like(got)
        return jnp.where(index == 1, got, zero), jnp.where(index == 0, got, zero)
    forward = [(i, i + 1) for i in range(count - 1)]
    backward = [(i + 1, i) for i in range(count - 1)]
    return lax.ppermute(top, axis, forward), lax.ppermute(bottom, axis, backward)


def exchange_group(pairs, axis):
    if len(pairs) == 1:
        return [exchange(pairs[0][0], pairs[0][1], axis)]
    top = jnp.concatenate([item.reshape(-1) for item, _ in pairs])
    bottom = jnp.concatenate([item.reshape(-1) for _, item in pairs])
    low, high = exchange(top, bottom, axis)
    result = []
    offset = 0
    for item, _ in pairs:
        size = item.size
        result.append((low[offset:offset + size].reshape(item.shape), high[offset:offset + size].reshape(item.shape)))
        offset += size
    return result


def write_faces(x, value, columns, xf_lo, xf_hi, yf_lo, yf_hi, zf_lo, zf_hi):
    nx = yf_lo.shape[1]
    ny, nz = value.shape
    half = nz // 2
    lane = lax.broadcasted_iota(jnp.int32, (ny, nz), 1)

    @pl.when(x == 0)
    def _():
        xf_lo[0] = value

    @pl.when(x == nx - 1)
    def _():
        xf_hi[0] = value

    yf_lo[0, x] = value[0:1, :]
    yf_hi[0, x] = value[ny - 1:ny, :]
    columns = jnp.where(lane == x, pltpu.roll(value, x, 1), columns)
    columns = jnp.where(lane == half + x, pltpu.roll(value, lax.rem(half + x + 1, nz), 1), columns)
    return columns


def finish_faces(columns, xf_lo, xf_hi, yf_lo, yf_hi, zf_lo, zf_hi):
    nx = yf_lo.shape[1]
    half = columns.shape[1] // 2
    flipped = columns.T
    zf_lo[0] = flipped[0:nx, :]
    zf_hi[0] = flipped[half:half + nx, :]


def sweep_kernel(final, coef_ref, d_ref, r_ref, p_ref, fxp, fxm, fyp, fym, fzp, fzm, dg_ref, inv_ref,
                 xlo, xhi, ylo, yhi, zlo, zhi, r_out, d_out, p_out, *face_out):
    snapshot = pl.program_id(0)
    first = coef_ref[0]
    second = coef_ref[1]
    nx, ny, nz = d_ref.shape[1], d_ref.shape[2], d_ref.shape[3]
    row = lax.broadcasted_iota(jnp.int32, (ny, nz), 0)
    lane = lax.broadcasted_iota(jnp.int32, (ny, nz), 1)
    blank = jnp.zeros((nz - nx, ny), jnp.float32)
    low_cols = jnp.concatenate([zlo[0], blank], axis=0).T
    high_rows = zhi[0]
    high_cols = jnp.concatenate([high_rows[1:nx], blank, high_rows[0:1]], axis=0).T

    def body(x, carry):
        centre = d_ref[0, x]
        below = d_ref[0, jnp.maximum(x - 1, 0)]
        above = d_ref[0, jnp.minimum(x + 1, nx - 1)]
        x_minus = jnp.where(x == 0, xlo[0], below)
        x_plus = jnp.where(x == nx - 1, xhi[0], above)
        y_minus = jnp.where(row == 0, ylo[0, x], pltpu.roll(centre, 1, 0))
        y_plus = jnp.where(row == ny - 1, yhi[0, x], pltpu.roll(centre, ny - 1, 0))
        turn = lax.rem(nz - x, nz)
        z_minus = jnp.where(lane == 0, pltpu.roll(low_cols, turn, 1), pltpu.roll(centre, 1, 1))
        z_plus = jnp.where(lane == nz - 1, pltpu.roll(high_cols, turn, 1), pltpu.roll(centre, nz - 1, 1))
        beside = fxp[x] * x_plus + fxm[x] * x_minus
        beside = beside + fyp[x] * y_plus + fym[x] * y_minus
        beside = beside + fzp[x] * z_plus + fzm[x] * z_minus
        diag = dg_ref[x]
        residual = r_ref[0, x] - (diag * centre - beside)
        step_dir = first * centre + second * (residual * inv_ref[x])
        r_out[0, x] = residual
        d_out[0, x] = step_dir
        if final:
            p_out[x, :, snapshot, :] = p_ref[0, x] + step_dir
        else:
            p_out[0, x] = p_ref[0, x] + step_dir
        return write_faces(x, step_dir, carry, *face_out)

    columns = lax.fori_loop(0, nx, body, jnp.zeros((ny, nz), jnp.float32), unroll=32)
    finish_faces(columns, *face_out)


def initial_kernel(mid, r_ref, inv_ref, d_out, *face_out):
    nx, ny, nz = r_ref.shape[1], r_ref.shape[2], r_ref.shape[3]

    def body(x, carry):
        step_dir = r_ref[0, x] * inv_ref[x] * (1.0 / mid)
        d_out[0, x] = step_dir
        return write_faces(x, step_dir, carry, *face_out)

    columns = lax.fori_loop(0, nx, body, jnp.zeros((ny, nz), jnp.float32), unroll=4)
    finish_faces(columns, *face_out)


def specs(shape):
    steps, nx, ny, nz = shape
    full = pl.BlockSpec((1, nx, ny, nz), lambda s: (s, 0, 0, 0))
    fixed = pl.BlockSpec((nx, ny, nz), lambda s: (0, 0, 0))
    x_face = pl.BlockSpec((1, ny, nz), lambda s: (s, 0, 0))
    y_face = pl.BlockSpec((1, nx, 1, nz), lambda s: (s, 0, 0, 0))
    z_face = pl.BlockSpec((1, nx, ny), lambda s: (s, 0, 0))
    face_specs = [x_face, x_face, y_face, y_face, z_face, z_face]
    face_shapes = [
        jax.ShapeDtypeStruct((steps, ny, nz), jnp.float32),
        jax.ShapeDtypeStruct((steps, ny, nz), jnp.float32),
        jax.ShapeDtypeStruct((steps, nx, 1, nz), jnp.float32),
        jax.ShapeDtypeStruct((steps, nx, 1, nz), jnp.float32),
        jax.ShapeDtypeStruct((steps, nx, ny), jnp.float32),
        jax.ShapeDtypeStruct((steps, nx, ny), jnp.float32),
    ]
    return full, fixed, face_specs, face_shapes


def run_initial(mid, source, inverse):
    full, fixed, face_specs, face_shapes = specs(source.shape)
    shape = jax.ShapeDtypeStruct(source.shape, jnp.float32)
    size = source.size
    outs = pl.pallas_call(
        functools.partial(initial_kernel, mid),
        grid=(source.shape[0],),
        in_specs=[full, fixed],
        out_specs=[full] + face_specs,
        out_shape=[shape] + face_shapes,
        cost_estimate=pl.CostEstimate(flops=2 * size, transcendentals=0, bytes_accessed=8 * size + 4 * size // source.shape[0]),
        name="chebyshev_start",
    )(source, inverse)
    return outs[0], outs[1:]


def run_sweep(first, second, step_dir, residual, potential, faces, diagonal, inverse, halos, final=False):
    full, fixed, face_specs, face_shapes = specs(step_dir.shape)
    steps, nx, ny, nz = step_dir.shape
    x_face, y_face = face_specs[0], face_specs[2]
    shape = jax.ShapeDtypeStruct(step_dir.shape, jnp.float32)
    if final:
        out_spec = pl.BlockSpec((nx, ny, steps, nz), lambda s: (0, 0, 0, 0))
        out_shape = jax.ShapeDtypeStruct((nx, ny, steps, nz), jnp.float32)
    else:
        out_spec, out_shape = full, shape
    size = step_dir.size
    outs = pl.pallas_call(
        functools.partial(sweep_kernel, final),
        grid=(steps,),
        in_specs=[pl.BlockSpec(memory_space=pltpu.SMEM), full, full, full] + [fixed] * 8 + [x_face, x_face, y_face, y_face, face_specs[4], face_specs[4]],
        out_specs=[full, full, out_spec] + face_specs,
        out_shape=[shape, shape, out_shape] + face_shapes,
        cost_estimate=pl.CostEstimate(flops=30 * size, transcendentals=0, bytes_accessed=4 * 7 * size + 4 * 7 * size // steps),
        name="chebyshev_sweep",
    )(jnp.array([first, second], jnp.float32), step_dir, residual, potential, *faces, diagonal, inverse, *halos)
    return outs[0], outs[1], outs[2], outs[3:]


def local(
    heart_state,
    cell_type,
    gate_half,
    gate_slope,
    gate_tau,
    conduct,
    reversal,
    block_device,
    block_row,
    tissue,
    tissue_sigma,
):
    voltage = heart_state[0]
    gate_state = heart_state[1:]
    heart_x, heart_y, row_len = voltage.shape
    blocks = heart_x * heart_y
    devices = lax.axis_size("gx") * lax.axis_size("gy") * lax.axis_size("gz")
    capacity = 3 * blocks // devices
    slots = devices * capacity
    torso_x, torso_y, torso_z = tissue.shape
    torso_rows = torso_x * torso_y

    dest_dev = block_device.reshape(blocks)
    dest_row = block_row.reshape(blocks)
    one_hot = (dest_dev[:, None] == jnp.arange(devices, dtype=jnp.int32)[None, :]).astype(jnp.int32)
    running = jnp.cumsum(one_hot, axis=0) - 1
    slot_rank = jnp.sum(running * one_hot, axis=1)
    slot_index = dest_dev * capacity + slot_rank
    slot_match = slot_index[None, :] == jnp.arange(slots, dtype=jnp.int32)[:, None]
    slot_used = jnp.any(slot_match, axis=1)
    slot_block = jnp.argmax(slot_match, axis=1).astype(jnp.int32)
    send_rows = jnp.where(slot_used, dest_row[slot_block], torso_rows)
    recv_rows = lax.all_to_all(
        send_rows.reshape(devices, capacity), ("gx", "gy", "gz"), 0, 0, tiled=True
    ).reshape(slots)
    row_match = recv_rows[None, :] == jnp.arange(torso_rows, dtype=jnp.int32)[:, None]
    row_used = jnp.any(row_match, axis=1)
    row_slot = jnp.argmax(row_match, axis=1).astype(jnp.int32)

    sigma = []
    for dim_index in range(3):
        value = jnp.zeros(tissue.shape, jnp.float32)
        for tissue_kind in range(tissue_sigma.shape[0]):
            value = value + jnp.where(tissue == tissue_kind, tissue_sigma[tissue_kind, dim_index], 0.0)
        sigma.append(value)
    riders = [faces_of(sigma[dim_index], dim_index) for dim_index in range(3)]

    currents = []
    for time_step in range(STEPS):
        gate_state, ion_current = membrane(
            voltage, gate_state, cell_type, gate_half, gate_slope, gate_tau, conduct, reversal
        )
        laplace, carried = heart_laplace(voltage, riders if time_step == 0 else None)
        if time_step == 0:
            sigma_halos = [item[0] for item in carried]
        current = SIGMA_HEART * laplace
        currents.append(current)
        voltage = voltage + DT_HEART * (current - ion_current)
    heart_next = jnp.concatenate([voltage[None], gate_state], axis=0)

    payload = jnp.stack([item.reshape(blocks, row_len) for item in currents], axis=0)
    send_values = jnp.where(slot_used[None, :, None], jnp.take(payload, slot_block, axis=1), 0.0)
    received = lax.all_to_all(
        send_values.reshape(STEPS, devices, capacity, row_len),
        ("gx", "gy", "gz"),
        1,
        1,
        tiled=True,
    ).reshape(STEPS, slots, row_len)
    source = jnp.where(row_used[None, :, None], jnp.take(received, row_slot, axis=1), 0.0)
    source = source.reshape(STEPS, torso_x, torso_y, torso_z)

    faces = []
    for dim_index in range(3):
        low, high = sigma_halos[dim_index]
        minus, plus = shifted(sigma[dim_index], low, high, dim_index)
        faces.append(0.5 * (sigma[dim_index] + plus))
        faces.append(0.5 * (sigma[dim_index] + minus))
    diagonal = SCREEN + faces[0] + faces[1] + faces[2] + faces[3] + faces[4] + faces[5]

    spectrum_mid, first_coef, second_coef = chebyshev_weights(SWEEPS)
    residual = source
    inverse = 1.0 / diagonal
    step_dir, dir_faces = run_initial(spectrum_mid, residual, inverse)
    potential = step_dir
    for sweep in range(1, SWEEPS):
        x_low, x_high = exchange(dir_faces[1], dir_faces[0], "gx")
        y_low, y_high = exchange(dir_faces[3], dir_faces[2], "gy")
        z_low, z_high = exchange(dir_faces[5], dir_faces[4], "gz")
        halos = (x_low, x_high, y_low, y_high, z_low, z_high)
        residual, step_dir, potential, dir_faces = run_sweep(
            first_coef[sweep - 1], second_coef[sweep - 1], step_dir, residual, potential, faces, diagonal, inverse, halos,
            final=sweep == SWEEPS - 1,
        )
    return (heart_next, potential)


def solution(mesh):
    in_specs = (
        P(None, "gx", "gy", "gz"),
        P("gx", "gy", "gz"),
        P(),
        P(),
        P(),
        P(),
        P(),
        P("gx", "gy", "gz"),
        P("gx", "gy", "gz"),
        P("gx", "gy", "gz"),
        P(),
    )
    out_specs = (P(None, "gx", "gy", "gz"), P("gx", "gy", None, "gz"))
    return jax.shard_map(local, mesh=mesh, in_specs=in_specs, out_specs=out_specs, check_vma=False)
```

```python
import jax
import jax.numpy as jnp
from jax import lax
from jax.sharding import PartitionSpec as P
from jax.experimental import pallas as pl
from jax.experimental.pallas import tpu as pltpu
import functools

STEPS = 4
SWEEPS = 4


DT_HEART = 0.05
SIGMA_HEART = 1.0
SCREEN = 0.05
LOW_EDGE = 0.1
HIGH_EDGE = 1.9


def chebyshev_weights(sweep_count):
    spectrum_mid = 0.5 * (HIGH_EDGE + LOW_EDGE)
    half_width = 0.5 * (HIGH_EDGE - LOW_EDGE)
    half_ratio = spectrum_mid / half_width
    rho_old = 1.0 / half_ratio
    first_coef = []
    second_coef = []
    for sweep in range(1, sweep_count):
        rho_new = 1.0 / (2.0 * half_ratio - rho_old)
        first_coef.append(rho_new * rho_old)
        second_coef.append(2.0 * rho_new / half_width)
        rho_old = rho_new
    return (spectrum_mid, first_coef, second_coef)


def face_halos(block, axis, dim):
    top = lax.index_in_dim(block, block.shape[dim] - 1, axis=dim, keepdims=False)
    bottom = lax.index_in_dim(block, 0, axis=dim, keepdims=False)
    return exchange(top, bottom, axis)


def shifted(block, low, high, dim):
    n = block.shape[dim]
    low = jnp.expand_dims(low, dim)
    high = jnp.expand_dims(high, dim)
    minus = jnp.concatenate([low, lax.slice_in_dim(block, 0, n - 1, axis=dim)], axis=dim)
    plus = jnp.concatenate([lax.slice_in_dim(block, 1, n, axis=dim), high], axis=dim)
    return minus, plus


def membrane(voltage, gate_state, cell_type, gate_half, gate_slope, gate_tau, conduct, reversal):
    gate_count = gate_half.shape[0]
    lead_shape = (-1,) + (1,) * voltage.ndim
    gate_sign = jnp.where(jnp.arange(gate_count) % 2 == 0, 1.0, -1.0).astype(jnp.float32)
    exponent = (gate_sign / gate_slope).reshape(lead_shape) * (
        voltage[None] - gate_half.reshape(lead_shape)
    )
    steady = jax.nn.sigmoid(exponent)
    time_const = gate_tau.reshape(lead_shape) * (0.5 + steady)
    gate_state = steady + (gate_state - steady) * jnp.exp(-DT_HEART / time_const)
    weight = jnp.zeros(gate_state[0::2].shape, jnp.float32)
    for cell_kind in range(conduct.shape[0]):
        weight = weight + jnp.where(
            cell_type[None] == cell_kind, conduct[cell_kind].reshape(lead_shape), 0.0
        )
    ion_current = jnp.sum(
        weight
        * gate_state[0::2]
        * gate_state[1::2]
        * (voltage[None] - reversal.reshape(lead_shape)),
        axis=0,
    )
    return (gate_state, ion_current)


def faces_of(block, dim):
    top = lax.index_in_dim(block, block.shape[dim] - 1, axis=dim, keepdims=False)
    bottom = lax.index_in_dim(block, 0, axis=dim, keepdims=False)
    return top, bottom


def heart_laplace(voltage, riders=None):
    parts = []
    carried = []
    for index, (axis, dim) in enumerate((("gx", 0), ("gy", 1), ("gz", 2))):
        pairs = [faces_of(voltage, dim)]
        if riders is not None:
            pairs.append(riders[index])
        got = exchange_group(pairs, axis)
        minus, plus = shifted(voltage, got[0][0], got[0][1], dim)
        parts.append((plus, minus))
        carried.append(got[1:])
    total = parts[0][0] + parts[0][1]
    total = total + parts[1][0] + parts[1][1]
    total = total + parts[2][0] + parts[2][1]
    return total - 6.0 * voltage, carried


def exchange(top, bottom, axis):
    count = lax.axis_size(axis)
    if count == 2:
        index = lax.axis_index(axis)
        got = lax.ppermute(jnp.where(index == 0, top, bottom), axis, [(0, 1), (1, 0)])
        zero = jnp.zeros_like(got)
        return jnp.where(index == 1, got, zero), jnp.where(index == 0, got, zero)
    forward = [(i, i + 1) for i in range(count - 1)]
    backward = [(i + 1, i) for i in range(count - 1)]
    return lax.ppermute(top, axis, forward), lax.ppermute(bottom, axis, backward)


def exchange_group(pairs, axis):
    if len(pairs) == 1:
        return [exchange(pairs[0][0], pairs[0][1], axis)]
    top = jnp.concatenate([item.reshape(-1) for item, _ in pairs])
    bottom = jnp.concatenate([item.reshape(-1) for _, item in pairs])
    low, high = exchange(top, bottom, axis)
    result = []
    offset = 0
    for item, _ in pairs:
        size = item.size
        result.append((low[offset:offset + size].reshape(item.shape), high[offset:offset + size].reshape(item.shape)))
        offset += size
    return result


def write_faces(x, value, columns, xf_lo, xf_hi, yf_lo, yf_hi, zf_lo, zf_hi):
    nx = yf_lo.shape[1]
    ny, nz = value.shape
    half = nz // 2
    lane = lax.broadcasted_iota(jnp.int32, (ny, nz), 1)

    yf_lo[0, x] = value[0:1, :]
    yf_hi[0, x] = value[ny - 1:ny, :]
    columns = jnp.where(lane == x, pltpu.roll(value, x, 1), columns)
    columns = jnp.where(lane == half + x, pltpu.roll(value, lax.rem(half + x + 1, nz), 1), columns)
    return columns


def finish_faces(d_out, columns, xf_lo, xf_hi, yf_lo, yf_hi, zf_lo, zf_hi):
    nx = yf_lo.shape[1]
    xf_lo[0] = d_out[0, 0]
    xf_hi[0] = d_out[0, nx - 1]
    half = columns.shape[1] // 2
    flipped = columns.T
    zf_lo[0] = flipped[0:nx, :]
    zf_hi[0] = flipped[half:half + nx, :]


def sweep_kernel(final, coef_ref, d_ref, r_ref, p_ref, fxp, fxm, fyp, fym, fzp, fzm, dg_ref, inv_ref,
                 xlo, xhi, ylo, yhi, zlo, zhi, r_out, d_out, p_out, *face_out):
    snapshot = pl.program_id(0)
    first = coef_ref[0]
    second = coef_ref[1]
    nx, ny, nz = d_ref.shape[1], d_ref.shape[2], d_ref.shape[3]
    row = lax.broadcasted_iota(jnp.int32, (ny, nz), 0)
    lane = lax.broadcasted_iota(jnp.int32, (ny, nz), 1)
    blank = jnp.zeros((nz - nx, ny), jnp.float32)
    low_cols = jnp.concatenate([zlo[0], blank], axis=0).T
    high_rows = zhi[0]
    high_cols = jnp.concatenate([high_rows[1:nx], blank, high_rows[0:1]], axis=0).T

    def body(x, carry):
        centre = d_ref[0, x]
        below = d_ref[0, jnp.maximum(x - 1, 0)]
        above = d_ref[0, jnp.minimum(x + 1, nx - 1)]
        x_minus = jnp.where(x == 0, xlo[0], below)
        x_plus = jnp.where(x == nx - 1, xhi[0], above)
        y_minus = jnp.where(row == 0, ylo[0, x], pltpu.roll(centre, 1, 0))
        y_plus = jnp.where(row == ny - 1, yhi[0, x], pltpu.roll(centre, ny - 1, 0))
        turn = lax.rem(nz - x, nz)
        z_minus = jnp.where(lane == 0, pltpu.roll(low_cols, turn, 1), pltpu.roll(centre, 1, 1))
        z_plus = jnp.where(lane == nz - 1, pltpu.roll(high_cols, turn, 1), pltpu.roll(centre, nz - 1, 1))
        beside = fxp[x] * x_plus + fxm[x] * x_minus
        beside = beside + fyp[x] * y_plus + fym[x] * y_minus
        beside = beside + fzp[x] * z_plus + fzm[x] * z_minus
        diag = dg_ref[x]
        residual = r_ref[0, x] - (diag * centre - beside)
        step_dir = first * centre + second * (residual * inv_ref[x])
        r_out[0, x] = residual
        d_out[0, x] = step_dir
        if final:
            p_out[x, :, snapshot, :] = p_ref[0, x] + step_dir
        else:
            p_out[0, x] = p_ref[0, x] + step_dir
        return write_faces(x, step_dir, carry, *face_out)

    columns = lax.fori_loop(0, nx, body, jnp.zeros((ny, nz), jnp.float32), unroll=16)
    finish_faces(d_out, columns, *face_out)


def initial_kernel(mid, r_ref, inv_ref, d_out, *face_out):
    nx, ny, nz = r_ref.shape[1], r_ref.shape[2], r_ref.shape[3]

    def body(x, carry):
        step_dir = r_ref[0, x] * inv_ref[x] * (1.0 / mid)
        d_out[0, x] = step_dir
        return write_faces(x, step_dir, carry, *face_out)

    columns = lax.fori_loop(0, nx, body, jnp.zeros((ny, nz), jnp.float32), unroll=4)
    finish_faces(d_out, columns, *face_out)


def specs(shape):
    steps, nx, ny, nz = shape
    full = pl.BlockSpec((1, nx, ny, nz), lambda s: (s, 0, 0, 0))
    fixed = pl.BlockSpec((nx, ny, nz), lambda s: (0, 0, 0))
    x_face = pl.BlockSpec((1, ny, nz), lambda s: (s, 0, 0))
    y_face = pl.BlockSpec((1, nx, 1, nz), lambda s: (s, 0, 0, 0))
    z_face = pl.BlockSpec((1, nx, ny), lambda s: (s, 0, 0))
    face_specs = [x_face, x_face, y_face, y_face, z_face, z_face]
    face_shapes = [
        jax.ShapeDtypeStruct((steps, ny, nz), jnp.float32),
        jax.ShapeDtypeStruct((steps, ny, nz), jnp.float32),
        jax.ShapeDtypeStruct((steps, nx, 1, nz), jnp.float32),
        jax.ShapeDtypeStruct((steps, nx, 1, nz), jnp.float32),
        jax.ShapeDtypeStruct((steps, nx, ny), jnp.float32),
        jax.ShapeDtypeStruct((steps, nx, ny), jnp.float32),
    ]
    return full, fixed, face_specs, face_shapes


def run_initial(mid, source, inverse):
    full, fixed, face_specs, face_shapes = specs(source.shape)
    shape = jax.ShapeDtypeStruct(source.shape, jnp.float32)
    size = source.size
    outs = pl.pallas_call(
        functools.partial(initial_kernel, mid),
        grid=(source.shape[0],),
        in_specs=[full, fixed],
        out_specs=[full] + face_specs,
        out_shape=[shape] + face_shapes,
        cost_estimate=pl.CostEstimate(flops=2 * size, transcendentals=0, bytes_accessed=8 * size + 4 * size // source.shape[0]),
        name="chebyshev_start",
    )(source, inverse)
    return outs[0], outs[1:]


def run_sweep(first, second, step_dir, residual, potential, faces, diagonal, inverse, halos, final=False):
    full, fixed, face_specs, face_shapes = specs(step_dir.shape)
    steps, nx, ny, nz = step_dir.shape
    x_face, y_face = face_specs[0], face_specs[2]
    shape = jax.ShapeDtypeStruct(step_dir.shape, jnp.float32)
    if final:
        out_spec = pl.BlockSpec((nx, ny, steps, nz), lambda s: (0, 0, 0, 0))
        out_shape = jax.ShapeDtypeStruct((nx, ny, steps, nz), jnp.float32)
    else:
        out_spec, out_shape = full, shape
    size = step_dir.size
    outs = pl.pallas_call(
        functools.partial(sweep_kernel, final),
        grid=(steps,),
        in_specs=[pl.BlockSpec(memory_space=pltpu.SMEM), full, full, full] + [fixed] * 8 + [x_face, x_face, y_face, y_face, face_specs[4], face_specs[4]],
        out_specs=[full, full, out_spec] + face_specs,
        out_shape=[shape, shape, out_shape] + face_shapes,
        cost_estimate=pl.CostEstimate(flops=30 * size, transcendentals=0, bytes_accessed=4 * 7 * size + 4 * 7 * size // steps),
        name="chebyshev_sweep",
    )(jnp.array([first, second], jnp.float32), step_dir, residual, potential, *faces, diagonal, inverse, *halos)
    return outs[0], outs[1], outs[2], outs[3:]


def local(
    heart_state,
    cell_type,
    gate_half,
    gate_slope,
    gate_tau,
    conduct,
    reversal,
    block_device,
    block_row,
    tissue,
    tissue_sigma,
):
    voltage = heart_state[0]
    gate_state = heart_state[1:]
    heart_x, heart_y, row_len = voltage.shape
    blocks = heart_x * heart_y
    devices = lax.axis_size("gx") * lax.axis_size("gy") * lax.axis_size("gz")
    capacity = 3 * blocks // devices
    slots = devices * capacity
    torso_x, torso_y, torso_z = tissue.shape
    torso_rows = torso_x * torso_y

    dest_dev = block_device.reshape(blocks)
    dest_row = block_row.reshape(blocks)
    one_hot = (dest_dev[:, None] == jnp.arange(devices, dtype=jnp.int32)[None, :]).astype(jnp.int32)
    running = jnp.cumsum(one_hot, axis=0) - 1
    slot_rank = jnp.sum(running * one_hot, axis=1)
    slot_index = dest_dev * capacity + slot_rank
    slot_match = slot_index[None, :] == jnp.arange(slots, dtype=jnp.int32)[:, None]
    slot_used = jnp.any(slot_match, axis=1)
    slot_block = jnp.argmax(slot_match, axis=1).astype(jnp.int32)
    send_rows = jnp.where(slot_used, dest_row[slot_block], torso_rows)
    recv_rows = lax.all_to_all(
        send_rows.reshape(devices, capacity), ("gx", "gy", "gz"), 0, 0, tiled=True
    ).reshape(slots)
    row_match = recv_rows[None, :] == jnp.arange(torso_rows, dtype=jnp.int32)[:, None]
    row_used = jnp.any(row_match, axis=1)
    row_slot = jnp.argmax(row_match, axis=1).astype(jnp.int32)

    sigma = []
    for dim_index in range(3):
        value = jnp.zeros(tissue.shape, jnp.float32)
        for tissue_kind in range(tissue_sigma.shape[0]):
            value = value + jnp.where(tissue == tissue_kind, tissue_sigma[tissue_kind, dim_index], 0.0)
        sigma.append(value)
    riders = [faces_of(sigma[dim_index], dim_index) for dim_index in range(3)]

    currents = []
    for time_step in range(STEPS):
        gate_state, ion_current = membrane(
            voltage, gate_state, cell_type, gate_half, gate_slope, gate_tau, conduct, reversal
        )
        laplace, carried = heart_laplace(voltage, riders if time_step == 0 else None)
        if time_step == 0:
            sigma_halos = [item[0] for item in carried]
        current = SIGMA_HEART * laplace
        currents.append(current)
        voltage = voltage + DT_HEART * (current - ion_current)
    heart_next = jnp.concatenate([voltage[None], gate_state], axis=0)

    payload = jnp.stack([item.reshape(blocks, row_len) for item in currents], axis=0)
    send_values = jnp.where(slot_used[None, :, None], jnp.take(payload, slot_block, axis=1), 0.0)
    received = lax.all_to_all(
        send_values.reshape(STEPS, devices, capacity, row_len),
        ("gx", "gy", "gz"),
        1,
        1,
        tiled=True,
    ).reshape(STEPS, slots, row_len)
    source = jnp.where(row_used[None, :, None], jnp.take(received, row_slot, axis=1), 0.0)
    source = source.reshape(STEPS, torso_x, torso_y, torso_z)

    faces = []
    for dim_index in range(3):
        low, high = sigma_halos[dim_index]
        minus, plus = shifted(sigma[dim_index], low, high, dim_index)
        faces.append(0.5 * (sigma[dim_index] + plus))
        faces.append(0.5 * (sigma[dim_index] + minus))
    diagonal = SCREEN + faces[0] + faces[1] + faces[2] + faces[3] + faces[4] + faces[5]

    spectrum_mid, first_coef, second_coef = chebyshev_weights(SWEEPS)
    residual = source
    inverse = 1.0 / diagonal
    step_dir, dir_faces = run_initial(spectrum_mid, residual, inverse)
    potential = step_dir
    for sweep in range(1, SWEEPS):
        x_low, x_high = exchange(dir_faces[1], dir_faces[0], "gx")
        y_low, y_high = exchange(dir_faces[3], dir_faces[2], "gy")
        z_low, z_high = exchange(dir_faces[5], dir_faces[4], "gz")
        halos = (x_low, x_high, y_low, y_high, z_low, z_high)
        residual, step_dir, potential, dir_faces = run_sweep(
            first_coef[sweep - 1], second_coef[sweep - 1], step_dir, residual, potential, faces, diagonal, inverse, halos,
            final=sweep == SWEEPS - 1,
        )
    return (heart_next, potential)


def solution(mesh):
    in_specs = (
        P(None, "gx", "gy", "gz"),
        P("gx", "gy", "gz"),
        P(),
        P(),
        P(),
        P(),
        P(),
        P("gx", "gy", "gz"),
        P("gx", "gy", "gz"),
        P("gx", "gy", "gz"),
        P(),
    )
    out_specs = (P(None, "gx", "gy", "gz"), P("gx", "gy", None, "gz"))
    return jax.shard_map(local, mesh=mesh, in_specs=in_specs, out_specs=out_specs, check_vma=False)
```

```python
import jax
import jax.numpy as jnp
from jax import lax
from jax.sharding import PartitionSpec as P
from jax.experimental import pallas as pl
from jax.experimental.pallas import tpu as pltpu
import functools

STEPS = 4
SWEEPS = 4


DT_HEART = 0.05
SIGMA_HEART = 1.0
SCREEN = 0.05
LOW_EDGE = 0.1
HIGH_EDGE = 1.9


def chebyshev_weights(sweep_count):
    spectrum_mid = 0.5 * (HIGH_EDGE + LOW_EDGE)
    half_width = 0.5 * (HIGH_EDGE - LOW_EDGE)
    half_ratio = spectrum_mid / half_width
    rho_old = 1.0 / half_ratio
    first_coef = []
    second_coef = []
    for sweep in range(1, sweep_count):
        rho_new = 1.0 / (2.0 * half_ratio - rho_old)
        first_coef.append(rho_new * rho_old)
        second_coef.append(2.0 * rho_new / half_width)
        rho_old = rho_new
    return (spectrum_mid, first_coef, second_coef)


def face_halos(block, axis, dim):
    top = lax.index_in_dim(block, block.shape[dim] - 1, axis=dim, keepdims=False)
    bottom = lax.index_in_dim(block, 0, axis=dim, keepdims=False)
    return exchange(top, bottom, axis)


def shifted(block, low, high, dim):
    n = block.shape[dim]
    low = jnp.expand_dims(low, dim)
    high = jnp.expand_dims(high, dim)
    minus = jnp.concatenate([low, lax.slice_in_dim(block, 0, n - 1, axis=dim)], axis=dim)
    plus = jnp.concatenate([lax.slice_in_dim(block, 1, n, axis=dim), high], axis=dim)
    return minus, plus


def membrane(voltage, gate_state, cell_type, gate_half, gate_slope, gate_tau, conduct, reversal):
    gate_count = gate_half.shape[0]
    lead_shape = (-1,) + (1,) * voltage.ndim
    gate_sign = jnp.where(jnp.arange(gate_count) % 2 == 0, 1.0, -1.0).astype(jnp.float32)
    exponent = (gate_sign / gate_slope).reshape(lead_shape) * (
        voltage[None] - gate_half.reshape(lead_shape)
    )
    steady = jax.nn.sigmoid(exponent)
    time_const = gate_tau.reshape(lead_shape) * (0.5 + steady)
    gate_state = steady + (gate_state - steady) * jnp.exp(-DT_HEART / time_const)
    weight = jnp.zeros(gate_state[0::2].shape, jnp.float32)
    for cell_kind in range(conduct.shape[0]):
        weight = weight + jnp.where(
            cell_type[None] == cell_kind, conduct[cell_kind].reshape(lead_shape), 0.0
        )
    ion_current = jnp.sum(
        weight
        * gate_state[0::2]
        * gate_state[1::2]
        * (voltage[None] - reversal.reshape(lead_shape)),
        axis=0,
    )
    return (gate_state, ion_current)


def faces_of(block, dim):
    top = lax.index_in_dim(block, block.shape[dim] - 1, axis=dim, keepdims=False)
    bottom = lax.index_in_dim(block, 0, axis=dim, keepdims=False)
    return top, bottom


def heart_laplace(voltage, riders=None):
    parts = []
    carried = []
    for index, (axis, dim) in enumerate((("gx", 0), ("gy", 1), ("gz", 2))):
        pairs = [faces_of(voltage, dim)]
        if riders is not None:
            pairs.append(riders[index])
        got = exchange_group(pairs, axis)
        minus, plus = shifted(voltage, got[0][0], got[0][1], dim)
        parts.append((plus, minus))
        carried.append(got[1:])
    total = parts[0][0] + parts[0][1]
    total = total + parts[1][0] + parts[1][1]
    total = total + parts[2][0] + parts[2][1]
    return total - 6.0 * voltage, carried


def exchange(top, bottom, axis):
    count = lax.axis_size(axis)
    if count == 2:
        index = lax.axis_index(axis)
        got = lax.ppermute(jnp.where(index == 0, top, bottom), axis, [(0, 1), (1, 0)])
        zero = jnp.zeros_like(got)
        return jnp.where(index == 1, got, zero), jnp.where(index == 0, got, zero)
    forward = [(i, i + 1) for i in range(count - 1)]
    backward = [(i + 1, i) for i in range(count - 1)]
    return lax.ppermute(top, axis, forward), lax.ppermute(bottom, axis, backward)


def exchange_group(pairs, axis):
    if len(pairs) == 1:
        return [exchange(pairs[0][0], pairs[0][1], axis)]
    top = jnp.concatenate([item.reshape(-1) for item, _ in pairs])
    bottom = jnp.concatenate([item.reshape(-1) for _, item in pairs])
    low, high = exchange(top, bottom, axis)
    result = []
    offset = 0
    for item, _ in pairs:
        size = item.size
        result.append((low[offset:offset + size].reshape(item.shape), high[offset:offset + size].reshape(item.shape)))
        offset += size
    return result


def write_faces(x, value, columns, xf_lo, xf_hi, yf_lo, yf_hi, zf_lo, zf_hi):
    nx = yf_lo.shape[1]
    ny, nz = value.shape
    half = nz // 2
    lane = lax.broadcasted_iota(jnp.int32, (ny, nz), 1)

    yf_lo[0, x] = value[0:1, :]
    yf_hi[0, x] = value[ny - 1:ny, :]
    columns = jnp.where(lane == x, pltpu.roll(value, x, 1), columns)
    columns = jnp.where(lane == half + x, pltpu.roll(value, lax.rem(half + x + 1, nz), 1), columns)
    return columns


def finish_faces(d_out, columns, xf_lo, xf_hi, yf_lo, yf_hi, zf_lo, zf_hi):
    nx = yf_lo.shape[1]
    xf_lo[0] = d_out[0, 0]
    xf_hi[0] = d_out[0, nx - 1]
    half = columns.shape[1] // 2
    flipped = columns.T
    zf_lo[0] = flipped[0:nx, :]
    zf_hi[0] = flipped[half:half + nx, :]


def sweep_kernel(final, coef_ref, d_ref, r_ref, p_ref, fxp, fxm, fyp, fym, fzp, fzm, dg_ref, inv_ref,
                 xlo, xhi, ylo, yhi, zlo, zhi, r_out, d_out, p_out, *face_out):
    snapshot = pl.program_id(0)
    first = coef_ref[0]
    second = coef_ref[1]
    nx, ny, nz = d_ref.shape[1], d_ref.shape[2], d_ref.shape[3]
    row = lax.broadcasted_iota(jnp.int32, (ny, nz), 0)
    lane = lax.broadcasted_iota(jnp.int32, (ny, nz), 1)
    blank = jnp.zeros((nz - nx, ny), jnp.float32)
    low_cols = jnp.concatenate([zlo[0], blank], axis=0).T
    high_rows = zhi[0]
    high_cols = jnp.concatenate([high_rows[1:nx], blank, high_rows[0:1]], axis=0).T

    def body(x, carry):
        centre = d_ref[0, x]
        below = d_ref[0, jnp.maximum(x - 1, 0)]
        above = d_ref[0, jnp.minimum(x + 1, nx - 1)]
        x_minus = jnp.where(x == 0, xlo[0], below)
        x_plus = jnp.where(x == nx - 1, xhi[0], above)
        y_minus = jnp.where(row == 0, ylo[0, x], pltpu.roll(centre, 1, 0))
        y_plus = jnp.where(row == ny - 1, yhi[0, x], pltpu.roll(centre, ny - 1, 0))
        turn = lax.rem(nz - x, nz)
        z_minus = jnp.where(lane == 0, pltpu.roll(low_cols, turn, 1), pltpu.roll(centre, 1, 1))
        z_plus = jnp.where(lane == nz - 1, pltpu.roll(high_cols, turn, 1), pltpu.roll(centre, nz - 1, 1))
        beside = fxp[x] * x_plus + fxm[x] * x_minus
        beside = beside + fyp[x] * y_plus + fym[x] * y_minus
        beside = beside + fzp[x] * z_plus + fzm[x] * z_minus
        diag = dg_ref[x]
        residual = r_ref[0, x] - (diag * centre - beside)
        step_dir = first * centre + second * (residual * inv_ref[x])
        r_out[0, x] = residual
        d_out[0, x] = step_dir
        if final:
            p_out[x, :, snapshot, :] = p_ref[0, x] + step_dir
        else:
            p_out[0, x] = p_ref[0, x] + step_dir
        return write_faces(x, step_dir, carry, *face_out)

    columns = lax.fori_loop(0, nx, body, jnp.zeros((ny, nz), jnp.float32), unroll=16)
    finish_faces(d_out, columns, *face_out)


def initial_kernel(mid, r_ref, inv_ref, d_out, *face_out):
    nx, ny, nz = r_ref.shape[1], r_ref.shape[2], r_ref.shape[3]

    def body(x, carry):
        step_dir = r_ref[0, x] * inv_ref[x] * (1.0 / mid)
        d_out[0, x] = step_dir
        return write_faces(x, step_dir, carry, *face_out)

    columns = lax.fori_loop(0, nx, body, jnp.zeros((ny, nz), jnp.float32), unroll=16)
    finish_faces(d_out, columns, *face_out)


def specs(shape):
    steps, nx, ny, nz = shape
    full = pl.BlockSpec((1, nx, ny, nz), lambda s: (s, 0, 0, 0))
    fixed = pl.BlockSpec((nx, ny, nz), lambda s: (0, 0, 0))
    x_face = pl.BlockSpec((1, ny, nz), lambda s: (s, 0, 0))
    y_face = pl.BlockSpec((1, nx, 1, nz), lambda s: (s, 0, 0, 0))
    z_face = pl.BlockSpec((1, nx, ny), lambda s: (s, 0, 0))
    face_specs = [x_face, x_face, y_face, y_face, z_face, z_face]
    face_shapes = [
        jax.ShapeDtypeStruct((steps, ny, nz), jnp.float32),
        jax.ShapeDtypeStruct((steps, ny, nz), jnp.float32),
        jax.ShapeDtypeStruct((steps, nx, 1, nz), jnp.float32),
        jax.ShapeDtypeStruct((steps, nx, 1, nz), jnp.float32),
        jax.ShapeDtypeStruct((steps, nx, ny), jnp.float32),
        jax.ShapeDtypeStruct((steps, nx, ny), jnp.float32),
    ]
    return full, fixed, face_specs, face_shapes


def run_initial(mid, source, inverse):
    full, fixed, face_specs, face_shapes = specs(source.shape)
    shape = jax.ShapeDtypeStruct(source.shape, jnp.float32)
    size = source.size
    outs = pl.pallas_call(
        functools.partial(initial_kernel, mid),
        grid=(source.shape[0],),
        in_specs=[full, fixed],
        out_specs=[full] + face_specs,
        out_shape=[shape] + face_shapes,
        cost_estimate=pl.CostEstimate(flops=2 * size, transcendentals=0, bytes_accessed=8 * size + 4 * size // source.shape[0]),
        name="chebyshev_start",
    )(source, inverse)
    return outs[0], outs[1:]


def run_sweep(first, second, step_dir, residual, potential, faces, diagonal, inverse, halos, final=False):
    full, fixed, face_specs, face_shapes = specs(step_dir.shape)
    steps, nx, ny, nz = step_dir.shape
    x_face, y_face = face_specs[0], face_specs[2]
    shape = jax.ShapeDtypeStruct(step_dir.shape, jnp.float32)
    if final:
        out_spec = pl.BlockSpec((nx, ny, steps, nz), lambda s: (0, 0, 0, 0))
        out_shape = jax.ShapeDtypeStruct((nx, ny, steps, nz), jnp.float32)
    else:
        out_spec, out_shape = full, shape
    size = step_dir.size
    outs = pl.pallas_call(
        functools.partial(sweep_kernel, final),
        grid=(steps,),
        in_specs=[pl.BlockSpec(memory_space=pltpu.SMEM), full, full, full] + [fixed] * 8 + [x_face, x_face, y_face, y_face, face_specs[4], face_specs[4]],
        out_specs=[full, full, out_spec] + face_specs,
        out_shape=[shape, shape, out_shape] + face_shapes,
        cost_estimate=pl.CostEstimate(flops=30 * size, transcendentals=0, bytes_accessed=4 * 7 * size + 4 * 7 * size // steps),
        name="chebyshev_sweep",
    )(jnp.array([first, second], jnp.float32), step_dir, residual, potential, *faces, diagonal, inverse, *halos)
    return outs[0], outs[1], outs[2], outs[3:]


def local(
    heart_state,
    cell_type,
    gate_half,
    gate_slope,
    gate_tau,
    conduct,
    reversal,
    block_device,
    block_row,
    tissue,
    tissue_sigma,
):
    voltage = heart_state[0]
    gate_state = heart_state[1:]
    heart_x, heart_y, row_len = voltage.shape
    blocks = heart_x * heart_y
    devices = lax.axis_size("gx") * lax.axis_size("gy") * lax.axis_size("gz")
    capacity = 3 * blocks // devices
    slots = devices * capacity
    torso_x, torso_y, torso_z = tissue.shape
    torso_rows = torso_x * torso_y

    dest_dev = block_device.reshape(blocks)
    dest_row = block_row.reshape(blocks)
    one_hot = (dest_dev[:, None] == jnp.arange(devices, dtype=jnp.int32)[None, :]).astype(jnp.int32)
    running = jnp.cumsum(one_hot, axis=0) - 1
    slot_rank = jnp.sum(running * one_hot, axis=1)
    slot_index = dest_dev * capacity + slot_rank
    slot_match = slot_index[None, :] == jnp.arange(slots, dtype=jnp.int32)[:, None]
    slot_used = jnp.any(slot_match, axis=1)
    slot_block = jnp.argmax(slot_match, axis=1).astype(jnp.int32)
    send_rows = jnp.where(slot_used, dest_row[slot_block], torso_rows)
    recv_rows = lax.all_to_all(
        send_rows.reshape(devices, capacity), ("gx", "gy", "gz"), 0, 0, tiled=True
    ).reshape(slots)
    row_match = recv_rows[None, :] == jnp.arange(torso_rows, dtype=jnp.int32)[:, None]
    row_used = jnp.any(row_match, axis=1)
    row_slot = jnp.argmax(row_match, axis=1).astype(jnp.int32)

    sigma = []
    for dim_index in range(3):
        value = jnp.zeros(tissue.shape, jnp.float32)
        for tissue_kind in range(tissue_sigma.shape[0]):
            value = value + jnp.where(tissue == tissue_kind, tissue_sigma[tissue_kind, dim_index], 0.0)
        sigma.append(value)
    riders = [faces_of(sigma[dim_index], dim_index) for dim_index in range(3)]

    currents = []
    for time_step in range(STEPS):
        gate_state, ion_current = membrane(
            voltage, gate_state, cell_type, gate_half, gate_slope, gate_tau, conduct, reversal
        )
        laplace, carried = heart_laplace(voltage, riders if time_step == 0 else None)
        if time_step == 0:
            sigma_halos = [item[0] for item in carried]
        current = SIGMA_HEART * laplace
        currents.append(current)
        voltage = voltage + DT_HEART * (current - ion_current)
    heart_next = jnp.concatenate([voltage[None], gate_state], axis=0)

    payload = jnp.stack([item.reshape(blocks, row_len) for item in currents], axis=0)
    send_values = jnp.where(slot_used[None, :, None], jnp.take(payload, slot_block, axis=1), 0.0)
    received = lax.all_to_all(
        send_values.reshape(STEPS, devices, capacity, row_len),
        ("gx", "gy", "gz"),
        1,
        1,
        tiled=True,
    ).reshape(STEPS, slots, row_len)
    source = jnp.where(row_used[None, :, None], jnp.take(received, row_slot, axis=1), 0.0)
    source = source.reshape(STEPS, torso_x, torso_y, torso_z)

    faces = []
    for dim_index in range(3):
        low, high = sigma_halos[dim_index]
        minus, plus = shifted(sigma[dim_index], low, high, dim_index)
        faces.append(0.5 * (sigma[dim_index] + plus))
        faces.append(0.5 * (sigma[dim_index] + minus))
    diagonal = SCREEN + faces[0] + faces[1] + faces[2] + faces[3] + faces[4] + faces[5]

    spectrum_mid, first_coef, second_coef = chebyshev_weights(SWEEPS)
    residual = source
    inverse = 1.0 / diagonal
    step_dir, dir_faces = run_initial(spectrum_mid, residual, inverse)
    potential = step_dir
    for sweep in range(1, SWEEPS):
        x_low, x_high = exchange(dir_faces[1], dir_faces[0], "gx")
        y_low, y_high = exchange(dir_faces[3], dir_faces[2], "gy")
        z_low, z_high = exchange(dir_faces[5], dir_faces[4], "gz")
        halos = (x_low, x_high, y_low, y_high, z_low, z_high)
        residual, step_dir, potential, dir_faces = run_sweep(
            first_coef[sweep - 1], second_coef[sweep - 1], step_dir, residual, potential, faces, diagonal, inverse, halos,
            final=sweep == SWEEPS - 1,
        )
    return (heart_next, potential)


def solution(mesh):
    in_specs = (
        P(None, "gx", "gy", "gz"),
        P("gx", "gy", "gz"),
        P(),
        P(),
        P(),
        P(),
        P(),
        P("gx", "gy", "gz"),
        P("gx", "gy", "gz"),
        P("gx", "gy", "gz"),
        P(),
    )
    out_specs = (P(None, "gx", "gy", "gz"), P("gx", "gy", None, "gz"))
    return jax.shard_map(local, mesh=mesh, in_specs=in_specs, out_specs=out_specs, check_vma=False)
```

```python
import jax
import jax.numpy as jnp
from jax import lax
from jax.sharding import PartitionSpec as P
from jax.experimental import pallas as pl
from jax.experimental.pallas import tpu as pltpu
import functools

STEPS = 4
SWEEPS = 4


DT_HEART = 0.05
SIGMA_HEART = 1.0
SCREEN = 0.05
LOW_EDGE = 0.1
HIGH_EDGE = 1.9


def chebyshev_weights(sweep_count):
    spectrum_mid = 0.5 * (HIGH_EDGE + LOW_EDGE)
    half_width = 0.5 * (HIGH_EDGE - LOW_EDGE)
    half_ratio = spectrum_mid / half_width
    rho_old = 1.0 / half_ratio
    first_coef = []
    second_coef = []
    for sweep in range(1, sweep_count):
        rho_new = 1.0 / (2.0 * half_ratio - rho_old)
        first_coef.append(rho_new * rho_old)
        second_coef.append(2.0 * rho_new / half_width)
        rho_old = rho_new
    return (spectrum_mid, first_coef, second_coef)


def face_halos(block, axis, dim):
    top = lax.index_in_dim(block, block.shape[dim] - 1, axis=dim, keepdims=False)
    bottom = lax.index_in_dim(block, 0, axis=dim, keepdims=False)
    return exchange(top, bottom, axis)


def shifted(block, low, high, dim):
    n = block.shape[dim]
    low = jnp.expand_dims(low, dim)
    high = jnp.expand_dims(high, dim)
    minus = jnp.concatenate([low, lax.slice_in_dim(block, 0, n - 1, axis=dim)], axis=dim)
    plus = jnp.concatenate([lax.slice_in_dim(block, 1, n, axis=dim), high], axis=dim)
    return minus, plus


def membrane(voltage, gate_state, cell_type, gate_half, gate_slope, gate_tau, conduct, reversal):
    gate_count = gate_half.shape[0]
    lead_shape = (-1,) + (1,) * voltage.ndim
    gate_sign = jnp.where(jnp.arange(gate_count) % 2 == 0, 1.0, -1.0).astype(jnp.float32)
    exponent = (gate_sign / gate_slope).reshape(lead_shape) * (
        voltage[None] - gate_half.reshape(lead_shape)
    )
    steady = jax.nn.sigmoid(exponent)
    time_const = gate_tau.reshape(lead_shape) * (0.5 + steady)
    gate_state = steady + (gate_state - steady) * jnp.exp(-DT_HEART / time_const)
    weight = jnp.zeros(gate_state[0::2].shape, jnp.float32)
    for cell_kind in range(conduct.shape[0]):
        weight = weight + jnp.where(
            cell_type[None] == cell_kind, conduct[cell_kind].reshape(lead_shape), 0.0
        )
    ion_current = jnp.sum(
        weight
        * gate_state[0::2]
        * gate_state[1::2]
        * (voltage[None] - reversal.reshape(lead_shape)),
        axis=0,
    )
    return (gate_state, ion_current)


def faces_of(block, dim):
    top = lax.index_in_dim(block, block.shape[dim] - 1, axis=dim, keepdims=False)
    bottom = lax.index_in_dim(block, 0, axis=dim, keepdims=False)
    return top, bottom


def heart_laplace(voltage, riders=None):
    parts = []
    carried = []
    for index, (axis, dim) in enumerate((("gx", 0), ("gy", 1), ("gz", 2))):
        pairs = [faces_of(voltage, dim)]
        if riders is not None:
            pairs.append(riders[index])
        got = exchange_group(pairs, axis)
        minus, plus = shifted(voltage, got[0][0], got[0][1], dim)
        parts.append((plus, minus))
        carried.append(got[1:])
    total = parts[0][0] + parts[0][1]
    total = total + parts[1][0] + parts[1][1]
    total = total + parts[2][0] + parts[2][1]
    return total - 6.0 * voltage, carried


def exchange(top, bottom, axis):
    count = lax.axis_size(axis)
    if count == 2:
        index = lax.axis_index(axis)
        got = lax.ppermute(jnp.where(index == 0, top, bottom), axis, [(0, 1), (1, 0)])
        zero = jnp.zeros_like(got)
        return jnp.where(index == 1, got, zero), jnp.where(index == 0, got, zero)
    forward = [(i, i + 1) for i in range(count - 1)]
    backward = [(i + 1, i) for i in range(count - 1)]
    return lax.ppermute(top, axis, forward), lax.ppermute(bottom, axis, backward)


def exchange_group(pairs, axis):
    if len(pairs) == 1:
        return [exchange(pairs[0][0], pairs[0][1], axis)]
    top = jnp.concatenate([item.reshape(-1) for item, _ in pairs])
    bottom = jnp.concatenate([item.reshape(-1) for _, item in pairs])
    low, high = exchange(top, bottom, axis)
    result = []
    offset = 0
    for item, _ in pairs:
        size = item.size
        result.append((low[offset:offset + size].reshape(item.shape), high[offset:offset + size].reshape(item.shape)))
        offset += size
    return result


def write_faces(x, value, columns, xf_lo, xf_hi, yf_lo, yf_hi, zf_lo, zf_hi):
    nx = yf_lo.shape[1]
    ny, nz = value.shape
    half = nz // 2
    lane = lax.broadcasted_iota(jnp.int32, (ny, nz), 1)

    yf_lo[0, x] = value[0:1, :]
    yf_hi[0, x] = value[ny - 1:ny, :]
    columns = jnp.where(lane == x, pltpu.roll(value, x, 1), columns)
    columns = jnp.where(lane == half + x, pltpu.roll(value, lax.rem(half + x + 1, nz), 1), columns)
    return columns


def finish_faces(d_out, columns, xf_lo, xf_hi, yf_lo, yf_hi, zf_lo, zf_hi):
    nx = yf_lo.shape[1]
    xf_lo[0] = d_out[0, 0]
    xf_hi[0] = d_out[0, nx - 1]
    half = columns.shape[1] // 2
    flipped = columns.T
    zf_lo[0] = flipped[0:nx, :]
    zf_hi[0] = flipped[half:half + nx, :]


def sweep_kernel(final, coef_ref, d_ref, r_ref, p_ref, fxp, fxm, fyp, fym, fzp, fzm, dg_ref, inv_ref,
                 xlo, xhi, ylo, yhi, zlo, zhi, r_out, d_out, p_out, *face_out):
    snapshot = pl.program_id(0)
    first = coef_ref[0]
    second = coef_ref[1]
    nx, ny, nz = d_ref.shape[1], d_ref.shape[2], d_ref.shape[3]
    row = lax.broadcasted_iota(jnp.int32, (ny, nz), 0)
    lane = lax.broadcasted_iota(jnp.int32, (ny, nz), 1)
    blank = jnp.zeros((nz - nx, ny), jnp.float32)
    low_cols = jnp.concatenate([zlo[0], blank], axis=0).T
    high_rows = zhi[0]
    high_cols = jnp.concatenate([high_rows[1:nx], blank, high_rows[0:1]], axis=0).T

    def body(x, carry):
        centre = d_ref[0, x]
        below = d_ref[0, jnp.maximum(x - 1, 0)]
        above = d_ref[0, jnp.minimum(x + 1, nx - 1)]
        x_minus = jnp.where(x == 0, xlo[0], below)
        x_plus = jnp.where(x == nx - 1, xhi[0], above)
        y_minus = jnp.where(row == 0, ylo[0, x], pltpu.roll(centre, 1, 0))
        y_plus = jnp.where(row == ny - 1, yhi[0, x], pltpu.roll(centre, ny - 1, 0))
        turn = lax.rem(nz - x, nz)
        z_minus = jnp.where(lane == 0, pltpu.roll(low_cols, turn, 1), pltpu.roll(centre, 1, 1))
        z_plus = jnp.where(lane == nz - 1, pltpu.roll(high_cols, turn, 1), pltpu.roll(centre, nz - 1, 1))
        beside = fxp[x] * x_plus + fxm[x] * x_minus
        beside = beside + fyp[x] * y_plus + fym[x] * y_minus
        beside = beside + fzp[x] * z_plus + fzm[x] * z_minus
        diag = dg_ref[x]
        residual = r_ref[0, x] - (diag * centre - beside)
        step_dir = first * centre + second * (residual * inv_ref[x])
        r_out[0, x] = residual
        d_out[0, x] = step_dir
        if final:
            p_out[x, :, snapshot, :] = p_ref[0, x] + step_dir
        else:
            p_out[0, x] = p_ref[0, x] + step_dir
        return write_faces(x, step_dir, carry, *face_out)

    columns = lax.fori_loop(0, nx, body, jnp.zeros((ny, nz), jnp.float32), unroll=32)
    finish_faces(d_out, columns, *face_out)


def initial_kernel(mid, r_ref, inv_ref, d_out, *face_out):
    nx, ny, nz = r_ref.shape[1], r_ref.shape[2], r_ref.shape[3]

    def body(x, carry):
        step_dir = r_ref[0, x] * inv_ref[x] * (1.0 / mid)
        d_out[0, x] = step_dir
        return write_faces(x, step_dir, carry, *face_out)

    columns = lax.fori_loop(0, nx, body, jnp.zeros((ny, nz), jnp.float32), unroll=16)
    finish_faces(d_out, columns, *face_out)


def specs(shape):
    steps, nx, ny, nz = shape
    full = pl.BlockSpec((1, nx, ny, nz), lambda s: (s, 0, 0, 0))
    fixed = pl.BlockSpec((nx, ny, nz), lambda s: (0, 0, 0))
    x_face = pl.BlockSpec((1, ny, nz), lambda s: (s, 0, 0))
    y_face = pl.BlockSpec((1, nx, 1, nz), lambda s: (s, 0, 0, 0))
    z_face = pl.BlockSpec((1, nx, ny), lambda s: (s, 0, 0))
    face_specs = [x_face, x_face, y_face, y_face, z_face, z_face]
    face_shapes = [
        jax.ShapeDtypeStruct((steps, ny, nz), jnp.float32),
        jax.ShapeDtypeStruct((steps, ny, nz), jnp.float32),
        jax.ShapeDtypeStruct((steps, nx, 1, nz), jnp.float32),
        jax.ShapeDtypeStruct((steps, nx, 1, nz), jnp.float32),
        jax.ShapeDtypeStruct((steps, nx, ny), jnp.float32),
        jax.ShapeDtypeStruct((steps, nx, ny), jnp.float32),
    ]
    return full, fixed, face_specs, face_shapes


def run_initial(mid, source, inverse):
    full, fixed, face_specs, face_shapes = specs(source.shape)
    shape = jax.ShapeDtypeStruct(source.shape, jnp.float32)
    size = source.size
    outs = pl.pallas_call(
        functools.partial(initial_kernel, mid),
        grid=(source.shape[0],),
        in_specs=[full, fixed],
        out_specs=[full] + face_specs,
        out_shape=[shape] + face_shapes,
        cost_estimate=pl.CostEstimate(flops=2 * size, transcendentals=0, bytes_accessed=8 * size + 4 * size // source.shape[0]),
        name="chebyshev_start",
    )(source, inverse)
    return outs[0], outs[1:]


def run_sweep(first, second, step_dir, residual, potential, faces, diagonal, inverse, halos, final=False):
    full, fixed, face_specs, face_shapes = specs(step_dir.shape)
    steps, nx, ny, nz = step_dir.shape
    x_face, y_face = face_specs[0], face_specs[2]
    shape = jax.ShapeDtypeStruct(step_dir.shape, jnp.float32)
    if final:
        out_spec = pl.BlockSpec((nx, ny, steps, nz), lambda s: (0, 0, 0, 0))
        out_shape = jax.ShapeDtypeStruct((nx, ny, steps, nz), jnp.float32)
    else:
        out_spec, out_shape = full, shape
    size = step_dir.size
    outs = pl.pallas_call(
        functools.partial(sweep_kernel, final),
        grid=(steps,),
        in_specs=[pl.BlockSpec(memory_space=pltpu.SMEM), full, full, full] + [fixed] * 8 + [x_face, x_face, y_face, y_face, face_specs[4], face_specs[4]],
        out_specs=[full, full, out_spec] + face_specs,
        out_shape=[shape, shape, out_shape] + face_shapes,
        cost_estimate=pl.CostEstimate(flops=30 * size, transcendentals=0, bytes_accessed=4 * 7 * size + 4 * 7 * size // steps),
        name="chebyshev_sweep",
    )(jnp.array([first, second], jnp.float32), step_dir, residual, potential, *faces, diagonal, inverse, *halos)
    return outs[0], outs[1], outs[2], outs[3:]


def local(
    heart_state,
    cell_type,
    gate_half,
    gate_slope,
    gate_tau,
    conduct,
    reversal,
    block_device,
    block_row,
    tissue,
    tissue_sigma,
):
    voltage = heart_state[0]
    gate_state = heart_state[1:]
    heart_x, heart_y, row_len = voltage.shape
    blocks = heart_x * heart_y
    devices = lax.axis_size("gx") * lax.axis_size("gy") * lax.axis_size("gz")
    capacity = 3 * blocks // devices
    slots = devices * capacity
    torso_x, torso_y, torso_z = tissue.shape
    torso_rows = torso_x * torso_y

    dest_dev = block_device.reshape(blocks)
    dest_row = block_row.reshape(blocks)
    one_hot = (dest_dev[:, None] == jnp.arange(devices, dtype=jnp.int32)[None, :]).astype(jnp.int32)
    running = jnp.cumsum(one_hot, axis=0) - 1
    slot_rank = jnp.sum(running * one_hot, axis=1)
    slot_index = dest_dev * capacity + slot_rank
    slot_match = slot_index[None, :] == jnp.arange(slots, dtype=jnp.int32)[:, None]
    slot_used = jnp.any(slot_match, axis=1)
    slot_block = jnp.argmax(slot_match, axis=1).astype(jnp.int32)
    send_rows = jnp.where(slot_used, dest_row[slot_block], torso_rows)
    recv_rows = lax.all_to_all(
        send_rows.reshape(devices, capacity), ("gx", "gy", "gz"), 0, 0, tiled=True
    ).reshape(slots)
    row_match = recv_rows[None, :] == jnp.arange(torso_rows, dtype=jnp.int32)[:, None]
    row_used = jnp.any(row_match, axis=1)
    row_slot = jnp.argmax(row_match, axis=1).astype(jnp.int32)

    sigma = []
    for dim_index in range(3):
        value = jnp.zeros(tissue.shape, jnp.float32)
        for tissue_kind in range(tissue_sigma.shape[0]):
            value = value + jnp.where(tissue == tissue_kind, tissue_sigma[tissue_kind, dim_index], 0.0)
        sigma.append(value)
    riders = [faces_of(sigma[dim_index], dim_index) for dim_index in range(3)]

    currents = []
    for time_step in range(STEPS):
        gate_state, ion_current = membrane(
            voltage, gate_state, cell_type, gate_half, gate_slope, gate_tau, conduct, reversal
        )
        laplace, carried = heart_laplace(voltage, riders if time_step == 0 else None)
        if time_step == 0:
            sigma_halos = [item[0] for item in carried]
        current = SIGMA_HEART * laplace
        currents.append(current)
        voltage = voltage + DT_HEART * (current - ion_current)
    heart_next = jnp.concatenate([voltage[None], gate_state], axis=0)

    payload = jnp.stack([item.reshape(blocks, row_len) for item in currents], axis=0)
    send_values = jnp.where(slot_used[None, :, None], jnp.take(payload, slot_block, axis=1), 0.0)
    received = lax.all_to_all(
        send_values.reshape(STEPS, devices, capacity, row_len),
        ("gx", "gy", "gz"),
        1,
        1,
        tiled=True,
    ).reshape(STEPS, slots, row_len)
    source = jnp.where(row_used[None, :, None], jnp.take(received, row_slot, axis=1), 0.0)
    source = source.reshape(STEPS, torso_x, torso_y, torso_z)

    faces = []
    for dim_index in range(3):
        low, high = sigma_halos[dim_index]
        minus, plus = shifted(sigma[dim_index], low, high, dim_index)
        faces.append(0.5 * (sigma[dim_index] + plus))
        faces.append(0.5 * (sigma[dim_index] + minus))
    diagonal = SCREEN + faces[0] + faces[1] + faces[2] + faces[3] + faces[4] + faces[5]

    spectrum_mid, first_coef, second_coef = chebyshev_weights(SWEEPS)
    residual = source
    inverse = 1.0 / diagonal
    step_dir, dir_faces = run_initial(spectrum_mid, residual, inverse)
    potential = step_dir
    for sweep in range(1, SWEEPS):
        x_low, x_high = exchange(dir_faces[1], dir_faces[0], "gx")
        y_low, y_high = exchange(dir_faces[3], dir_faces[2], "gy")
        z_low, z_high = exchange(dir_faces[5], dir_faces[4], "gz")
        halos = (x_low, x_high, y_low, y_high, z_low, z_high)
        residual, step_dir, potential, dir_faces = run_sweep(
            first_coef[sweep - 1], second_coef[sweep - 1], step_dir, residual, potential, faces, diagonal, inverse, halos,
            final=sweep == SWEEPS - 1,
        )
    return (heart_next, potential)


def solution(mesh):
    in_specs = (
        P(None, "gx", "gy", "gz"),
        P("gx", "gy", "gz"),
        P(),
        P(),
        P(),
        P(),
        P(),
        P("gx", "gy", "gz"),
        P("gx", "gy", "gz"),
        P("gx", "gy", "gz"),
        P(),
    )
    out_specs = (P(None, "gx", "gy", "gz"), P("gx", "gy", None, "gz"))
    return jax.shard_map(local, mesh=mesh, in_specs=in_specs, out_specs=out_specs, check_vma=False)
```

```python
import jax
import jax.numpy as jnp
from jax import lax
from jax.sharding import PartitionSpec as P
from jax.experimental import pallas as pl
from jax.experimental.pallas import tpu as pltpu
import functools

STEPS = 4
SWEEPS = 4


DT_HEART = 0.05
SIGMA_HEART = 1.0
SCREEN = 0.05
LOW_EDGE = 0.1
HIGH_EDGE = 1.9


def chebyshev_weights(sweep_count):
    spectrum_mid = 0.5 * (HIGH_EDGE + LOW_EDGE)
    half_width = 0.5 * (HIGH_EDGE - LOW_EDGE)
    half_ratio = spectrum_mid / half_width
    rho_old = 1.0 / half_ratio
    first_coef = []
    second_coef = []
    for sweep in range(1, sweep_count):
        rho_new = 1.0 / (2.0 * half_ratio - rho_old)
        first_coef.append(rho_new * rho_old)
        second_coef.append(2.0 * rho_new / half_width)
        rho_old = rho_new
    return (spectrum_mid, first_coef, second_coef)


def face_halos(block, axis, dim):
    top = lax.index_in_dim(block, block.shape[dim] - 1, axis=dim, keepdims=False)
    bottom = lax.index_in_dim(block, 0, axis=dim, keepdims=False)
    return exchange(top, bottom, axis)


def shifted(block, low, high, dim):
    n = block.shape[dim]
    low = jnp.expand_dims(low, dim)
    high = jnp.expand_dims(high, dim)
    minus = jnp.concatenate([low, lax.slice_in_dim(block, 0, n - 1, axis=dim)], axis=dim)
    plus = jnp.concatenate([lax.slice_in_dim(block, 1, n, axis=dim), high], axis=dim)
    return minus, plus


def membrane(voltage, gate_state, cell_type, gate_half, gate_slope, gate_tau, conduct, reversal):
    gate_count = gate_half.shape[0]
    lead_shape = (-1,) + (1,) * voltage.ndim
    gate_sign = jnp.where(jnp.arange(gate_count) % 2 == 0, 1.0, -1.0).astype(jnp.float32)
    exponent = (gate_sign / gate_slope).reshape(lead_shape) * (
        voltage[None] - gate_half.reshape(lead_shape)
    )
    steady = jax.nn.sigmoid(exponent)
    time_const = gate_tau.reshape(lead_shape) * (0.5 + steady)
    gate_state = steady + (gate_state - steady) * jnp.exp(-DT_HEART / time_const)
    weight = jnp.zeros(gate_state[0::2].shape, jnp.float32)
    for cell_kind in range(conduct.shape[0]):
        weight = weight + jnp.where(
            cell_type[None] == cell_kind, conduct[cell_kind].reshape(lead_shape), 0.0
        )
    ion_current = jnp.sum(
        weight
        * gate_state[0::2]
        * gate_state[1::2]
        * (voltage[None] - reversal.reshape(lead_shape)),
        axis=0,
    )
    return (gate_state, ion_current)


def faces_of(block, dim):
    top = lax.index_in_dim(block, block.shape[dim] - 1, axis=dim, keepdims=False)
    bottom = lax.index_in_dim(block, 0, axis=dim, keepdims=False)
    return top, bottom


def heart_laplace(voltage, riders=None):
    parts = []
    carried = []
    for index, (axis, dim) in enumerate((("gx", 0), ("gy", 1), ("gz", 2))):
        pairs = [faces_of(voltage, dim)]
        if riders is not None:
            pairs.append(riders[index])
        got = exchange_group(pairs, axis)
        minus, plus = shifted(voltage, got[0][0], got[0][1], dim)
        parts.append((plus, minus))
        carried.append(got[1:])
    total = parts[0][0] + parts[0][1]
    total = total + parts[1][0] + parts[1][1]
    total = total + parts[2][0] + parts[2][1]
    return total - 6.0 * voltage, carried


def exchange(top, bottom, axis):
    count = lax.axis_size(axis)
    if count == 2:
        index = lax.axis_index(axis)
        got = lax.ppermute(jnp.where(index == 0, top, bottom), axis, [(0, 1), (1, 0)])
        zero = jnp.zeros_like(got)
        return jnp.where(index == 1, got, zero), jnp.where(index == 0, got, zero)
    forward = [(i, i + 1) for i in range(count - 1)]
    backward = [(i + 1, i) for i in range(count - 1)]
    return lax.ppermute(top, axis, forward), lax.ppermute(bottom, axis, backward)


def exchange_group(pairs, axis):
    if len(pairs) == 1:
        return [exchange(pairs[0][0], pairs[0][1], axis)]
    top = jnp.concatenate([item.reshape(-1) for item, _ in pairs])
    bottom = jnp.concatenate([item.reshape(-1) for _, item in pairs])
    low, high = exchange(top, bottom, axis)
    result = []
    offset = 0
    for item, _ in pairs:
        size = item.size
        result.append((low[offset:offset + size].reshape(item.shape), high[offset:offset + size].reshape(item.shape)))
        offset += size
    return result


def write_faces(x, value, columns, xf_lo, xf_hi, yf_lo, yf_hi, zf_lo, zf_hi):
    nx = yf_lo.shape[1]
    ny, nz = value.shape
    half = nz // 2
    lane = lax.broadcasted_iota(jnp.int32, (ny, nz), 1)

    yf_lo[0, x] = value[0:1, :]
    yf_hi[0, x] = value[ny - 1:ny, :]
    columns = jnp.where(lane == x, pltpu.roll(value, x, 1), columns)
    columns = jnp.where(lane == half + x, pltpu.roll(value, lax.rem(half + x + 1, nz), 1), columns)
    return columns


def finish_faces(d_out, columns, xf_lo, xf_hi, yf_lo, yf_hi, zf_lo, zf_hi):
    nx = yf_lo.shape[1]
    xf_lo[0] = d_out[0, 0]
    xf_hi[0] = d_out[0, nx - 1]
    half = columns.shape[1] // 2
    flipped = columns.T
    zf_lo[0] = flipped[0:nx, :]
    zf_hi[0] = flipped[half:half + nx, :]


def sweep_kernel(final, coef_ref, d_ref, r_ref, p_ref, fxp, fxm, fyp, fym, fzp, fzm, dg_ref, inv_ref,
                 xlo, xhi, ylo, yhi, zlo, zhi, r_out, d_out, p_out, *face_out):
    snapshot = pl.program_id(0)
    first = coef_ref[0]
    second = coef_ref[1]
    nx, ny, nz = d_ref.shape[1], d_ref.shape[2], d_ref.shape[3]
    row = lax.broadcasted_iota(jnp.int32, (ny, nz), 0)
    lane = lax.broadcasted_iota(jnp.int32, (ny, nz), 1)
    blank = jnp.zeros((nz - nx, ny), jnp.float32)
    low_cols = jnp.concatenate([zlo[0], blank], axis=0).T
    high_rows = zhi[0]
    high_cols = jnp.concatenate([high_rows[1:nx], blank, high_rows[0:1]], axis=0).T

    def body(x, carry):
        centre = d_ref[0, x]
        below = d_ref[0, jnp.maximum(x - 1, 0)]
        above = d_ref[0, jnp.minimum(x + 1, nx - 1)]
        x_minus = jnp.where(x == 0, xlo[0], below)
        x_plus = jnp.where(x == nx - 1, xhi[0], above)
        y_minus = jnp.where(row == 0, ylo[0, x], pltpu.roll(centre, 1, 0))
        y_plus = jnp.where(row == ny - 1, yhi[0, x], pltpu.roll(centre, ny - 1, 0))
        turn = lax.rem(nz - x, nz)
        z_minus = jnp.where(lane == 0, pltpu.roll(low_cols, turn, 1), pltpu.roll(centre, 1, 1))
        z_plus = jnp.where(lane == nz - 1, pltpu.roll(high_cols, turn, 1), pltpu.roll(centre, nz - 1, 1))
        beside = fxp[x] * x_plus + fxm[x] * x_minus
        beside = beside + fyp[x] * y_plus + fym[x] * y_minus
        beside = beside + fzp[x] * z_plus + fzm[x] * z_minus
        diag = dg_ref[x]
        residual = r_ref[0, x] - (diag * centre - beside)
        step_dir = first * centre + second * (residual * inv_ref[x])
        r_out[0, x] = residual
        d_out[0, x] = step_dir
        if final:
            p_out[x, :, snapshot, :] = p_ref[0, x] + step_dir
        else:
            p_out[0, x] = p_ref[0, x] + step_dir
        return write_faces(x, step_dir, carry, *face_out)

    columns = lax.fori_loop(0, nx, body, jnp.zeros((ny, nz), jnp.float32), unroll=8)
    finish_faces(d_out, columns, *face_out)


def initial_kernel(mid, r_ref, inv_ref, d_out, *face_out):
    nx, ny, nz = r_ref.shape[1], r_ref.shape[2], r_ref.shape[3]

    def body(x, carry):
        step_dir = r_ref[0, x] * inv_ref[x] * (1.0 / mid)
        d_out[0, x] = step_dir
        return write_faces(x, step_dir, carry, *face_out)

    columns = lax.fori_loop(0, nx, body, jnp.zeros((ny, nz), jnp.float32), unroll=16)
    finish_faces(d_out, columns, *face_out)


def specs(shape):
    steps, nx, ny, nz = shape
    full = pl.BlockSpec((1, nx, ny, nz), lambda s: (s, 0, 0, 0))
    fixed = pl.BlockSpec((nx, ny, nz), lambda s: (0, 0, 0))
    x_face = pl.BlockSpec((1, ny, nz), lambda s: (s, 0, 0))
    y_face = pl.BlockSpec((1, nx, 1, nz), lambda s: (s, 0, 0, 0))
    z_face = pl.BlockSpec((1, nx, ny), lambda s: (s, 0, 0))
    face_specs = [x_face, x_face, y_face, y_face, z_face, z_face]
    face_shapes = [
        jax.ShapeDtypeStruct((steps, ny, nz), jnp.float32),
        jax.ShapeDtypeStruct((steps, ny, nz), jnp.float32),
        jax.ShapeDtypeStruct((steps, nx, 1, nz), jnp.float32),
        jax.ShapeDtypeStruct((steps, nx, 1, nz), jnp.float32),
        jax.ShapeDtypeStruct((steps, nx, ny), jnp.float32),
        jax.ShapeDtypeStruct((steps, nx, ny), jnp.float32),
    ]
    return full, fixed, face_specs, face_shapes


def run_initial(mid, source, inverse):
    full, fixed, face_specs, face_shapes = specs(source.shape)
    shape = jax.ShapeDtypeStruct(source.shape, jnp.float32)
    size = source.size
    outs = pl.pallas_call(
        functools.partial(initial_kernel, mid),
        grid=(source.shape[0],),
        in_specs=[full, fixed],
        out_specs=[full] + face_specs,
        out_shape=[shape] + face_shapes,
        cost_estimate=pl.CostEstimate(flops=2 * size, transcendentals=0, bytes_accessed=8 * size + 4 * size // source.shape[0]),
        name="chebyshev_start",
    )(source, inverse)
    return outs[0], outs[1:]


def run_sweep(first, second, step_dir, residual, potential, faces, diagonal, inverse, halos, final=False):
    full, fixed, face_specs, face_shapes = specs(step_dir.shape)
    steps, nx, ny, nz = step_dir.shape
    x_face, y_face = face_specs[0], face_specs[2]
    shape = jax.ShapeDtypeStruct(step_dir.shape, jnp.float32)
    if final:
        out_spec = pl.BlockSpec((nx, ny, steps, nz), lambda s: (0, 0, 0, 0))
        out_shape = jax.ShapeDtypeStruct((nx, ny, steps, nz), jnp.float32)
    else:
        out_spec, out_shape = full, shape
    size = step_dir.size
    outs = pl.pallas_call(
        functools.partial(sweep_kernel, final),
        grid=(steps,),
        in_specs=[pl.BlockSpec(memory_space=pltpu.SMEM), full, full, full] + [fixed] * 8 + [x_face, x_face, y_face, y_face, face_specs[4], face_specs[4]],
        out_specs=[full, full, out_spec] + face_specs,
        out_shape=[shape, shape, out_shape] + face_shapes,
        cost_estimate=pl.CostEstimate(flops=30 * size, transcendentals=0, bytes_accessed=4 * 7 * size + 4 * 7 * size // steps),
        name="chebyshev_sweep",
    )(jnp.array([first, second], jnp.float32), step_dir, residual, potential, *faces, diagonal, inverse, *halos)
    return outs[0], outs[1], outs[2], outs[3:]


def local(
    heart_state,
    cell_type,
    gate_half,
    gate_slope,
    gate_tau,
    conduct,
    reversal,
    block_device,
    block_row,
    tissue,
    tissue_sigma,
):
    voltage = heart_state[0]
    gate_state = heart_state[1:]
    heart_x, heart_y, row_len = voltage.shape
    blocks = heart_x * heart_y
    devices = lax.axis_size("gx") * lax.axis_size("gy") * lax.axis_size("gz")
    capacity = 3 * blocks // devices
    slots = devices * capacity
    torso_x, torso_y, torso_z = tissue.shape
    torso_rows = torso_x * torso_y

    dest_dev = block_device.reshape(blocks)
    dest_row = block_row.reshape(blocks)
    one_hot = (dest_dev[:, None] == jnp.arange(devices, dtype=jnp.int32)[None, :]).astype(jnp.int32)
    running = jnp.cumsum(one_hot, axis=0) - 1
    slot_rank = jnp.sum(running * one_hot, axis=1)
    slot_index = dest_dev * capacity + slot_rank
    slot_match = slot_index[None, :] == jnp.arange(slots, dtype=jnp.int32)[:, None]
    slot_used = jnp.any(slot_match, axis=1)
    slot_block = jnp.argmax(slot_match, axis=1).astype(jnp.int32)
    send_rows = jnp.where(slot_used, dest_row[slot_block], torso_rows)
    recv_rows = lax.all_to_all(
        send_rows.reshape(devices, capacity), ("gx", "gy", "gz"), 0, 0, tiled=True
    ).reshape(slots)
    row_match = recv_rows[None, :] == jnp.arange(torso_rows, dtype=jnp.int32)[:, None]
    row_used = jnp.any(row_match, axis=1)
    row_slot = jnp.argmax(row_match, axis=1).astype(jnp.int32)

    sigma = []
    for dim_index in range(3):
        value = jnp.zeros(tissue.shape, jnp.float32)
        for tissue_kind in range(tissue_sigma.shape[0]):
            value = value + jnp.where(tissue == tissue_kind, tissue_sigma[tissue_kind, dim_index], 0.0)
        sigma.append(value)
    riders = [faces_of(sigma[dim_index], dim_index) for dim_index in range(3)]

    currents = []
    for time_step in range(STEPS):
        gate_state, ion_current = membrane(
            voltage, gate_state, cell_type, gate_half, gate_slope, gate_tau, conduct, reversal
        )
        laplace, carried = heart_laplace(voltage, riders if time_step == 0 else None)
        if time_step == 0:
            sigma_halos = [item[0] for item in carried]
        current = SIGMA_HEART * laplace
        currents.append(current)
        voltage = voltage + DT_HEART * (current - ion_current)
    heart_next = jnp.concatenate([voltage[None], gate_state], axis=0)

    payload = jnp.stack([item.reshape(blocks, row_len) for item in currents], axis=0)
    send_values = jnp.where(slot_used[None, :, None], jnp.take(payload, slot_block, axis=1), 0.0)
    received = lax.all_to_all(
        send_values.reshape(STEPS, devices, capacity, row_len),
        ("gx", "gy", "gz"),
        1,
        1,
        tiled=True,
    ).reshape(STEPS, slots, row_len)
    source = jnp.where(row_used[None, :, None], jnp.take(received, row_slot, axis=1), 0.0)
    source = source.reshape(STEPS, torso_x, torso_y, torso_z)

    faces = []
    for dim_index in range(3):
        low, high = sigma_halos[dim_index]
        minus, plus = shifted(sigma[dim_index], low, high, dim_index)
        faces.append(0.5 * (sigma[dim_index] + plus))
        faces.append(0.5 * (sigma[dim_index] + minus))
    diagonal = SCREEN + faces[0] + faces[1] + faces[2] + faces[3] + faces[4] + faces[5]

    spectrum_mid, first_coef, second_coef = chebyshev_weights(SWEEPS)
    residual = source
    inverse = 1.0 / diagonal
    step_dir, dir_faces = run_initial(spectrum_mid, residual, inverse)
    potential = step_dir
    for sweep in range(1, SWEEPS):
        x_low, x_high = exchange(dir_faces[1], dir_faces[0], "gx")
        y_low, y_high = exchange(dir_faces[3], dir_faces[2], "gy")
        z_low, z_high = exchange(dir_faces[5], dir_faces[4], "gz")
        halos = (x_low, x_high, y_low, y_high, z_low, z_high)
        residual, step_dir, potential, dir_faces = run_sweep(
            first_coef[sweep - 1], second_coef[sweep - 1], step_dir, residual, potential, faces, diagonal, inverse, halos,
            final=sweep == SWEEPS - 1,
        )
    return (heart_next, potential)


def solution(mesh):
    in_specs = (
        P(None, "gx", "gy", "gz"),
        P("gx", "gy", "gz"),
        P(),
        P(),
        P(),
        P(),
        P(),
        P("gx", "gy", "gz"),
        P("gx", "gy", "gz"),
        P("gx", "gy", "gz"),
        P(),
    )
    out_specs = (P(None, "gx", "gy", "gz"), P("gx", "gy", None, "gz"))
    return jax.shard_map(local, mesh=mesh, in_specs=in_specs, out_specs=out_specs, check_vma=False)
```
